32 devices in a mesh: req: 8 (over z, y), tp: 4 (over x, core).
Axes of the slice: x: 2, y: 2, z: 4, core: 2. Of those that a mesh axis runs over, the one named last changes fastest.
Arguments:
- hidden: bfloat16 [4096, 2048], P('req', 'tp'), may hold values from -6 to 6
- queries: bfloat16 [4096, 2048], P('req', 'tp'), may hold values from -4 to 4
- new_keys: bfloat16 [4096, 512], P('req'), may hold values from -4 to 4
- new_values: bfloat16 [4096, 512], P('req'), may hold values from -6 to 6
- cache_keys: bfloat16 [384, 64, 512], P('req'), may hold values from -6 to 6
- cache_values: bfloat16 [384, 64, 512], P('req'), may hold values from -6 to 6
- out_weight: bfloat16 [2048, 2048], P('tp'), may hold values from -0.125 to 0.125
- attn_gain: bfloat16 [2048], P('tp'), may hold values from 0.099609375 to 1.8984375
- ple_input: bfloat16 [4096, 256], P('req'), may hold values from -6 to 6
- ple_gate_weight: bfloat16 [2048, 256], P('tp'), may hold values from -0.125 to 0.125
- ple_proj_weight: bfloat16 [256, 2048], P(None, 'tp'), may hold values from -0.375 to 0.375
- ple_gain: bfloat16 [2048], P('tp'), may hold values from 0.099609375 to 1.8984375
- page_holder: int32 [384, 1], P('req'), may hold values from 0 to 7; in each aligned block of 48 rows (0 to 47, 48 to 95, ...) at most 6 rows name the same one
- page_slot: int32 [384, 1], P('req'), may hold values from 0 to 47
- page_counts: int32 [8, 8], P('req'), may hold values from 1 to 12, 48 in all within a row
- last_fill: int32 [8, 8], P('req'), may hold values from 1 to 64
- row_counts: int32 [8, 8], P('req'), may hold values from 1 to 256, 512 in all within a row
Outputs:
- layer_out: bfloat16 [4096, 2048], P('req', 'tp')
The draws below stay inside these ranges and needn't reach their ends.
Inputs may be any that keep to these rules, and one draw needn't show every extreme that they name: `page_holder`: within the 48 page references of one device's requests (aligned blocks), no req index is named more than 6 times; in some block one is named exactly 6 times. `page_counts`: the 8 counts of one device sum to 48; some count equals 12. `row_counts`: the 8 counts of one device sum to 512; some count equals 256.
All inputs are finite; a program needn't handle non-finite values.
Results may differ from the reference program's by a relative error of at most 0.0061.
Values may be sent and summed in bfloat16 or wider, within the bound.
No kernel may reach another device: no remote copies, remote signals or barrier semaphores. Data moves between devices by JAX's collectives and lax.ppermute only.
A program may use at most 128 MiB of HBM per device.

```python
import math
import jax
import jax.numpy as jnp
import numpy as np
from jax import lax

D = 2048
HEADS = 8
KV_HEADS = 2
HD = 256
PLE = 256
ROWS_DEV = 512
SLOTS = 8
PAGE = 64
PAGES_DEV = 48
CTX_PAGES = 12
SPAN = 256
CAP = 6
TOKENS = 4096
POOL = 384
N_REQ = 8


def joint_draw(key):
    first = jax.random.fold_in(key, 11)
    second = jax.random.fold_in(key, 12)
    key_rows = jax.random.truncated_normal(first, -4.0, 4.0, (TOKENS, KV_HEADS * HD), jnp.float32)
    query_rows = jax.random.truncated_normal(second, -4.0, 4.0, (TOKENS, HEADS * HD), jnp.float32)
    return (query_rows.astype(jnp.bfloat16), key_rows.astype(jnp.bfloat16))


def draw_queries(key, part):
    return joint_draw(key)[0]


def draw_new_keys(key, part):
    return joint_draw(key)[1]


def touch_ends(array, own_key, least, high):
    longest = array.shape.index(max(array.shape))
    spots = []
    for shift in (0, 1):
        where = [jax.random.randint(jax.random.fold_in(own_key, axis), (), 0, length) for axis, length in enumerate(array.shape)]
        where[longest] = (where[longest] + shift) % array.shape[longest]
        spots.append(tuple(where))
    return array.at[spots[0]].set(least).at[spots[1]].set(high)


def level_of(own_key, dims, split, smallest, high):
    level, own = 1.0, jax.random.fold_in(own_key, 6)
    for axis_at, shards_of in split:
        steps = jnp.exp(jax.random.uniform(jax.random.fold_in(own, axis_at), (shards_of,), jnp.float32, smallest / len(split), high / len(split)))
        level = level * jnp.repeat(steps, dims[axis_at] // shards_of).reshape([-1 if axis == axis_at else 1 for axis in range(len(dims))])
    return level


def profile(count, total, most, skew):
    portions = [(1 << 20) // math.isqrt(rank ** skew) + 1 for rank in range(2, count + 1)]
    surplus, given = total - most - (count - 1), [1] * (count - 1)
    while surplus > 0:
        candidates = [i for i in range(count - 1) if given[i] < most]
        whole, left = sum([portions[i] for i in candidates]), surplus
        for i in candidates:
            more = min(most - given[i], max(1, left * portions[i] // whole), surplus)
            given[i] = given[i] + more
            surplus = surplus - more
    return np.array([most] + given)


def uneven(own_key, count, total, bound, skew):
    if count == 2:
        one = jax.random.randint(own_key, (), max(1, total - bound), min(bound, total - 1) + 1)
        return jnp.stack([one, total - one])
    tallies = jnp.asarray(profile(count, total, bound, skew), jnp.int32)
    couples = (count - 1) // 2
    giver, sink = tallies[1:1 + 2 * couples:2], tallies[2:2 + 2 * couples:2]
    margin = jnp.minimum(giver - 1, bound - sink)
    moved = jax.random.randint(jax.random.fold_in(own_key, 1), (couples,), 0, 1 << 20) % (margin + 1)
    tallies = tallies.at[1:1 + 2 * couples:2].set(giver - moved).at[2:2 + 2 * couples:2].set(sink + moved)
    return tallies[jax.random.permutation(jax.random.fold_in(own_key, 2), count)]


def routed_block(rng, own, number, rows, amount, top, most, slope):
    ranking = jax.random.permutation(rng, amount)
    packed, common = shares(amount, rows * top, most, slope, True), shares(amount, rows * top, most, slope, False)
    places = jnp.arange(amount)

    def named(lengths, turn):
        used = int((lengths > 0).sum())
        fixed = max(1, used // 4)
        passed = fixed + (places - fixed + turn * (used - fixed)) % max(1, amount - fixed)
        return jnp.zeros((amount,), jnp.int32).at[ranking[jnp.where(places < fixed, places, passed)]].set(jnp.asarray(lengths, jnp.int32))

    lengths = jnp.where(number % 4 == 0, named(packed, number // 4), named(common, number - number // 4 - 1))
    mixed = jax.random.permutation(jax.random.fold_in(own, 3), amount)
    giver, taker = mixed[0:amount // 2 * 2:2], mixed[1:amount // 2 * 2:2]
    margin = jnp.minimum(lengths[giver] - 1, most - lengths[taker]) // 2
    margin = jnp.where((giver == ranking[0]) | (taker == ranking[0]) | (lengths[taker] == 0), 0, jnp.maximum(margin, 0))
    passed = jax.random.randint(jax.random.fold_in(own, 4), (amount // 2,), 0, 1 << 20) % (margin + 1)
    lengths = lengths.at[giver].add(-passed).at[taker].add(passed)
    items = jnp.searchsorted(jnp.cumsum(lengths), jnp.arange(rows * top), side="right").astype(jnp.int32)
    table = items.reshape(top, rows).T
    table = table[jax.random.permutation(jax.random.fold_in(own, 1), rows)]
    turn = jax.random.randint(jax.random.fold_in(own, 2), (rows, 1), 0, top)
    return jnp.take_along_axis(table, (jnp.arange(top)[None, :] + turn) % top, axis=1)


def shares(number_of, total, most, slope, full):
    portions = [(1 << 20) // math.isqrt(standing ** slope) + 1 for standing in range(1, number_of + 1)]
    largest = most if full else min(most, max(-(-total // number_of), total * portions[0] // sum(portions)))
    least = 1 if total - largest >= number_of - 1 else 0
    given, spare = [largest] + [least] * (number_of - 1), total - largest - least * (number_of - 1)
    while spare > 0:
        free = [i for i in range(1, number_of) if given[i] < largest] or [i for i in range(1, number_of) if given[i] < most]
        mass, remaining = sum([portions[i] for i in free]), spare
        for i in free:
            extra = min(most - given[i], max(1, remaining * portions[i] // mass), spare)
            given[i] = given[i] + extra
            spare = spare - extra
    return np.array(given)


def scatter_about(rng, shape, spread, reach, pieces=(), kind=jnp.bfloat16):
    values = jax.random.normal(rng, shape, jnp.float32) * spread
    if len(pieces) > 0:
        values = level_of(rng, shape, pieces, -0.22, 0.18) * values
    return jnp.clip(values, min=-reach, max=reach).astype(kind)


def setup_inputs(seed: int = 0) -> dict:
    keys = jax.random.split(jax.random.key(seed), 18)
    hidden = scatter_about(keys[0], (TOKENS, D), 1.0, 6.0, ((0, 8), (1, 4)))
    queries = draw_queries(jax.random.fold_in(keys[17], 71), 0)
    new_keys = draw_new_keys(jax.random.fold_in(keys[17], 71), 0)
    new_values = scatter_about(keys[3], (TOKENS, KV_HEADS * HD), 1.0, 6.0, ((0, 8),))
    cache_keys = scatter_about(keys[4], (POOL, PAGE, KV_HEADS * HD), 1.0, 6.0, ((0, 8),))
    cache_values = scatter_about(keys[5], (POOL, PAGE, KV_HEADS * HD), 1.0, 6.0, ((0, 8),))
    out_weight = scatter_about(keys[6], (HEADS * HD, D), (HEADS * HD) ** -0.5, 0.125, ((0, 4),))
    attn_gain = jnp.clip(1.0 + 0.18 * jax.random.normal(keys[7], (D,), jnp.float32), 0.099609375, 1.8984375).astype(jnp.bfloat16)
    ple_input = scatter_about(keys[8], (TOKENS, PLE), 1.0, 6.0, ((0, 8),))
    ple_gate_weight = scatter_about(keys[9], (D, PLE), D ** -0.5, 0.125, ((0, 4),))
    ple_proj_weight = scatter_about(keys[10], (PLE, D), PLE ** -0.5, 0.375, ((1, 4),))
    ple_gain = jnp.clip(1.0 + 0.18 * jax.random.normal(keys[11], (D,), jnp.float32), 0.099609375, 1.8984375).astype(jnp.bfloat16)
    page_holder_keys = jax.random.split(jax.random.fold_in(keys[12], 1), POOL // PAGES_DEV)
    page_holder_turns = jax.random.permutation(jax.random.fold_in(keys[12], 3), POOL // PAGES_DEV)
    page_holder = jax.vmap(lambda own, number: routed_block(jax.random.fold_in(keys[12], 2), own, number, PAGES_DEV, N_REQ, 1, CAP, 1))(page_holder_keys, page_holder_turns).reshape((POOL, 1))
    page_slot = touch_ends(jax.random.randint(keys[13], (POOL, 1), 0, PAGES_DEV), jax.random.fold_in(keys[13], 1), 0, PAGES_DEV - 1).astype(jnp.int32)
    page_counts = jax.vmap(lambda own: uneven(own, SLOTS, PAGES_DEV, CTX_PAGES, 2))(jax.random.split(keys[14], N_REQ)).reshape((N_REQ, SLOTS)).astype(jnp.int32)
    last_fill = touch_ends(jax.random.randint(keys[15], (N_REQ, SLOTS), 1, PAGE + 1), jax.random.fold_in(keys[15], 1), 1, PAGE).astype(jnp.int32)
    row_counts = jax.vmap(lambda own: uneven(own, SLOTS, ROWS_DEV, SPAN, 2))(jax.random.split(keys[16], N_REQ)).reshape((N_REQ, SLOTS)).astype(jnp.int32)
    return dict(hidden=hidden, queries=queries, new_keys=new_keys, new_values=new_values, cache_keys=cache_keys, cache_values=cache_values, out_weight=out_weight, attn_gain=attn_gain, ple_input=ple_input, ple_gate_weight=ple_gate_weight, ple_proj_weight=ple_proj_weight, ple_gain=ple_gain, page_holder=page_holder, page_slot=page_slot, page_counts=page_counts, last_fill=last_fill, row_counts=row_counts)


def slot_lookup(positions, counts):
    starts = jnp.cumsum(counts) - counts
    owning = lax.optimization_barrier(jnp.sum((positions[:, None] >= starts[None, :]).astype(jnp.int32), axis=1)) - 1
    return (owning, starts)

def table_pick(table, owning):
    onehot = owning[:, None] == jnp.arange(table.shape[0], dtype=jnp.int32)[None, :]
    return lax.optimization_barrier(jnp.sum(jnp.where(onehot, table[None, :], 0), axis=1))

def attend_masks(counts_of_pages, fill_row, counts_of_rows, page_len, page_total, row_total):
    key_index = jnp.arange(page_total * page_len, dtype=jnp.int32)
    page_ref = key_index // page_len
    within = key_index % page_len
    page_owner, page_starts = slot_lookup(page_ref, counts_of_pages)
    context_len = (counts_of_pages - 1) * page_len + fill_row
    position = (page_ref - table_pick(page_starts, page_owner)) * page_len + within
    valid = position < table_pick(context_len, page_owner)
    row_index = jnp.arange(row_total, dtype=jnp.int32)
    row_owner = slot_lookup(row_index, counts_of_rows)[0]
    context_mask = (row_owner[:, None] == page_owner[None, :]) & valid[None, :]
    causal = (row_owner[:, None] == row_owner[None, :]) & (row_index[None, :] <= row_index[:, None])
    return jnp.concatenate([context_mask, causal], axis=1)

def rms_scale(values, gain):
    return values * lax.rsqrt(lax.optimization_barrier(jnp.mean(values * values, axis=-1, keepdims=True)) + 1e-06) * gain.astype(jnp.float32)

def reference(hidden, queries, new_keys, new_values, cache_keys, cache_values, out_weight, attn_gain, ple_input, ple_gate_weight, ple_proj_weight, ple_gain, page_holder, page_slot, page_counts, last_fill, row_counts):
    group = HEADS // KV_HEADS
    scale = 1.0 / math.sqrt(HD)

    def one_device(owner):
        row_start = (owner * ROWS_DEV).astype(jnp.int32)
        query_rows = lax.dynamic_slice_in_dim(queries, row_start, ROWS_DEV, 0).astype(jnp.float32).reshape(ROWS_DEV, HEADS, HD)
        fresh_keys = lax.dynamic_slice_in_dim(new_keys, row_start, ROWS_DEV, 0)
        fresh_values = lax.dynamic_slice_in_dim(new_values, row_start, ROWS_DEV, 0)
        ref_start = (owner * PAGES_DEV).astype(jnp.int32)
        holders = lax.dynamic_slice_in_dim(page_holder[:, 0], ref_start, PAGES_DEV, 0)
        places = lax.dynamic_slice_in_dim(page_slot[:, 0], ref_start, PAGES_DEV, 0)
        global_ids = (holders * PAGES_DEV + places).astype(jnp.int32)
        context_keys = cache_keys[global_ids].reshape(PAGES_DEV * PAGE, KV_HEADS * HD)
        context_values = cache_values[global_ids].reshape(PAGES_DEV * PAGE, KV_HEADS * HD)
        all_keys = jnp.concatenate([context_keys, fresh_keys], 0).astype(jnp.float32).reshape(-1, KV_HEADS, HD)
        all_values = jnp.concatenate([context_values, fresh_values], 0).astype(jnp.float32).reshape(-1, KV_HEADS, HD)
        all_keys = jnp.repeat(all_keys, group, axis=1)
        all_values = jnp.repeat(all_values, group, axis=1)
        masking = attend_masks(page_counts[owner], last_fill[owner], row_counts[owner], PAGE, PAGES_DEV, ROWS_DEV)
        scores = jnp.einsum('rhd,khd->hrk', query_rows, all_keys) * scale
        scores = jnp.where(masking[None], scores, -1e+30)
        highest = lax.optimization_barrier(jnp.max(scores, axis=-1, keepdims=True))
        expo = jnp.exp(scores - highest)
        weights = lax.optimization_barrier((expo / lax.optimization_barrier(jnp.sum(expo, axis=-1, keepdims=True))).astype(jnp.bfloat16)).astype(jnp.float32)
        result = jnp.einsum('hrk,khd->rhd', weights, all_values)
        return result.astype(jnp.bfloat16).reshape(ROWS_DEV, HEADS * HD)
    attention = lax.map(one_device, jnp.arange(N_REQ, dtype=jnp.int32)).reshape(TOKENS, HEADS * HD)
    projected = jnp.dot(attention, out_weight, preferred_element_type=jnp.float32)
    mixed_state = (hidden.astype(jnp.float32) + rms_scale(projected, attn_gain)).astype(jnp.bfloat16)
    gate = jnp.dot(mixed_state, ple_gate_weight, preferred_element_type=jnp.float32)
    activated = (jax.nn.gelu(gate, approximate=True) * ple_input.astype(jnp.float32)).astype(jnp.bfloat16)
    lifted = jnp.dot(activated, ple_proj_weight, preferred_element_type=jnp.float32)
    return (mixed_state.astype(jnp.float32) + rms_scale(lifted, ple_gain)).astype(jnp.bfloat16)
```

```python
import math

import jax
import jax.numpy as jnp
from jax import lax
from jax.sharding import PartitionSpec as P

D = 2048
HD = 256


def slot_lookup(positions, counts):
    starts = jnp.cumsum(counts) - counts
    owning = jnp.sum((positions[:, None] >= starts[None, :]).astype(jnp.int32), axis=1) - 1
    return (owning, starts)


def table_pick(table, owning):
    onehot = owning[:, None] == jnp.arange(table.shape[0], dtype=jnp.int32)[None, :]
    return jnp.sum(jnp.where(onehot, table[None, :], 0), axis=1)


def attend_masks(counts_of_pages, fill_row, counts_of_rows, page_len, page_total, row_total):
    key_index = jnp.arange(page_total * page_len, dtype=jnp.int32)
    page_ref = key_index // page_len
    within = key_index % page_len
    page_owner, page_starts = slot_lookup(page_ref, counts_of_pages)
    context_len = (counts_of_pages - 1) * page_len + fill_row
    position = (page_ref - table_pick(page_starts, page_owner)) * page_len + within
    valid = position < table_pick(context_len, page_owner)
    row_index = jnp.arange(row_total, dtype=jnp.int32)
    row_owner = slot_lookup(row_index, counts_of_rows)[0]
    context_mask = (row_owner[:, None] == page_owner[None, :]) & valid[None, :]
    causal = (row_owner[:, None] == row_owner[None, :]) & (row_index[None, :] <= row_index[:, None])
    return jnp.concatenate([context_mask, causal], axis=1)


def shards(
    hidden,
    queries,
    new_keys,
    new_values,
    cache_keys,
    cache_values,
    out_weight,
    attn_gain,
    ple_input,
    ple_gate_weight,
    ple_proj_weight,
    ple_gain,
    page_holder,
    page_slot,
    page_counts,
    last_fill,
    row_counts,
):
    row_total = hidden.shape[0]
    page_total = cache_keys.shape[0]
    page_len = cache_keys.shape[1]
    req_count = lax.axis_size("req")
    tp_index = lax.axis_index("tp")
    local_heads = queries.shape[1] // HD
    kv_head = tp_index // 2
    capacity = max(2, page_total // req_count)
    holders = page_holder[:, 0]
    places = page_slot[:, 0]
    ref_index = jnp.arange(page_total, dtype=jnp.int32)
    earlier = (holders[:, None] == holders[None, :]) & (ref_index[:, None] > ref_index[None, :])
    ranking = jnp.sum(earlier.astype(jnp.int32), axis=1)
    matched = (holders[:, None, None] == jnp.arange(req_count, dtype=jnp.int32)[None, :, None]) & (
        ranking[:, None, None] == jnp.arange(capacity, dtype=jnp.int32)[None, None, :]
    )
    request_table = jnp.sum(jnp.where(matched, places[:, None, None] + 1, 0), axis=0) - 1
    asked = lax.all_to_all(request_table, "req", split_axis=0, concat_axis=0, tiled=True)
    wanted = jnp.maximum(asked, 0)
    head_keys = lax.dynamic_slice_in_dim(cache_keys, kv_head * HD, HD, 2)
    head_values = lax.dynamic_slice_in_dim(cache_values, kv_head * HD, HD, 2)
    stacked = jnp.concatenate([head_keys, head_values], axis=2)
    arrival_index = holders * capacity + ranking
    outgoing = stacked[wanted]
    arrived = lax.all_to_all(outgoing, "req", split_axis=0, concat_axis=0, tiled=True)
    context = arrived.reshape(req_count * capacity, page_len, 2 * HD)[arrival_index]
    context_keys = context[:, :, :HD].reshape(page_total * page_len, HD)
    context_values = context[:, :, HD:].reshape(page_total * page_len, HD)
    fresh_keys = lax.dynamic_slice_in_dim(new_keys, kv_head * HD, HD, 1)
    fresh_values = lax.dynamic_slice_in_dim(new_values, kv_head * HD, HD, 1)
    all_keys = jnp.concatenate([context_keys, fresh_keys], axis=0)
    all_values = jnp.concatenate([context_values, fresh_values], axis=0)
    masking = attend_masks(
        page_counts[0], last_fill[0], row_counts[0], page_len, page_total, row_total
    )
    query_rows = queries.reshape(row_total, local_heads, HD)
    scores = jnp.einsum("rhd,kd->hrk", query_rows, all_keys, preferred_element_type=jnp.float32) * (
        1.0 / math.sqrt(HD)
    )
    scores = jnp.where(masking[None], scores, -1e30)
    highest = jnp.max(scores, axis=-1, keepdims=True)
    expo = jnp.exp(scores - highest)
    weights = (expo / jnp.sum(expo, axis=-1, keepdims=True)).astype(jnp.bfloat16)
    attention = jnp.einsum("hrk,kd->rhd", weights, all_values, preferred_element_type=jnp.float32)
    attention = attention.astype(jnp.bfloat16).reshape(row_total, local_heads * HD)
    tp_size = lax.axis_size("tp")
    full_weight = lax.all_gather(out_weight, "tp", axis=0, tiled=True)
    full_gate_weight = lax.all_gather(ple_gate_weight, "tp", axis=0, tiled=True)
    full_proj_weight = lax.all_gather(ple_proj_weight, "tp", axis=1, tiled=True)
    full_attn_gain = lax.all_gather(attn_gain, "tp", axis=0, tiled=True)
    full_ple_gain = lax.all_gather(ple_gain, "tp", axis=0, tiled=True)
    row_hidden = lax.all_to_all(hidden, "tp", split_axis=0, concat_axis=1, tiled=True)
    row_attention = lax.all_to_all(attention, "tp", split_axis=0, concat_axis=1, tiled=True)
    part_rows = row_attention.shape[0]
    row_ple = lax.dynamic_slice_in_dim(ple_input, tp_index * part_rows, part_rows, 0)
    projected = jnp.dot(row_attention, full_weight, preferred_element_type=jnp.float32)
    squares = jnp.sum(projected * projected, axis=1)
    normed = (
        projected
        * lax.rsqrt(squares / D + 1e-06)[:, None]
        * full_attn_gain.astype(jnp.float32)[None, :]
    )
    mixed_state = (row_hidden.astype(jnp.float32) + normed).astype(jnp.bfloat16)
    gate = jnp.dot(mixed_state, full_gate_weight, preferred_element_type=jnp.float32)
    activated = (jax.nn.gelu(gate, approximate=True) * row_ple.astype(jnp.float32)).astype(
        jnp.bfloat16
    )
    lifted = jnp.dot(activated, full_proj_weight, preferred_element_type=jnp.float32)
    lift_squares = jnp.sum(lifted * lifted, axis=1)
    lift_normed = (
        lifted
        * lax.rsqrt(lift_squares / D + 1e-06)[:, None]
        * full_ple_gain.astype(jnp.float32)[None, :]
    )
    row_out = (mixed_state.astype(jnp.float32) + lift_normed).astype(jnp.bfloat16)
    return lax.all_to_all(row_out, "tp", split_axis=1, concat_axis=0, tiled=True)


def solution(mesh):
    return jax.shard_map(
        shards,
        mesh=mesh,
        in_specs=(
            P("req", "tp"),
            P("req", "tp"),
            P("req", None),
            P("req", None),
            P("req", None, None),
            P("req", None, None),
            P("tp", None),
            P("tp"),
            P("req", None),
            P("tp", None),
            P(None, "tp"),
            P("tp"),
            P("req", None),
            P("req", None),
            P("req", None),
            P("req", None),
            P("req", None),
        ),
        out_specs=P("req", "tp"),
        check_vma=False,
    )
```

```python
import math

import jax
import jax.numpy as jnp
from jax import lax
from jax.sharding import PartitionSpec as P

D = 2048
HD = 256


def slot_lookup(positions, counts):
    starts = jnp.cumsum(counts) - counts
    owning = jnp.sum((positions[:, None] >= starts[None, :]).astype(jnp.int32), axis=1) - 1
    return (owning, starts)


def table_pick(table, owning):
    onehot = owning[:, None] == jnp.arange(table.shape[0], dtype=jnp.int32)[None, :]
    return jnp.sum(jnp.where(onehot, table[None, :], 0), axis=1)


def attend_masks(counts_of_pages, fill_row, counts_of_rows, page_len, page_total, row_total):
    key_index = jnp.arange(page_total * page_len, dtype=jnp.int32)
    page_ref = key_index // page_len
    within = key_index % page_len
    page_owner, page_starts = slot_lookup(page_ref, counts_of_pages)
    context_len = (counts_of_pages - 1) * page_len + fill_row
    position = (page_ref - table_pick(page_starts, page_owner)) * page_len + within
    valid = position < table_pick(context_len, page_owner)
    row_index = jnp.arange(row_total, dtype=jnp.int32)
    row_owner = slot_lookup(row_index, counts_of_rows)[0]
    context_mask = (row_owner[:, None] == page_owner[None, :]) & valid[None, :]
    causal = (row_owner[:, None] == row_owner[None, :]) & (row_index[None, :] <= row_index[:, None])
    return jnp.concatenate([context_mask, causal], axis=1)


def shards(
    hidden,
    queries,
    new_keys,
    new_values,
    cache_keys,
    cache_values,
    out_weight,
    attn_gain,
    ple_input,
    ple_gate_weight,
    ple_proj_weight,
    ple_gain,
    page_holder,
    page_slot,
    page_counts,
    last_fill,
    row_counts,
):
    row_total = hidden.shape[0]
    page_total = cache_keys.shape[0]
    page_len = cache_keys.shape[1]
    req_count = lax.axis_size("req")
    tp_index = lax.axis_index("tp")
    local_heads = queries.shape[1] // HD
    kv_head = tp_index // 2
    capacity = max(2, page_total // req_count)
    holders = page_holder[:, 0]
    places = page_slot[:, 0]
    ref_index = jnp.arange(page_total, dtype=jnp.int32)
    earlier = (holders[:, None] == holders[None, :]) & (ref_index[:, None] > ref_index[None, :])
    ranking = jnp.sum(earlier.astype(jnp.int32), axis=1)
    matched = (holders[:, None, None] == jnp.arange(req_count, dtype=jnp.int32)[None, :, None]) & (
        ranking[:, None, None] == jnp.arange(capacity, dtype=jnp.int32)[None, None, :]
    )
    request_table = jnp.sum(jnp.where(matched, places[:, None, None] + 1, 0), axis=0) - 1
    asked = lax.all_to_all(request_table, "req", split_axis=0, concat_axis=0, tiled=True)
    wanted = jnp.maximum(asked, 0)
    tp_count = lax.axis_size("tp")
    half = tp_index % 2
    partner = [(i, i ^ 1) for i in range(tp_count)]
    own_cache = jnp.where(half == 0, cache_keys, cache_values)
    head_cache = lax.dynamic_slice_in_dim(own_cache, kv_head * HD, HD, 2)
    arrival_index = holders * capacity + ranking
    outgoing = head_cache[wanted]
    arrived = lax.all_to_all(outgoing, "req", split_axis=0, concat_axis=0, tiled=True)
    swapped = lax.ppermute(arrived, "tp", partner)
    key_pages = jnp.where(half == 0, arrived, swapped)
    value_pages = jnp.where(half == 0, swapped, arrived)
    context_keys = key_pages.reshape(req_count * capacity, page_len, HD)[arrival_index].reshape(
        page_total * page_len, HD
    )
    context_values = value_pages.reshape(req_count * capacity, page_len, HD)[
        arrival_index
    ].reshape(page_total * page_len, HD)
    fresh_keys = lax.dynamic_slice_in_dim(new_keys, kv_head * HD, HD, 1)
    fresh_values = lax.dynamic_slice_in_dim(new_values, kv_head * HD, HD, 1)
    all_keys = jnp.concatenate([context_keys, fresh_keys], axis=0)
    all_values = jnp.concatenate([context_values, fresh_values], axis=0)
    masking = attend_masks(
        page_counts[0], last_fill[0], row_counts[0], page_len, page_total, row_total
    )
    query_rows = queries.reshape(row_total, local_heads, HD)
    scores = jnp.einsum("rhd,kd->hrk", query_rows, all_keys, preferred_element_type=jnp.float32) * (
        1.0 / math.sqrt(HD)
    )
    scores = jnp.where(masking[None], scores, -1e30)
    highest = jnp.max(scores, axis=-1, keepdims=True)
    expo = jnp.exp(scores - highest)
    weights = (expo / jnp.sum(expo, axis=-1, keepdims=True)).astype(jnp.bfloat16)
    attention = jnp.einsum("hrk,kd->rhd", weights, all_values, preferred_element_type=jnp.float32)
    attention = attention.astype(jnp.bfloat16).reshape(row_total, local_heads * HD)
    tp_size = lax.axis_size("tp")
    full_weight = lax.all_gather(out_weight, "tp", axis=0, tiled=True)
    full_gate_weight = lax.all_gather(ple_gate_weight, "tp", axis=0, tiled=True)
    full_proj_weight = lax.all_gather(ple_proj_weight, "tp", axis=1, tiled=True)
    hidden_parts = hidden.reshape(tp_size, -1, hidden.shape[1])
    gain_rows = jnp.zeros((8, hidden.shape[1]), hidden.dtype).at[0].set(attn_gain).at[1].set(ple_gain)
    with_gains = jnp.concatenate(
        [hidden_parts, jnp.broadcast_to(gain_rows[None], (tp_size, 8, hidden.shape[1]))], axis=1
    )
    row_hidden_gains = lax.all_to_all(
        with_gains.reshape(-1, hidden.shape[1]), "tp", split_axis=0, concat_axis=1, tiled=True
    )
    row_hidden = row_hidden_gains[: hidden_parts.shape[1]]
    full_attn_gain = row_hidden_gains[hidden_parts.shape[1]]
    full_ple_gain = row_hidden_gains[hidden_parts.shape[1] + 1]
    row_attention = lax.all_to_all(attention, "tp", split_axis=0, concat_axis=1, tiled=True)
    part_rows = row_attention.shape[0]
    row_ple = lax.dynamic_slice_in_dim(ple_input, tp_index * part_rows, part_rows, 0)
    projected = jnp.dot(row_attention, full_weight, preferred_element_type=jnp.float32)
    squares = jnp.sum(projected * projected, axis=1)
    normed = (
        projected
        * lax.rsqrt(squares / D + 1e-06)[:, None]
        * full_attn_gain.astype(jnp.float32)[None, :]
    )
    mixed_state = (row_hidden.astype(jnp.float32) + normed).astype(jnp.bfloat16)
    gate = jnp.dot(mixed_state, full_gate_weight, preferred_element_type=jnp.float32)
    activated = (jax.nn.gelu(gate, approximate=True) * row_ple.astype(jnp.float32)).astype(
        jnp.bfloat16
    )
    lifted = jnp.dot(activated, full_proj_weight, preferred_element_type=jnp.float32)
    lift_squares = jnp.sum(lifted * lifted, axis=1)
    lift_normed = (
        lifted
        * lax.rsqrt(lift_squares / D + 1e-06)[:, None]
        * full_ple_gain.astype(jnp.float32)[None, :]
    )
    row_out = (mixed_state.astype(jnp.float32) + lift_normed).astype(jnp.bfloat16)
    return lax.all_to_all(row_out, "tp", split_axis=1, concat_axis=0, tiled=True)


def solution(mesh):
    return jax.shard_map(
        shards,
        mesh=mesh,
        in_specs=(
            P("req", "tp"),
            P("req", "tp"),
            P("req", None),
            P("req", None),
            P("req", None, None),
            P("req", None, None),
            P("tp", None),
            P("tp"),
            P("req", None),
            P("tp", None),
            P(None, "tp"),
            P("tp"),
            P("req", None),
            P("req", None),
            P("req", None),
            P("req", None),
            P("req", None),
        ),
        out_specs=P("req", "tp"),
        check_vma=False,
    )
```

```python
import math

import jax
import jax.numpy as jnp
from jax import lax
from jax.experimental import pallas as pl
from jax.experimental.pallas import tpu as pltpu
from jax.sharding import PartitionSpec as P

D = 2048
HD = 256


def slot_lookup(positions, counts):
    starts = jnp.cumsum(counts) - counts
    owning = jnp.sum((positions[:, None] >= starts[None, :]).astype(jnp.int32), axis=1) - 1
    return (owning, starts)


def table_pick(table, owning):
    onehot = owning[:, None] == jnp.arange(table.shape[0], dtype=jnp.int32)[None, :]
    return jnp.sum(jnp.where(onehot, table[None, :], 0), axis=1)


def attend_masks(counts_of_pages, fill_row, counts_of_rows, page_len, page_total, row_total):
    key_index = jnp.arange(page_total * page_len, dtype=jnp.int32)
    page_ref = key_index // page_len
    within = key_index % page_len
    page_owner, page_starts = slot_lookup(page_ref, counts_of_pages)
    context_len = (counts_of_pages - 1) * page_len + fill_row
    position = (page_ref - table_pick(page_starts, page_owner)) * page_len + within
    valid = position < table_pick(context_len, page_owner)
    row_index = jnp.arange(row_total, dtype=jnp.int32)
    row_owner = slot_lookup(row_index, counts_of_rows)[0]
    context_mask = (row_owner[:, None] == page_owner[None, :]) & valid[None, :]
    causal = (row_owner[:, None] == row_owner[None, :]) & (row_index[None, :] <= row_index[:, None])
    return jnp.concatenate([context_mask, causal], axis=1)


ROW_BLOCK = 128
KEY_CHUNK = 256


def pick(table, index):
    onehot = index[:, None] == jnp.arange(table.shape[0], dtype=jnp.int32)[None, :]
    return jnp.sum(jnp.where(onehot, table[None, :], 0), axis=1)


def attention_kernel(
    ranges_ref, q_ref, k_ref, v_ref, kown_ref, kpos_ref, rown_ref, o_ref, s_scr, acc_scr
):
    block = pl.program_id(0)
    ctx_lo = ranges_ref[block, 0]
    ctx_n = ranges_ref[block, 1]
    new_lo = ranges_ref[block, 2]
    total = ctx_n + ranges_ref[block, 3]
    first_new = ranges_ref[block, 4]
    heads = q_ref.shape[1] // HD
    q = q_ref[...]
    stacked = jnp.concatenate([q[:, h * HD:(h + 1) * HD] for h in range(heads)], axis=0)
    row_owner = rown_ref[...]
    row_index = block * ROW_BLOCK + lax.broadcasted_iota(jnp.int32, (ROW_BLOCK, 1), 0)
    scale = 1.0 / math.sqrt(HD)

    def chunk_of(t):
        return jnp.where(t < ctx_n, ctx_lo + t, first_new + new_lo + t - ctx_n)

    def scores_pass(t, highest):
        c = chunk_of(t)
        start = pl.multiple_of(c * KEY_CHUNK, KEY_CHUNK)
        keys = k_ref[pl.ds(start, KEY_CHUNK), :]
        s = lax.dot_general(
            stacked, keys, (((1,), (1,)), ((), ())), preferred_element_type=jnp.float32
        ) * scale
        seen = (kown_ref[c] == row_owner) & (kpos_ref[c] <= row_index)
        seen = jnp.concatenate([seen] * heads, axis=0)
        s = jnp.where(seen, s, -1e30)
        s_scr[c] = s
        return jnp.maximum(highest, jnp.max(s, axis=1, keepdims=True))

    highest = lax.fori_loop(
        0, total, scores_pass, jnp.full((heads * ROW_BLOCK, 1), -1e30, jnp.float32)
    )

    def exp_pass(t, summed):
        c = chunk_of(t)
        e = jnp.exp(s_scr[c] - highest)
        s_scr[c] = e
        return summed + jnp.sum(e, axis=1, keepdims=True)

    summed = lax.fori_loop(0, total, exp_pass, jnp.zeros((heads * ROW_BLOCK, 1), jnp.float32))
    acc_scr[...] = jnp.zeros(acc_scr.shape, jnp.float32)

    def value_pass(t, carry):
        c = chunk_of(t)
        start = pl.multiple_of(c * KEY_CHUNK, KEY_CHUNK)
        w = (s_scr[c] / summed).astype(jnp.bfloat16)
        acc_scr[...] += jnp.dot(w, v_ref[pl.ds(start, KEY_CHUNK), :], preferred_element_type=jnp.float32)
        return carry

    lax.fori_loop(0, total, value_pass, 0)
    for h in range(heads):
        o_ref[:, h * HD:(h + 1) * HD] = acc_scr[h * ROW_BLOCK:(h + 1) * ROW_BLOCK, :].astype(
            jnp.bfloat16
        )


def sparse_attention(queries, keys, values, page_counts, last_fill, row_counts, page_len):
    row_total = queries.shape[0]
    key_total = keys.shape[0]
    ctx_total = key_total - row_total
    page_total = ctx_total // page_len
    heads = queries.shape[1] // HD
    blocks = row_total // ROW_BLOCK
    chunks = key_total // KEY_CHUNK
    ctx_chunks = ctx_total // KEY_CHUNK
    key_index = jnp.arange(ctx_total, dtype=jnp.int32)
    page_ref = key_index // page_len
    page_owner, page_starts = slot_lookup(page_ref, page_counts)
    context_len = (page_counts - 1) * page_len + last_fill
    position = (page_ref - table_pick(page_starts, page_owner)) * page_len + key_index % page_len
    valid = position < table_pick(context_len, page_owner)
    row_index = jnp.arange(row_total, dtype=jnp.int32)
    row_owner, row_starts = slot_lookup(row_index, row_counts)
    key_owner = jnp.concatenate([jnp.where(valid, page_owner, -1), row_owner])
    key_pos = jnp.concatenate([jnp.full((ctx_total,), -1, jnp.int32), row_index])
    first = row_owner[::ROW_BLOCK]
    last = row_owner[ROW_BLOCK - 1::ROW_BLOCK]
    ctx_from = pick(page_starts, first) * page_len
    ctx_to = (pick(page_starts, last) + pick(page_counts, last)) * page_len
    ctx_lo = ctx_from // KEY_CHUNK
    ctx_n = (ctx_to + KEY_CHUNK - 1) // KEY_CHUNK - ctx_lo
    new_from = pick(row_starts, first)
    new_to = jnp.arange(1, blocks + 1, dtype=jnp.int32) * ROW_BLOCK
    new_lo = new_from // KEY_CHUNK
    new_n = (new_to + KEY_CHUNK - 1) // KEY_CHUNK - new_lo
    ranges = jnp.stack(
        [ctx_lo, ctx_n, new_lo, new_n, jnp.full((blocks,), ctx_chunks, jnp.int32)], axis=1
    ).astype(jnp.int32)
    full = lambda b, r: (0, 0)
    return pl.pallas_call(
        attention_kernel,
        grid_spec=pltpu.PrefetchScalarGridSpec(
            num_scalar_prefetch=1,
            grid=(blocks,),
            in_specs=[
                pl.BlockSpec((ROW_BLOCK, heads * HD), lambda b, r: (b, 0)),
                pl.BlockSpec((key_total, HD), full),
                pl.BlockSpec((key_total, HD), full),
                pl.BlockSpec((chunks, 1, KEY_CHUNK), lambda b, r: (0, 0, 0)),
                pl.BlockSpec((chunks, 1, KEY_CHUNK), lambda b, r: (0, 0, 0)),
                pl.BlockSpec((ROW_BLOCK, 1), lambda b, r: (b, 0)),
            ],
            out_specs=pl.BlockSpec((ROW_BLOCK, heads * HD), lambda b, r: (b, 0)),
            scratch_shapes=[
                pltpu.VMEM((chunks, heads * ROW_BLOCK, KEY_CHUNK), jnp.float32),
                pltpu.VMEM((heads * ROW_BLOCK, HD), jnp.float32),
            ],
        ),
        out_shape=jax.ShapeDtypeStruct((row_total, heads * HD), jnp.bfloat16),
    )(
        ranges,
        queries,
        keys,
        values,
        key_owner.reshape(chunks, 1, KEY_CHUNK),
        key_pos.reshape(chunks, 1, KEY_CHUNK),
        row_owner.reshape(row_total, 1),
    )


def shards(
    hidden,
    queries,
    new_keys,
    new_values,
    cache_keys,
    cache_values,
    out_weight,
    attn_gain,
    ple_input,
    ple_gate_weight,
    ple_proj_weight,
    ple_gain,
    page_holder,
    page_slot,
    page_counts,
    last_fill,
    row_counts,
):
    row_total = hidden.shape[0]
    page_total = cache_keys.shape[0]
    page_len = cache_keys.shape[1]
    req_count = lax.axis_size("req")
    tp_index = lax.axis_index("tp")
    local_heads = queries.shape[1] // HD
    kv_head = tp_index // 2
    capacity = max(2, page_total // req_count)
    holders = page_holder[:, 0]
    places = page_slot[:, 0]
    ref_index = jnp.arange(page_total, dtype=jnp.int32)
    earlier = (holders[:, None] == holders[None, :]) & (ref_index[:, None] > ref_index[None, :])
    ranking = jnp.sum(earlier.astype(jnp.int32), axis=1)
    matched = (holders[:, None, None] == jnp.arange(req_count, dtype=jnp.int32)[None, :, None]) & (
        ranking[:, None, None] == jnp.arange(capacity, dtype=jnp.int32)[None, None, :]
    )
    request_table = jnp.sum(jnp.where(matched, places[:, None, None] + 1, 0), axis=0) - 1
    asked = lax.all_to_all(request_table, "req", split_axis=0, concat_axis=0, tiled=True)
    wanted = jnp.maximum(asked, 0)
    tp_count = lax.axis_size("tp")
    half = tp_index % 2
    partner = [(i, i ^ 1) for i in range(tp_count)]
    own_cache = jnp.where(half == 0, cache_keys, cache_values)
    head_cache = lax.dynamic_slice_in_dim(own_cache, kv_head * HD, HD, 2)
    arrival_index = holders * capacity + ranking
    outgoing = head_cache[wanted]
    arrived = lax.all_to_all(outgoing, "req", split_axis=0, concat_axis=0, tiled=True)
    swapped = lax.ppermute(arrived, "tp", partner)
    key_pages = jnp.where(half == 0, arrived, swapped)
    value_pages = jnp.where(half == 0, swapped, arrived)
    context_keys = key_pages.reshape(req_count * capacity, page_len, HD)[arrival_index].reshape(
        page_total * page_len, HD
    )
    context_values = value_pages.reshape(req_count * capacity, page_len, HD)[
        arrival_index
    ].reshape(page_total * page_len, HD)
    fresh_keys = lax.dynamic_slice_in_dim(new_keys, kv_head * HD, HD, 1)
    fresh_values = lax.dynamic_slice_in_dim(new_values, kv_head * HD, HD, 1)
    all_keys = jnp.concatenate([context_keys, fresh_keys], axis=0)
    all_values = jnp.concatenate([context_values, fresh_values], axis=0)
    attention = sparse_attention(
        queries, all_keys, all_values, page_counts[0], last_fill[0], row_counts[0], page_len
    )
    tp_size = lax.axis_size("tp")
    full_weight = lax.all_gather(out_weight, "tp", axis=0, tiled=True)
    full_gate_weight = lax.all_gather(ple_gate_weight, "tp", axis=0, tiled=True)
    full_proj_weight = lax.all_gather(ple_proj_weight, "tp", axis=1, tiled=True)
    hidden_parts = hidden.reshape(tp_size, -1, hidden.shape[1])
    gain_rows = jnp.zeros((8, hidden.shape[1]), hidden.dtype).at[0].set(attn_gain).at[1].set(ple_gain)
    with_gains = jnp.concatenate(
        [hidden_parts, jnp.broadcast_to(gain_rows[None], (tp_size, 8, hidden.shape[1]))], axis=1
    )
    row_hidden_gains = lax.all_to_all(
        with_gains.reshape(-1, hidden.shape[1]), "tp", split_axis=0, concat_axis=1, tiled=True
    )
    row_hidden = row_hidden_gains[: hidden_parts.shape[1]]
    full_attn_gain = row_hidden_gains[hidden_parts.shape[1]]
    full_ple_gain = row_hidden_gains[hidden_parts.shape[1] + 1]
    row_attention = lax.all_to_all(attention, "tp", split_axis=0, concat_axis=1, tiled=True)
    part_rows = row_attention.shape[0]
    row_ple = lax.dynamic_slice_in_dim(ple_input, tp_index * part_rows, part_rows, 0)
    projected = jnp.dot(row_attention, full_weight, preferred_element_type=jnp.float32)
    squares = jnp.sum(projected * projected, axis=1)
    normed = (
        projected
        * lax.rsqrt(squares / D + 1e-06)[:, None]
        * full_attn_gain.astype(jnp.float32)[None, :]
    )
    mixed_state = (row_hidden.astype(jnp.float32) + normed).astype(jnp.bfloat16)
    gate = jnp.dot(mixed_state, full_gate_weight, preferred_element_type=jnp.float32)
    activated = (jax.nn.gelu(gate, approximate=True) * row_ple.astype(jnp.float32)).astype(
        jnp.bfloat16
    )
    lifted = jnp.dot(activated, full_proj_weight, preferred_element_type=jnp.float32)
    lift_squares = jnp.sum(lifted * lifted, axis=1)
    lift_normed = (
        lifted
        * lax.rsqrt(lift_squares / D + 1e-06)[:, None]
        * full_ple_gain.astype(jnp.float32)[None, :]
    )
    row_out = (mixed_state.astype(jnp.float32) + lift_normed).astype(jnp.bfloat16)
    return lax.all_to_all(row_out, "tp", split_axis=1, concat_axis=0, tiled=True)


def solution(mesh):
    return jax.shard_map(
        shards,
        mesh=mesh,
        in_specs=(
            P("req", "tp"),
            P("req", "tp"),
            P("req", None),
            P("req", None),
            P("req", None, None),
            P("req", None, None),
            P("tp", None),
            P("tp"),
            P("req", None),
            P("tp", None),
            P(None, "tp"),
            P("tp"),
            P("req", None),
            P("req", None),
            P("req", None),
            P("req", None),
            P("req", None),
        ),
        out_specs=P("req", "tp"),
        check_vma=False,
    )
```

```python
import math

import jax
import jax.numpy as jnp
from jax import lax
from jax.experimental import pallas as pl
from jax.experimental.pallas import tpu as pltpu
from jax.sharding import PartitionSpec as P

D = 2048
HD = 256


def slot_lookup(positions, counts):
    starts = jnp.cumsum(counts) - counts
    owning = jnp.sum((positions[:, None] >= starts[None, :]).astype(jnp.int32), axis=1) - 1
    return (owning, starts)


def table_pick(table, owning):
    onehot = owning[:, None] == jnp.arange(table.shape[0], dtype=jnp.int32)[None, :]
    return jnp.sum(jnp.where(onehot, table[None, :], 0), axis=1)


def attend_masks(counts_of_pages, fill_row, counts_of_rows, page_len, page_total, row_total):
    key_index = jnp.arange(page_total * page_len, dtype=jnp.int32)
    page_ref = key_index // page_len
    within = key_index % page_len
    page_owner, page_starts = slot_lookup(page_ref, counts_of_pages)
    context_len = (counts_of_pages - 1) * page_len + fill_row
    position = (page_ref - table_pick(page_starts, page_owner)) * page_len + within
    valid = position < table_pick(context_len, page_owner)
    row_index = jnp.arange(row_total, dtype=jnp.int32)
    row_owner = slot_lookup(row_index, counts_of_rows)[0]
    context_mask = (row_owner[:, None] == page_owner[None, :]) & valid[None, :]
    causal = (row_owner[:, None] == row_owner[None, :]) & (row_index[None, :] <= row_index[:, None])
    return jnp.concatenate([context_mask, causal], axis=1)


ROW_BLOCK = 128
KEY_CHUNK = 256


def pick(table, index):
    onehot = index[:, None] == jnp.arange(table.shape[0], dtype=jnp.int32)[None, :]
    return jnp.sum(jnp.where(onehot, table[None, :], 0), axis=1)


def attention_kernel(
    ranges_ref,
    slots_ref,
    meta_ref,
    q_ref,
    own_ref,
    partner_ref,
    fresh_k_ref,
    fresh_v_ref,
    kown_ref,
    kpos_ref,
    rown_ref,
    o_ref,
    s_scr,
    acc_scr,
):
    block = pl.program_id(0)
    ctx_lo = ranges_ref[block, 0]
    ctx_n = ranges_ref[block, 1]
    new_lo = ranges_ref[block, 2]
    total = ctx_n + ranges_ref[block, 3]
    ctx_chunks = ranges_ref[block, 4]
    keys_are_own = meta_ref[0] == 0
    heads = q_ref.shape[1] // HD
    page_len = own_ref.shape[1]
    per_chunk = KEY_CHUNK // page_len
    q = q_ref[...]
    stacked = jnp.concatenate([q[:, h * HD:(h + 1) * HD] for h in range(heads)], axis=0)
    row_owner = rown_ref[...]
    row_index = block * ROW_BLOCK + lax.broadcasted_iota(jnp.int32, (ROW_BLOCK, 1), 0)
    scale = 1.0 / math.sqrt(HD)

    def chunk_of(t):
        return jnp.where(t < ctx_n, ctx_lo + t, ctx_chunks + new_lo + t - ctx_n)

    def load_chunk(c, want_keys, fresh_ref):
        pick_own = keys_are_own == want_keys

        def cached():
            pages = []
            for i in range(per_chunk):
                slot = slots_ref[c * per_chunk + i]
                pages.append(jnp.where(pick_own, own_ref[slot], partner_ref[slot]))
            return jnp.concatenate(pages, axis=0)

        def fresh():
            start = pl.multiple_of((c - ctx_chunks) * KEY_CHUNK, KEY_CHUNK)
            return fresh_ref[pl.ds(start, KEY_CHUNK), :]

        return lax.cond(c < ctx_chunks, cached, fresh)

    def scores_pass(t, highest):
        c = chunk_of(t)
        keys = load_chunk(c, True, fresh_k_ref)
        s = lax.dot_general(
            stacked, keys, (((1,), (1,)), ((), ())), preferred_element_type=jnp.float32
        ) * scale
        seen = (kown_ref[c] == row_owner) & (kpos_ref[c] <= row_index)
        seen = jnp.concatenate([seen] * heads, axis=0)
        s = jnp.where(seen, s, -1e30)
        s_scr[c] = s
        return jnp.maximum(highest, jnp.max(s, axis=1, keepdims=True))

    highest = lax.fori_loop(
        0, total, scores_pass, jnp.full((heads * ROW_BLOCK, 1), -1e30, jnp.float32)
    )

    def exp_pass(t, summed):
        c = chunk_of(t)
        e = jnp.exp(s_scr[c] - highest)
        s_scr[c] = e
        return summed + jnp.sum(e, axis=1, keepdims=True)

    summed = lax.fori_loop(0, total, exp_pass, jnp.zeros((heads * ROW_BLOCK, 1), jnp.float32))
    inverse = 1.0 / summed
    acc_scr[...] = jnp.zeros(acc_scr.shape, jnp.float32)

    def value_pass(t, carry):
        c = chunk_of(t)
        w = (s_scr[c] * inverse).astype(jnp.bfloat16)
        values = load_chunk(c, False, fresh_v_ref)
        acc_scr[...] += jnp.dot(w, values, preferred_element_type=jnp.float32)
        return carry

    lax.fori_loop(0, total, value_pass, 0)
    for h in range(heads):
        o_ref[:, h * HD:(h + 1) * HD] = acc_scr[h * ROW_BLOCK:(h + 1) * ROW_BLOCK, :].astype(
            jnp.bfloat16
        )


def sparse_attention(
    queries, own_pages, partner_pages, slots, new_keys, new_values, half, kv_head,
    page_counts, last_fill, row_counts, page_total,
):
    row_total = queries.shape[0]
    page_len = own_pages.shape[1]
    ctx_total = page_total * page_len
    key_total = ctx_total + row_total
    heads = queries.shape[1] // HD
    blocks = row_total // ROW_BLOCK
    chunks = key_total // KEY_CHUNK
    ctx_chunks = ctx_total // KEY_CHUNK
    key_index = jnp.arange(ctx_total, dtype=jnp.int32)
    page_ref = key_index // page_len
    page_owner, page_starts = slot_lookup(page_ref, page_counts)
    context_len = (page_counts - 1) * page_len + last_fill
    position = (page_ref - table_pick(page_starts, page_owner)) * page_len + key_index % page_len
    valid = position < table_pick(context_len, page_owner)
    row_index = jnp.arange(row_total, dtype=jnp.int32)
    row_owner, row_starts = slot_lookup(row_index, row_counts)
    key_owner = jnp.concatenate([jnp.where(valid, page_owner, -1), row_owner])
    key_pos = jnp.concatenate([jnp.full((ctx_total,), -1, jnp.int32), row_index])
    first = row_owner[::ROW_BLOCK]
    last = row_owner[ROW_BLOCK - 1::ROW_BLOCK]
    ctx_from = pick(page_starts, first) * page_len
    ctx_to = (pick(page_starts, last) + pick(page_counts, last)) * page_len
    ctx_lo = ctx_from // KEY_CHUNK
    ctx_n = (ctx_to + KEY_CHUNK - 1) // KEY_CHUNK - ctx_lo
    new_from = pick(row_starts, first)
    new_to = jnp.arange(1, blocks + 1, dtype=jnp.int32) * ROW_BLOCK
    new_lo = new_from // KEY_CHUNK
    new_n = (new_to + KEY_CHUNK - 1) // KEY_CHUNK - new_lo
    ranges = jnp.stack(
        [ctx_lo, ctx_n, new_lo, new_n, jnp.full((blocks,), ctx_chunks, jnp.int32)], axis=1
    ).astype(jnp.int32)
    meta = jnp.stack([half, kv_head]).astype(jnp.int32)
    whole = lambda b, r, s, m: (0, 0, 0)
    return pl.pallas_call(
        attention_kernel,
        grid_spec=pltpu.PrefetchScalarGridSpec(
            num_scalar_prefetch=3,
            grid=(blocks,),
            in_specs=[
                pl.BlockSpec((ROW_BLOCK, heads * HD), lambda b, r, s, m: (b, 0)),
                pl.BlockSpec(own_pages.shape, whole),
                pl.BlockSpec(partner_pages.shape, whole),
                pl.BlockSpec((row_total, HD), lambda b, r, s, m: (0, m[1])),
                pl.BlockSpec((row_total, HD), lambda b, r, s, m: (0, m[1])),
                pl.BlockSpec((chunks, 1, KEY_CHUNK), whole),
                pl.BlockSpec((chunks, 1, KEY_CHUNK), whole),
                pl.BlockSpec((ROW_BLOCK, 1), lambda b, r, s, m: (b, 0)),
            ],
            out_specs=pl.BlockSpec((ROW_BLOCK, heads * HD), lambda b, r, s, m: (b, 0)),
            scratch_shapes=[
                pltpu.VMEM((chunks, heads * ROW_BLOCK, KEY_CHUNK), jnp.float32),
                pltpu.VMEM((heads * ROW_BLOCK, HD), jnp.float32),
            ],
        ),
        out_shape=jax.ShapeDtypeStruct((row_total, heads * HD), jnp.bfloat16),
    )(
        ranges,
        slots.astype(jnp.int32),
        meta,
        queries,
        own_pages,
        partner_pages,
        new_keys,
        new_values,
        key_owner.reshape(chunks, 1, KEY_CHUNK),
        key_pos.reshape(chunks, 1, KEY_CHUNK),
        row_owner.reshape(row_total, 1),
    )


def shards(
    hidden,
    queries,
    new_keys,
    new_values,
    cache_keys,
    cache_values,
    out_weight,
    attn_gain,
    ple_input,
    ple_gate_weight,
    ple_proj_weight,
    ple_gain,
    page_holder,
    page_slot,
    page_counts,
    last_fill,
    row_counts,
):
    row_total = hidden.shape[0]
    page_total = cache_keys.shape[0]
    page_len = cache_keys.shape[1]
    req_count = lax.axis_size("req")
    tp_index = lax.axis_index("tp")
    local_heads = queries.shape[1] // HD
    kv_head = tp_index // 2
    capacity = max(2, page_total // req_count)
    holders = page_holder[:, 0]
    places = page_slot[:, 0]
    ref_index = jnp.arange(page_total, dtype=jnp.int32)
    earlier = (holders[:, None] == holders[None, :]) & (ref_index[:, None] > ref_index[None, :])
    ranking = jnp.sum(earlier.astype(jnp.int32), axis=1)
    matched = (holders[:, None, None] == jnp.arange(req_count, dtype=jnp.int32)[None, :, None]) & (
        ranking[:, None, None] == jnp.arange(capacity, dtype=jnp.int32)[None, None, :]
    )
    request_table = jnp.sum(jnp.where(matched, places[:, None, None] + 1, 0), axis=0) - 1
    asked = lax.all_to_all(request_table, "req", split_axis=0, concat_axis=0, tiled=True)
    wanted = jnp.maximum(asked, 0)
    tp_count = lax.axis_size("tp")
    half = tp_index % 2
    partner = [(i, i ^ 1) for i in range(tp_count)]
    arrival_index = holders * capacity + ranking

    def fetch_pages(cache):
        return lax.dynamic_slice_in_dim(cache, kv_head * HD, HD, 2)[wanted]

    outgoing = lax.cond(
        half == 0, lambda: fetch_pages(cache_keys), lambda: fetch_pages(cache_values)
    )
    arrived = lax.all_to_all(outgoing, "req", split_axis=0, concat_axis=0, tiled=True)
    swapped = lax.ppermute(arrived, "tp", partner)
    attention = sparse_attention(
        queries,
        arrived.reshape(-1, page_len, HD),
        swapped.reshape(-1, page_len, HD),
        arrival_index,
        new_keys,
        new_values,
        half,
        kv_head,
        page_counts[0], last_fill[0], row_counts[0], page_total,
    )
    tp_size = lax.axis_size("tp")
    full_weight = lax.all_gather(out_weight, "tp", axis=0, tiled=True)
    full_gate_weight = lax.all_gather(ple_gate_weight, "tp", axis=0, tiled=True)
    full_proj_weight = lax.all_gather(ple_proj_weight, "tp", axis=1, tiled=True)
    hidden_parts = hidden.reshape(tp_size, -1, hidden.shape[1])
    gain_rows = jnp.zeros((8, hidden.shape[1]), hidden.dtype).at[0].set(attn_gain).at[1].set(ple_gain)
    with_gains = jnp.concatenate(
        [hidden_parts, jnp.broadcast_to(gain_rows[None], (tp_size, 8, hidden.shape[1]))], axis=1
    )
    row_hidden_gains = lax.all_to_all(
        with_gains.reshape(-1, hidden.shape[1]), "tp", split_axis=0, concat_axis=1, tiled=True
    )
    row_hidden = row_hidden_gains[: hidden_parts.shape[1]]
    full_attn_gain = row_hidden_gains[hidden_parts.shape[1]]
    full_ple_gain = row_hidden_gains[hidden_parts.shape[1] + 1]
    row_attention = lax.all_to_all(attention, "tp", split_axis=0, concat_axis=1, tiled=True)
    part_rows = row_attention.shape[0]
    row_ple = lax.dynamic_slice_in_dim(ple_input, tp_index * part_rows, part_rows, 0)
    projected = jnp.dot(row_attention, full_weight, preferred_element_type=jnp.float32)
    squares = jnp.sum(projected * projected, axis=1)
    normed = (
        projected
        * lax.rsqrt(squares / D + 1e-06)[:, None]
        * full_attn_gain.astype(jnp.float32)[None, :]
    )
    mixed_state = (row_hidden.astype(jnp.float32) + normed).astype(jnp.bfloat16)
    gate = jnp.dot(mixed_state, full_gate_weight, preferred_element_type=jnp.float32)
    activated = (jax.nn.gelu(gate, approximate=True) * row_ple.astype(jnp.float32)).astype(
        jnp.bfloat16
    )
    lifted = jnp.dot(activated, full_proj_weight, preferred_element_type=jnp.float32)
    lift_squares = jnp.sum(lifted * lifted, axis=1)
    lift_normed = (
        lifted
        * lax.rsqrt(lift_squares / D + 1e-06)[:, None]
        * full_ple_gain.astype(jnp.float32)[None, :]
    )
    row_out = (mixed_state.astype(jnp.float32) + lift_normed).astype(jnp.bfloat16)
    return lax.all_to_all(row_out, "tp", split_axis=1, concat_axis=0, tiled=True)


def solution(mesh):
    return jax.shard_map(
        shards,
        mesh=mesh,
        in_specs=(
            P("req", "tp"),
            P("req", "tp"),
            P("req", None),
            P("req", None),
            P("req", None, None),
            P("req", None, None),
            P("tp", None),
            P("tp"),
            P("req", None),
            P("tp", None),
            P(None, "tp"),
            P("tp"),
            P("req", None),
            P("req", None),
            P("req", None),
            P("req", None),
            P("req", None),
        ),
        out_specs=P("req", "tp"),
        check_vma=False,
    )
```

```python
import math

import jax
import jax.numpy as jnp
from jax import lax
from jax.experimental import pallas as pl
from jax.experimental.pallas import tpu as pltpu
from jax.sharding import PartitionSpec as P

D = 2048
HD = 256


def slot_lookup(positions, counts):
    starts = jnp.cumsum(counts) - counts
    owning = jnp.sum((positions[:, None] >= starts[None, :]).astype(jnp.int32), axis=1) - 1
    return (owning, starts)


def table_pick(table, owning):
    onehot = owning[:, None] == jnp.arange(table.shape[0], dtype=jnp.int32)[None, :]
    return jnp.sum(jnp.where(onehot, table[None, :], 0), axis=1)


def attend_masks(counts_of_pages, fill_row, counts_of_rows, page_len, page_total, row_total):
    key_index = jnp.arange(page_total * page_len, dtype=jnp.int32)
    page_ref = key_index // page_len
    within = key_index % page_len
    page_owner, page_starts = slot_lookup(page_ref, counts_of_pages)
    context_len = (counts_of_pages - 1) * page_len + fill_row
    position = (page_ref - table_pick(page_starts, page_owner)) * page_len + within
    valid = position < table_pick(context_len, page_owner)
    row_index = jnp.arange(row_total, dtype=jnp.int32)
    row_owner = slot_lookup(row_index, counts_of_rows)[0]
    context_mask = (row_owner[:, None] == page_owner[None, :]) & valid[None, :]
    causal = (row_owner[:, None] == row_owner[None, :]) & (row_index[None, :] <= row_index[:, None])
    return jnp.concatenate([context_mask, causal], axis=1)


ROW_BLOCK = 128
KEY_CHUNK = 256


def pick(table, index):
    onehot = index[:, None] == jnp.arange(table.shape[0], dtype=jnp.int32)[None, :]
    return jnp.sum(jnp.where(onehot, table[None, :], 0), axis=1)


def attention_kernel(
    ranges_ref,
    slots_ref,
    meta_ref,
    q_ref,
    own_ref,
    partner_ref,
    fresh_k_ref,
    fresh_v_ref,
    kown_ref,
    kpos_ref,
    rown_ref,
    o_ref,
    s_scr,
    acc_scr,
):
    block = pl.program_id(0)
    ctx_lo = ranges_ref[block, 0]
    ctx_n = ranges_ref[block, 1]
    new_lo = ranges_ref[block, 2]
    total = ctx_n + ranges_ref[block, 3]
    ctx_chunks = ranges_ref[block, 4]
    keys_are_own = meta_ref[0] == 0
    heads = q_ref.shape[1] // HD
    page_len = own_ref.shape[1]
    per_chunk = KEY_CHUNK // page_len
    q = q_ref[...]
    stacked = jnp.concatenate([q[:, h * HD:(h + 1) * HD] for h in range(heads)], axis=0)
    row_owner = rown_ref[...]
    row_index = block * ROW_BLOCK + lax.broadcasted_iota(jnp.int32, (ROW_BLOCK, 1), 0)
    scale = 1.0 / math.sqrt(HD)

    def chunk_of(t):
        return jnp.where(t < ctx_n, ctx_lo + t, ctx_chunks + new_lo + t - ctx_n)

    def load_chunk(c, want_keys, fresh_ref):
        pick_own = keys_are_own == want_keys

        def cached():
            pages = []
            for i in range(per_chunk):
                slot = slots_ref[c * per_chunk + i]
                pages.append(jnp.where(pick_own, own_ref[slot], partner_ref[slot]))
            return jnp.concatenate(pages, axis=0)

        def fresh():
            start = pl.multiple_of((c - ctx_chunks) * KEY_CHUNK, KEY_CHUNK)
            return fresh_ref[pl.ds(start, KEY_CHUNK), :]

        return lax.cond(c < ctx_chunks, cached, fresh)

    def scores_pass(t, highest):
        c = chunk_of(t)
        keys = load_chunk(c, True, fresh_k_ref)
        s = lax.dot_general(
            stacked, keys, (((1,), (1,)), ((), ())), preferred_element_type=jnp.float32
        ) * scale
        seen = (kown_ref[c] == row_owner) & (kpos_ref[c] <= row_index)
        seen = jnp.concatenate([seen] * heads, axis=0)
        s = jnp.where(seen, s, -1e30)
        s_scr[c] = s
        return jnp.maximum(highest, jnp.max(s, axis=1, keepdims=True))

    highest = lax.fori_loop(
        0, total, scores_pass, jnp.full((heads * ROW_BLOCK, 1), -1e30, jnp.float32)
    )

    def exp_pass(t, summed):
        c = chunk_of(t)
        e = jnp.exp(s_scr[c] - highest)
        s_scr[c] = e
        return summed + jnp.sum(e, axis=1, keepdims=True)

    summed = lax.fori_loop(0, total, exp_pass, jnp.zeros((heads * ROW_BLOCK, 1), jnp.float32))
    inverse = 1.0 / summed
    acc_scr[...] = jnp.zeros(acc_scr.shape, jnp.float32)

    def value_pass(t, carry):
        c = chunk_of(t)
        w = (s_scr[c] * inverse).astype(jnp.bfloat16)
        values = load_chunk(c, False, fresh_v_ref)
        acc_scr[...] += jnp.dot(w, values, preferred_element_type=jnp.float32)
        return carry

    lax.fori_loop(0, total, value_pass, 0)
    for h in range(heads):
        o_ref[:, h * HD:(h + 1) * HD] = acc_scr[h * ROW_BLOCK:(h + 1) * ROW_BLOCK, :].astype(
            jnp.bfloat16
        )


def sparse_attention(
    queries, own_pages, partner_pages, slots, new_keys, new_values, half, kv_head,
    page_counts, last_fill, row_counts, page_total,
):
    row_total = queries.shape[0]
    page_len = own_pages.shape[1]
    ctx_total = page_total * page_len
    key_total = ctx_total + row_total
    heads = queries.shape[1] // HD
    blocks = row_total // ROW_BLOCK
    chunks = key_total // KEY_CHUNK
    ctx_chunks = ctx_total // KEY_CHUNK
    key_index = jnp.arange(ctx_total, dtype=jnp.int32)
    page_ref = key_index // page_len
    page_owner, page_starts = slot_lookup(page_ref, page_counts)
    context_len = (page_counts - 1) * page_len + last_fill
    position = (page_ref - table_pick(page_starts, page_owner)) * page_len + key_index % page_len
    valid = position < table_pick(context_len, page_owner)
    row_index = jnp.arange(row_total, dtype=jnp.int32)
    row_owner, row_starts = slot_lookup(row_index, row_counts)
    key_owner = jnp.concatenate([jnp.where(valid, page_owner, -1), row_owner])
    key_pos = jnp.concatenate([jnp.full((ctx_total,), -1, jnp.int32), row_index])
    first = row_owner[::ROW_BLOCK]
    last = row_owner[ROW_BLOCK - 1::ROW_BLOCK]
    ctx_from = pick(page_starts, first) * page_len
    ctx_to = (pick(page_starts, last) + pick(page_counts, last)) * page_len
    ctx_lo = ctx_from // KEY_CHUNK
    ctx_n = (ctx_to + KEY_CHUNK - 1) // KEY_CHUNK - ctx_lo
    new_from = pick(row_starts, first)
    new_to = jnp.arange(1, blocks + 1, dtype=jnp.int32) * ROW_BLOCK
    new_lo = new_from // KEY_CHUNK
    new_n = (new_to + KEY_CHUNK - 1) // KEY_CHUNK - new_lo
    ranges = jnp.stack(
        [ctx_lo, ctx_n, new_lo, new_n, jnp.full((blocks,), ctx_chunks, jnp.int32)], axis=1
    ).astype(jnp.int32)
    meta = jnp.stack([half, kv_head]).astype(jnp.int32)
    whole = lambda b, r, s, m: (0, 0, 0)
    return pl.pallas_call(
        attention_kernel,
        grid_spec=pltpu.PrefetchScalarGridSpec(
            num_scalar_prefetch=3,
            grid=(blocks,),
            in_specs=[
                pl.BlockSpec((ROW_BLOCK, heads * HD), lambda b, r, s, m: (b, 0)),
                pl.BlockSpec(own_pages.shape, whole),
                pl.BlockSpec(partner_pages.shape, whole),
                pl.BlockSpec((row_total, HD), lambda b, r, s, m: (0, m[1])),
                pl.BlockSpec((row_total, HD), lambda b, r, s, m: (0, m[1])),
                pl.BlockSpec((chunks, 1, KEY_CHUNK), whole),
                pl.BlockSpec((chunks, 1, KEY_CHUNK), whole),
                pl.BlockSpec((ROW_BLOCK, 1), lambda b, r, s, m: (b, 0)),
            ],
            out_specs=pl.BlockSpec((ROW_BLOCK, heads * HD), lambda b, r, s, m: (b, 0)),
            scratch_shapes=[
                pltpu.VMEM((chunks, heads * ROW_BLOCK, KEY_CHUNK), jnp.float32),
                pltpu.VMEM((heads * ROW_BLOCK, HD), jnp.float32),
            ],
        ),
        out_shape=jax.ShapeDtypeStruct((row_total, heads * HD), jnp.bfloat16),
    )(
        ranges,
        slots.astype(jnp.int32),
        meta,
        queries,
        own_pages,
        partner_pages,
        new_keys,
        new_values,
        key_owner.reshape(chunks, 1, KEY_CHUNK),
        key_pos.reshape(chunks, 1, KEY_CHUNK),
        row_owner.reshape(row_total, 1),
    )


def rows_to_columns(x, axis_name):
    count = lax.axis_size(axis_name)
    me = lax.axis_index(axis_name)
    parts = x.reshape(count, x.shape[0] // count, x.shape[1])
    received = [parts[me]]
    for shift in range(1, count):
        outgoing = lax.dynamic_index_in_dim(parts, (me + shift) % count, 0, keepdims=False)
        perm = [(i, (i + shift) % count) for i in range(count)]
        received.append(lax.ppermute(outgoing, axis_name, perm))
    order = (me - jnp.arange(count, dtype=jnp.int32)) % count
    blocks = jnp.stack(received)[order]
    return jnp.transpose(blocks, (1, 0, 2)).reshape(parts.shape[1], count * x.shape[1])


def columns_to_rows(x, axis_name):
    count = lax.axis_size(axis_name)
    me = lax.axis_index(axis_name)
    width = x.shape[1] // count
    received = [lax.dynamic_slice_in_dim(x, me * width, width, 1)]
    for shift in range(1, count):
        outgoing = lax.dynamic_slice_in_dim(x, ((me + shift) % count) * width, width, 1)
        perm = [(i, (i + shift) % count) for i in range(count)]
        received.append(lax.ppermute(outgoing, axis_name, perm))
    order = (me - jnp.arange(count, dtype=jnp.int32)) % count
    return jnp.stack(received)[order].reshape(count * x.shape[0], width)


def shards(
    hidden,
    queries,
    new_keys,
    new_values,
    cache_keys,
    cache_values,
    out_weight,
    attn_gain,
    ple_input,
    ple_gate_weight,
    ple_proj_weight,
    ple_gain,
    page_holder,
    page_slot,
    page_counts,
    last_fill,
    row_counts,
):
    row_total = hidden.shape[0]
    page_total = cache_keys.shape[0]
    page_len = cache_keys.shape[1]
    req_count = lax.axis_size("req")
    tp_index = lax.axis_index("tp")
    local_heads = queries.shape[1] // HD
    kv_head = tp_index // 2
    capacity = max(2, page_total // req_count)
    holders = page_holder[:, 0]
    places = page_slot[:, 0]
    ref_index = jnp.arange(page_total, dtype=jnp.int32)
    earlier = (holders[:, None] == holders[None, :]) & (ref_index[:, None] > ref_index[None, :])
    ranking = jnp.sum(earlier.astype(jnp.int32), axis=1)
    matched = (holders[:, None, None] == jnp.arange(req_count, dtype=jnp.int32)[None, :, None]) & (
        ranking[:, None, None] == jnp.arange(capacity, dtype=jnp.int32)[None, None, :]
    )
    request_table = jnp.sum(jnp.where(matched, places[:, None, None] + 1, 0), axis=0) - 1
    asked = lax.all_to_all(request_table, "req", split_axis=0, concat_axis=0, tiled=True)
    wanted = jnp.maximum(asked, 0)
    tp_count = lax.axis_size("tp")
    half = tp_index % 2
    partner = [(i, i ^ 1) for i in range(tp_count)]
    arrival_index = holders * capacity + ranking

    def fetch_pages(cache):
        return cache.reshape(page_total, page_len, -1, HD)[wanted, :, kv_head]

    outgoing = lax.cond(
        half == 0, lambda: fetch_pages(cache_keys), lambda: fetch_pages(cache_values)
    )
    arrived = lax.all_to_all(outgoing, "req", split_axis=0, concat_axis=0, tiled=True)
    swapped = lax.ppermute(arrived, "tp", partner)
    attention = sparse_attention(
        queries,
        arrived.reshape(-1, page_len, HD),
        swapped.reshape(-1, page_len, HD),
        arrival_index,
        new_keys,
        new_values,
        half,
        kv_head,
        page_counts[0], last_fill[0], row_counts[0], page_total,
    )
    tp_size = lax.axis_size("tp")
    full_weight = lax.all_gather(out_weight, "tp", axis=0, tiled=True)
    full_gate_weight = lax.all_gather(ple_gate_weight, "tp", axis=0, tiled=True)
    full_proj_weight = lax.all_gather(ple_proj_weight, "tp", axis=1, tiled=True)
    hidden_parts = hidden.reshape(tp_size, -1, hidden.shape[1])
    gain_rows = jnp.zeros((8, hidden.shape[1]), hidden.dtype).at[0].set(attn_gain).at[1].set(ple_gain)
    with_gains = jnp.concatenate(
        [hidden_parts, jnp.broadcast_to(gain_rows[None], (tp_size, 8, hidden.shape[1]))], axis=1
    )
    row_hidden_gains = rows_to_columns(with_gains.reshape(-1, hidden.shape[1]), "tp")
    row_hidden = row_hidden_gains[: hidden_parts.shape[1]]
    full_attn_gain = row_hidden_gains[hidden_parts.shape[1]]
    full_ple_gain = row_hidden_gains[hidden_parts.shape[1] + 1]
    row_attention = rows_to_columns(attention, "tp")
    part_rows = row_attention.shape[0]
    row_ple = lax.dynamic_slice_in_dim(ple_input, tp_index * part_rows, part_rows, 0)
    projected = jnp.dot(row_attention, full_weight, preferred_element_type=jnp.float32)
    squares = jnp.sum(projected * projected, axis=1)
    normed = (
        projected
        * lax.rsqrt(squares / D + 1e-06)[:, None]
        * full_attn_gain.astype(jnp.float32)[None, :]
    )
    mixed_state = (row_hidden.astype(jnp.float32) + normed).astype(jnp.bfloat16)
    gate = jnp.dot(mixed_state, full_gate_weight, preferred_element_type=jnp.float32)
    activated = (jax.nn.gelu(gate, approximate=True) * row_ple.astype(jnp.float32)).astype(
        jnp.bfloat16
    )
    lifted = jnp.dot(activated, full_proj_weight, preferred_element_type=jnp.float32)
    lift_squares = jnp.sum(lifted * lifted, axis=1)
    lift_normed = (
        lifted
        * lax.rsqrt(lift_squares / D + 1e-06)[:, None]
        * full_ple_gain.astype(jnp.float32)[None, :]
    )
    row_out = (mixed_state.astype(jnp.float32) + lift_normed).astype(jnp.bfloat16)
    return columns_to_rows(row_out, "tp")


def solution(mesh):
    return jax.shard_map(
        shards,
        mesh=mesh,
        in_specs=(
            P("req", "tp"),
            P("req", "tp"),
            P("req", None),
            P("req", None),
            P("req", None, None),
            P("req", None, None),
            P("tp", None),
            P("tp"),
            P("req", None),
            P("tp", None),
            P(None, "tp"),
            P("tp"),
            P("req", None),
            P("req", None),
            P("req", None),
            P("req", None),
            P("req", None),
        ),
        out_specs=P("req", "tp"),
        check_vma=False,
    )
```

```python
import math

import jax
import jax.numpy as jnp
from jax import lax
from jax.experimental import pallas as pl
from jax.experimental.pallas import tpu as pltpu
from jax.sharding import PartitionSpec as P

D = 2048
HD = 256


def slot_lookup(positions, counts):
    starts = jnp.cumsum(counts) - counts
    owning = jnp.sum((positions[:, None] >= starts[None, :]).astype(jnp.int32), axis=1) - 1
    return (owning, starts)


def table_pick(table, owning):
    onehot = owning[:, None] == jnp.arange(table.shape[0], dtype=jnp.int32)[None, :]
    return jnp.sum(jnp.where(onehot, table[None, :], 0), axis=1)


def attend_masks(counts_of_pages, fill_row, counts_of_rows, page_len, page_total, row_total):
    key_index = jnp.arange(page_total * page_len, dtype=jnp.int32)
    page_ref = key_index // page_len
    within = key_index % page_len
    page_owner, page_starts = slot_lookup(page_ref, counts_of_pages)
    context_len = (counts_of_pages - 1) * page_len + fill_row
    position = (page_ref - table_pick(page_starts, page_owner)) * page_len + within
    valid = position < table_pick(context_len, page_owner)
    row_index = jnp.arange(row_total, dtype=jnp.int32)
    row_owner = slot_lookup(row_index, counts_of_rows)[0]
    context_mask = (row_owner[:, None] == page_owner[None, :]) & valid[None, :]
    causal = (row_owner[:, None] == row_owner[None, :]) & (row_index[None, :] <= row_index[:, None])
    return jnp.concatenate([context_mask, causal], axis=1)


ROW_BLOCK = 128
KEY_CHUNK = 256


def pick(table, index):
    onehot = index[:, None] == jnp.arange(table.shape[0], dtype=jnp.int32)[None, :]
    return jnp.sum(jnp.where(onehot, table[None, :], 0), axis=1)


def attention_kernel(
    ranges_ref,
    slots_ref,
    meta_ref,
    q_ref,
    own_ref,
    partner_ref,
    fresh_k_ref,
    fresh_v_ref,
    kown_ref,
    kpos_ref,
    rown_ref,
    o_ref,
    s_scr,
    acc_scr,
):
    block = pl.program_id(0)
    ctx_lo = ranges_ref[block, 0]
    ctx_n = ranges_ref[block, 1]
    new_lo = ranges_ref[block, 2]
    total = ctx_n + ranges_ref[block, 3]
    ctx_chunks = ranges_ref[block, 4]
    keys_are_own = meta_ref[0] == 0
    heads = q_ref.shape[1] // HD
    page_len = own_ref.shape[1]
    per_chunk = KEY_CHUNK // page_len
    q = q_ref[...]
    stacked = jnp.concatenate([q[:, h * HD:(h + 1) * HD] for h in range(heads)], axis=0)
    row_owner = rown_ref[...]
    row_index = block * ROW_BLOCK + lax.broadcasted_iota(jnp.int32, (ROW_BLOCK, 1), 0)
    scale = 1.0 / math.sqrt(HD)

    def chunk_of(t):
        return jnp.where(t < ctx_n, ctx_lo + t, ctx_chunks + new_lo + t - ctx_n)

    def load_chunk(c, want_keys, fresh_ref):
        pick_own = keys_are_own == want_keys

        def cached():
            pages = []
            for i in range(per_chunk):
                slot = slots_ref[c * per_chunk + i]
                pages.append(jnp.where(pick_own, own_ref[slot], partner_ref[slot]))
            return jnp.concatenate(pages, axis=0)

        def fresh():
            start = pl.multiple_of((c - ctx_chunks) * KEY_CHUNK, KEY_CHUNK)
            return fresh_ref[pl.ds(start, KEY_CHUNK), :]

        return lax.cond(c < ctx_chunks, cached, fresh)

    def scores_pass(t, highest):
        c = chunk_of(t)
        keys = load_chunk(c, True, fresh_k_ref)
        s = lax.dot_general(
            stacked, keys, (((1,), (1,)), ((), ())), preferred_element_type=jnp.float32
        ) * scale
        seen = (kown_ref[c] == row_owner) & (kpos_ref[c] <= row_index)
        seen = jnp.concatenate([seen] * heads, axis=0)
        s = jnp.where(seen, s, -1e30)
        s_scr[c] = s
        return jnp.maximum(highest, jnp.max(s, axis=1, keepdims=True))

    highest = lax.fori_loop(
        0, total, scores_pass, jnp.full((heads * ROW_BLOCK, 1), -1e30, jnp.float32)
    )

    def exp_pass(t, summed):
        c = chunk_of(t)
        e = jnp.exp(s_scr[c] - highest)
        s_scr[c] = e
        return summed + jnp.sum(e, axis=1, keepdims=True)

    summed = lax.fori_loop(0, total, exp_pass, jnp.zeros((heads * ROW_BLOCK, 1), jnp.float32))
    inverse = 1.0 / summed
    acc_scr[...] = jnp.zeros(acc_scr.shape, jnp.float32)

    def value_pass(t, carry):
        c = chunk_of(t)
        w = (s_scr[c] * inverse).astype(jnp.bfloat16)
        values = load_chunk(c, False, fresh_v_ref)
        acc_scr[...] += jnp.dot(w, values, preferred_element_type=jnp.float32)
        return carry

    lax.fori_loop(0, total, value_pass, 0)
    for h in range(heads):
        o_ref[:, h * HD:(h + 1) * HD] = acc_scr[h * ROW_BLOCK:(h + 1) * ROW_BLOCK, :].astype(
            jnp.bfloat16
        )


def sparse_attention(
    queries, own_pages, partner_pages, slots, new_keys, new_values, half, kv_head,
    page_counts, last_fill, row_counts, page_total,
):
    row_total = queries.shape[0]
    page_len = own_pages.shape[1]
    ctx_total = page_total * page_len
    key_total = ctx_total + row_total
    heads = queries.shape[1] // HD
    blocks = row_total // ROW_BLOCK
    chunks = key_total // KEY_CHUNK
    ctx_chunks = ctx_total // KEY_CHUNK
    key_index = jnp.arange(ctx_total, dtype=jnp.int32)
    page_ref = key_index // page_len
    page_owner, page_starts = slot_lookup(page_ref, page_counts)
    context_len = (page_counts - 1) * page_len + last_fill
    position = (page_ref - table_pick(page_starts, page_owner)) * page_len + key_index % page_len
    valid = position < table_pick(context_len, page_owner)
    row_index = jnp.arange(row_total, dtype=jnp.int32)
    row_owner, row_starts = slot_lookup(row_index, row_counts)
    key_owner = jnp.concatenate([jnp.where(valid, page_owner, -1), row_owner])
    key_pos = jnp.concatenate([jnp.full((ctx_total,), -1, jnp.int32), row_index])
    first = row_owner[::ROW_BLOCK]
    last = row_owner[ROW_BLOCK - 1::ROW_BLOCK]
    ctx_from = pick(page_starts, first) * page_len
    ctx_to = (pick(page_starts, last) + pick(page_counts, last)) * page_len
    ctx_lo = ctx_from // KEY_CHUNK
    ctx_n = (ctx_to + KEY_CHUNK - 1) // KEY_CHUNK - ctx_lo
    new_from = pick(row_starts, first)
    new_to = jnp.arange(1, blocks + 1, dtype=jnp.int32) * ROW_BLOCK
    new_lo = new_from // KEY_CHUNK
    new_n = (new_to + KEY_CHUNK - 1) // KEY_CHUNK - new_lo
    ranges = jnp.stack(
        [ctx_lo, ctx_n, new_lo, new_n, jnp.full((blocks,), ctx_chunks, jnp.int32)], axis=1
    ).astype(jnp.int32)
    meta = jnp.stack([half, kv_head]).astype(jnp.int32)
    whole = lambda b, r, s, m: (0, 0, 0)
    return pl.pallas_call(
        attention_kernel,
        grid_spec=pltpu.PrefetchScalarGridSpec(
            num_scalar_prefetch=3,
            grid=(blocks,),
            in_specs=[
                pl.BlockSpec((ROW_BLOCK, heads * HD), lambda b, r, s, m: (b, 0)),
                pl.BlockSpec(own_pages.shape, whole),
                pl.BlockSpec(partner_pages.shape, whole),
                pl.BlockSpec((row_total, HD), lambda b, r, s, m: (0, m[1])),
                pl.BlockSpec((row_total, HD), lambda b, r, s, m: (0, m[1])),
                pl.BlockSpec((chunks, 1, KEY_CHUNK), whole),
                pl.BlockSpec((chunks, 1, KEY_CHUNK), whole),
                pl.BlockSpec((ROW_BLOCK, 1), lambda b, r, s, m: (b, 0)),
            ],
            out_specs=pl.BlockSpec((ROW_BLOCK, heads * HD), lambda b, r, s, m: (b, 0)),
            scratch_shapes=[
                pltpu.VMEM((chunks, heads * ROW_BLOCK, KEY_CHUNK), jnp.float32),
                pltpu.VMEM((heads * ROW_BLOCK, HD), jnp.float32),
            ],
        ),
        out_shape=jax.ShapeDtypeStruct((row_total, heads * HD), jnp.bfloat16),
    )(
        ranges,
        slots.astype(jnp.int32),
        meta,
        queries,
        own_pages,
        partner_pages,
        new_keys,
        new_values,
        key_owner.reshape(chunks, 1, KEY_CHUNK),
        key_pos.reshape(chunks, 1, KEY_CHUNK),
        row_owner.reshape(row_total, 1),
    )


def from_each(parts, axis_name):
    count = lax.axis_size(axis_name)
    me = lax.axis_index(axis_name)
    received = [lax.dynamic_index_in_dim(parts, me, 0, keepdims=False)]
    for shift in range(1, count):
        outgoing = lax.dynamic_index_in_dim(parts, (me + shift) % count, 0, keepdims=False)
        perm = [(i, (i + shift) % count) for i in range(count)]
        received.append(lax.ppermute(outgoing, axis_name, perm))
    order = (me - jnp.arange(count, dtype=jnp.int32)) % count
    return jnp.stack(received)[order]


def gather_over(x, axis_name, axis):
    count = lax.axis_size(axis_name)
    blocks = from_each(jnp.broadcast_to(x[None], (count,) + x.shape), axis_name)
    return jnp.concatenate([blocks[j] for j in range(count)], axis=axis)


def rows_to_columns(x, axis_name):
    count = lax.axis_size(axis_name)
    me = lax.axis_index(axis_name)
    parts = x.reshape(count, x.shape[0] // count, x.shape[1])
    received = [parts[me]]
    for shift in range(1, count):
        outgoing = lax.dynamic_index_in_dim(parts, (me + shift) % count, 0, keepdims=False)
        perm = [(i, (i + shift) % count) for i in range(count)]
        received.append(lax.ppermute(outgoing, axis_name, perm))
    order = (me - jnp.arange(count, dtype=jnp.int32)) % count
    blocks = jnp.stack(received)[order]
    return jnp.transpose(blocks, (1, 0, 2)).reshape(parts.shape[1], count * x.shape[1])


def columns_to_rows(x, axis_name):
    count = lax.axis_size(axis_name)
    me = lax.axis_index(axis_name)
    width = x.shape[1] // count
    received = [lax.dynamic_slice_in_dim(x, me * width, width, 1)]
    for shift in range(1, count):
        outgoing = lax.dynamic_slice_in_dim(x, ((me + shift) % count) * width, width, 1)
        perm = [(i, (i + shift) % count) for i in range(count)]
        received.append(lax.ppermute(outgoing, axis_name, perm))
    order = (me - jnp.arange(count, dtype=jnp.int32)) % count
    return jnp.stack(received)[order].reshape(count * x.shape[0], width)


def shards(
    hidden,
    queries,
    new_keys,
    new_values,
    cache_keys,
    cache_values,
    out_weight,
    attn_gain,
    ple_input,
    ple_gate_weight,
    ple_proj_weight,
    ple_gain,
    page_holder,
    page_slot,
    page_counts,
    last_fill,
    row_counts,
):
    row_total = hidden.shape[0]
    page_total = cache_keys.shape[0]
    page_len = cache_keys.shape[1]
    req_count = lax.axis_size("req")
    tp_index = lax.axis_index("tp")
    local_heads = queries.shape[1] // HD
    kv_head = tp_index // 2
    capacity = max(2, page_total // req_count)
    holders = page_holder[:, 0]
    places = page_slot[:, 0]
    ref_index = jnp.arange(page_total, dtype=jnp.int32)
    earlier = (holders[:, None] == holders[None, :]) & (ref_index[:, None] > ref_index[None, :])
    ranking = jnp.sum(earlier.astype(jnp.int32), axis=1)
    matched = (holders[:, None, None] == jnp.arange(req_count, dtype=jnp.int32)[None, :, None]) & (
        ranking[:, None, None] == jnp.arange(capacity, dtype=jnp.int32)[None, None, :]
    )
    request_table = jnp.sum(jnp.where(matched, places[:, None, None] + 1, 0), axis=0) - 1
    if req_count <= 8:
        asked = from_each(request_table, "req")
    else:
        asked = lax.all_to_all(request_table, "req", split_axis=0, concat_axis=0, tiled=True)
    wanted = jnp.maximum(asked, 0)
    tp_count = lax.axis_size("tp")
    half = tp_index % 2
    partner = [(i, i ^ 1) for i in range(tp_count)]
    arrival_index = holders * capacity + ranking

    own_cache = jnp.where(half == 0, cache_keys, cache_values)
    outgoing = lax.dynamic_slice_in_dim(own_cache, kv_head * HD, HD, 2)[wanted]
    arrived = lax.all_to_all(outgoing, "req", split_axis=0, concat_axis=0, tiled=True)
    swapped = lax.ppermute(arrived, "tp", partner)
    attention = sparse_attention(
        queries,
        arrived.reshape(-1, page_len, HD),
        swapped.reshape(-1, page_len, HD),
        arrival_index,
        new_keys,
        new_values,
        half,
        kv_head,
        page_counts[0], last_fill[0], row_counts[0], page_total,
    )
    tp_size = lax.axis_size("tp")
    full_weight = lax.all_gather(out_weight, "tp", axis=0, tiled=True)
    full_gate_weight = gather_over(ple_gate_weight, "tp", 0)
    full_proj_weight = gather_over(ple_proj_weight, "tp", 1)
    hidden_parts = hidden.reshape(tp_size, -1, hidden.shape[1])
    gain_rows = jnp.zeros((8, hidden.shape[1]), hidden.dtype).at[0].set(attn_gain).at[1].set(ple_gain)
    with_gains = jnp.concatenate(
        [hidden_parts, jnp.broadcast_to(gain_rows[None], (tp_size, 8, hidden.shape[1]))], axis=1
    )
    row_hidden_gains = rows_to_columns(with_gains.reshape(-1, hidden.shape[1]), "tp")
    row_hidden = row_hidden_gains[: hidden_parts.shape[1]]
    full_attn_gain = row_hidden_gains[hidden_parts.shape[1]]
    full_ple_gain = row_hidden_gains[hidden_parts.shape[1] + 1]
    row_attention = rows_to_columns(attention, "tp")
    part_rows = row_attention.shape[0]
    row_ple = lax.dynamic_slice_in_dim(ple_input, tp_index * part_rows, part_rows, 0)
    projected = jnp.dot(row_attention, full_weight, preferred_element_type=jnp.float32)
    squares = jnp.sum(projected * projected, axis=1)
    normed = (
        projected
        * lax.rsqrt(squares / D + 1e-06)[:, None]
        * full_attn_gain.astype(jnp.float32)[None, :]
    )
    mixed_state = (row_hidden.astype(jnp.float32) + normed).astype(jnp.bfloat16)
    gate = jnp.dot(mixed_state, full_gate_weight, preferred_element_type=jnp.float32)
    activated = (jax.nn.gelu(gate, approximate=True) * row_ple.astype(jnp.float32)).astype(
        jnp.bfloat16
    )
    lifted = jnp.dot(activated, full_proj_weight, preferred_element_type=jnp.float32)
    lift_squares = jnp.sum(lifted * lifted, axis=1)
    lift_normed = (
        lifted
        * lax.rsqrt(lift_squares / D + 1e-06)[:, None]
        * full_ple_gain.astype(jnp.float32)[None, :]
    )
    row_out = (mixed_state.astype(jnp.float32) + lift_normed).astype(jnp.bfloat16)
    return columns_to_rows(row_out, "tp")


def solution(mesh):
    return jax.shard_map(
        shards,
        mesh=mesh,
        in_specs=(
            P("req", "tp"),
            P("req", "tp"),
            P("req", None),
            P("req", None),
            P("req", None, None),
            P("req", None, None),
            P("tp", None),
            P("tp"),
            P("req", None),
            P("tp", None),
            P(None, "tp"),
            P("tp"),
            P("req", None),
            P("req", None),
            P("req", None),
            P("req", None),
            P("req", None),
        ),
        out_specs=P("req", "tp"),
        check_vma=False,
    )
```

```python
import math

import jax
import jax.numpy as jnp
from jax import lax
from jax.experimental import pallas as pl
from jax.experimental.pallas import tpu as pltpu
from jax.sharding import PartitionSpec as P

D = 2048
HD = 256


def slot_lookup(positions, counts):
    starts = jnp.cumsum(counts) - counts
    owning = jnp.sum((positions[:, None] >= starts[None, :]).astype(jnp.int32), axis=1) - 1
    return (owning, starts)


def table_pick(table, owning):
    onehot = owning[:, None] == jnp.arange(table.shape[0], dtype=jnp.int32)[None, :]
    return jnp.sum(jnp.where(onehot, table[None, :], 0), axis=1)


def attend_masks(counts_of_pages, fill_row, counts_of_rows, page_len, page_total, row_total):
    key_index = jnp.arange(page_total * page_len, dtype=jnp.int32)
    page_ref = key_index // page_len
    within = key_index % page_len
    page_owner, page_starts = slot_lookup(page_ref, counts_of_pages)
    context_len = (counts_of_pages - 1) * page_len + fill_row
    position = (page_ref - table_pick(page_starts, page_owner)) * page_len + within
    valid = position < table_pick(context_len, page_owner)
    row_index = jnp.arange(row_total, dtype=jnp.int32)
    row_owner = slot_lookup(row_index, counts_of_rows)[0]
    context_mask = (row_owner[:, None] == page_owner[None, :]) & valid[None, :]
    causal = (row_owner[:, None] == row_owner[None, :]) & (row_index[None, :] <= row_index[:, None])
    return jnp.concatenate([context_mask, causal], axis=1)


ROW_BLOCK = 128
KEY_CHUNK = 256


def pick(table, index):
    onehot = index[:, None] == jnp.arange(table.shape[0], dtype=jnp.int32)[None, :]
    return jnp.sum(jnp.where(onehot, table[None, :], 0), axis=1)


def attention_kernel(
    ranges_ref,
    slots_ref,
    meta_ref,
    q_ref,
    own_ref,
    partner_ref,
    fresh_k_ref,
    fresh_v_ref,
    kown_ref,
    kpos_ref,
    rown_ref,
    o_ref,
    s_scr,
    acc_scr,
):
    block = pl.program_id(0)
    ctx_lo = ranges_ref[block, 0]
    ctx_n = ranges_ref[block, 1]
    new_lo = ranges_ref[block, 2]
    total = ctx_n + ranges_ref[block, 3]
    ctx_chunks = ranges_ref[block, 4]
    keys_are_own = meta_ref[0] == 0
    heads = q_ref.shape[1] // HD
    page_len = own_ref.shape[1]
    per_chunk = KEY_CHUNK // page_len
    q = q_ref[...]
    stacked = jnp.concatenate([q[:, h * HD:(h + 1) * HD] for h in range(heads)], axis=0)
    row_owner = rown_ref[...]
    row_index = block * ROW_BLOCK + lax.broadcasted_iota(jnp.int32, (ROW_BLOCK, 1), 0)
    scale = 1.0 / math.sqrt(HD)

    def chunk_of(t):
        return jnp.where(t < ctx_n, ctx_lo + t, ctx_chunks + new_lo + t - ctx_n)

    def load_chunk(c, want_keys, fresh_ref):
        pick_own = keys_are_own == want_keys

        def cached():
            pages = []
            for i in range(per_chunk):
                slot = slots_ref[c * per_chunk + i]
                pages.append(jnp.where(pick_own, own_ref[slot], partner_ref[slot]))
            return jnp.concatenate(pages, axis=0)

        def fresh():
            start = pl.multiple_of((c - ctx_chunks) * KEY_CHUNK, KEY_CHUNK)
            return fresh_ref[pl.ds(start, KEY_CHUNK), :]

        return lax.cond(c < ctx_chunks, cached, fresh)

    def scores_pass(t, highest):
        c = chunk_of(t)
        keys = load_chunk(c, True, fresh_k_ref)
        s = lax.dot_general(
            stacked, keys, (((1,), (1,)), ((), ())), preferred_element_type=jnp.float32
        ) * scale
        seen = (kown_ref[c] == row_owner) & (kpos_ref[c] <= row_index)
        seen = jnp.concatenate([seen] * heads, axis=0)
        s = jnp.where(seen, s, -1e30)
        s_scr[c] = s
        return jnp.maximum(highest, jnp.max(s, axis=1, keepdims=True))

    highest = lax.fori_loop(
        0, total, scores_pass, jnp.full((heads * ROW_BLOCK, 1), -1e30, jnp.float32)
    )

    def exp_pass(t, summed):
        c = chunk_of(t)
        e = jnp.exp(s_scr[c] - highest)
        s_scr[c] = e
        return summed + jnp.sum(e, axis=1, keepdims=True)

    summed = lax.fori_loop(0, total, exp_pass, jnp.zeros((heads * ROW_BLOCK, 1), jnp.float32))
    inverse = 1.0 / summed
    acc_scr[...] = jnp.zeros(acc_scr.shape, jnp.float32)

    def value_pass(t, carry):
        c = chunk_of(t)
        w = (s_scr[c] * inverse).astype(jnp.bfloat16)
        values = load_chunk(c, False, fresh_v_ref)
        acc_scr[...] += jnp.dot(w, values, preferred_element_type=jnp.float32)
        return carry

    lax.fori_loop(0, total, value_pass, 0)
    for h in range(heads):
        o_ref[:, h * HD:(h + 1) * HD] = acc_scr[h * ROW_BLOCK:(h + 1) * ROW_BLOCK, :].astype(
            jnp.bfloat16
        )


def sparse_attention(
    queries, own_pages, partner_pages, slots, new_keys, new_values, half, kv_head,
    page_counts, last_fill, row_counts, page_total,
):
    row_total = queries.shape[0]
    page_len = own_pages.shape[1]
    ctx_total = page_total * page_len
    key_total = ctx_total + row_total
    heads = queries.shape[1] // HD
    blocks = row_total // ROW_BLOCK
    chunks = key_total // KEY_CHUNK
    ctx_chunks = ctx_total // KEY_CHUNK
    key_index = jnp.arange(ctx_total, dtype=jnp.int32)
    page_ref = key_index // page_len
    page_owner, page_starts = slot_lookup(page_ref, page_counts)
    context_len = (page_counts - 1) * page_len + last_fill
    position = (page_ref - table_pick(page_starts, page_owner)) * page_len + key_index % page_len
    valid = position < table_pick(context_len, page_owner)
    row_index = jnp.arange(row_total, dtype=jnp.int32)
    row_owner, row_starts = slot_lookup(row_index, row_counts)
    key_owner = jnp.concatenate([jnp.where(valid, page_owner, -1), row_owner])
    key_pos = jnp.concatenate([jnp.full((ctx_total,), -1, jnp.int32), row_index])
    first = row_owner[::ROW_BLOCK]
    last = row_owner[ROW_BLOCK - 1::ROW_BLOCK]
    ctx_from = pick(page_starts, first) * page_len
    ctx_to = (pick(page_starts, last) + pick(page_counts, last)) * page_len
    ctx_lo = ctx_from // KEY_CHUNK
    ctx_n = (ctx_to + KEY_CHUNK - 1) // KEY_CHUNK - ctx_lo
    new_from = pick(row_starts, first)
    new_to = jnp.arange(1, blocks + 1, dtype=jnp.int32) * ROW_BLOCK
    new_lo = new_from // KEY_CHUNK
    new_n = (new_to + KEY_CHUNK - 1) // KEY_CHUNK - new_lo
    ranges = jnp.stack(
        [ctx_lo, ctx_n, new_lo, new_n, jnp.full((blocks,), ctx_chunks, jnp.int32)], axis=1
    ).astype(jnp.int32)
    meta = jnp.stack([half, kv_head]).astype(jnp.int32)
    whole = lambda b, r, s, m: (0, 0, 0)
    return pl.pallas_call(
        attention_kernel,
        grid_spec=pltpu.PrefetchScalarGridSpec(
            num_scalar_prefetch=3,
            grid=(blocks,),
            in_specs=[
                pl.BlockSpec((ROW_BLOCK, heads * HD), lambda b, r, s, m: (b, 0)),
                pl.BlockSpec(own_pages.shape, whole),
                pl.BlockSpec(partner_pages.shape, whole),
                pl.BlockSpec((row_total, HD), lambda b, r, s, m: (0, m[1])),
                pl.BlockSpec((row_total, HD), lambda b, r, s, m: (0, m[1])),
                pl.BlockSpec((chunks, 1, KEY_CHUNK), whole),
                pl.BlockSpec((chunks, 1, KEY_CHUNK), whole),
                pl.BlockSpec((ROW_BLOCK, 1), lambda b, r, s, m: (b, 0)),
            ],
            out_specs=pl.BlockSpec((ROW_BLOCK, heads * HD), lambda b, r, s, m: (b, 0)),
            scratch_shapes=[
                pltpu.VMEM((chunks, heads * ROW_BLOCK, KEY_CHUNK), jnp.float32),
                pltpu.VMEM((heads * ROW_BLOCK, HD), jnp.float32),
            ],
        ),
        out_shape=jax.ShapeDtypeStruct((row_total, heads * HD), jnp.bfloat16),
    )(
        ranges,
        slots.astype(jnp.int32),
        meta,
        queries,
        own_pages,
        partner_pages,
        new_keys,
        new_values,
        key_owner.reshape(chunks, 1, KEY_CHUNK),
        key_pos.reshape(chunks, 1, KEY_CHUNK),
        row_owner.reshape(row_total, 1),
    )


def rows_to_columns(x, axis_name):
    count = lax.axis_size(axis_name)
    me = lax.axis_index(axis_name)
    parts = x.reshape(count, x.shape[0] // count, x.shape[1])
    received = [parts[me]]
    for shift in range(1, count):
        outgoing = lax.dynamic_index_in_dim(parts, (me + shift) % count, 0, keepdims=False)
        perm = [(i, (i + shift) % count) for i in range(count)]
        received.append(lax.ppermute(outgoing, axis_name, perm))
    order = (me - jnp.arange(count, dtype=jnp.int32)) % count
    blocks = jnp.stack(received)[order]
    return jnp.transpose(blocks, (1, 0, 2)).reshape(parts.shape[1], count * x.shape[1])


def columns_to_rows(x, axis_name):
    count = lax.axis_size(axis_name)
    me = lax.axis_index(axis_name)
    width = x.shape[1] // count
    received = [lax.dynamic_slice_in_dim(x, me * width, width, 1)]
    for shift in range(1, count):
        outgoing = lax.dynamic_slice_in_dim(x, ((me + shift) % count) * width, width, 1)
        perm = [(i, (i + shift) % count) for i in range(count)]
        received.append(lax.ppermute(outgoing, axis_name, perm))
    order = (me - jnp.arange(count, dtype=jnp.int32)) % count
    return jnp.stack(received)[order].reshape(count * x.shape[0], width)


def shards(
    hidden,
    queries,
    new_keys,
    new_values,
    cache_keys,
    cache_values,
    out_weight,
    attn_gain,
    ple_input,
    ple_gate_weight,
    ple_proj_weight,
    ple_gain,
    page_holder,
    page_slot,
    page_counts,
    last_fill,
    row_counts,
):
    row_total = hidden.shape[0]
    page_total = cache_keys.shape[0]
    page_len = cache_keys.shape[1]
    req_count = lax.axis_size("req")
    tp_index = lax.axis_index("tp")
    local_heads = queries.shape[1] // HD
    kv_head = tp_index // 2
    capacity = max(2, page_total // req_count)
    holders = page_holder[:, 0]
    places = page_slot[:, 0]
    ref_index = jnp.arange(page_total, dtype=jnp.int32)
    earlier = (holders[:, None] == holders[None, :]) & (ref_index[:, None] > ref_index[None, :])
    ranking = jnp.sum(earlier.astype(jnp.int32), axis=1)
    matched = (holders[:, None, None] == jnp.arange(req_count, dtype=jnp.int32)[None, :, None]) & (
        ranking[:, None, None] == jnp.arange(capacity, dtype=jnp.int32)[None, None, :]
    )
    request_table = jnp.sum(jnp.where(matched, places[:, None, None] + 1, 0), axis=0) - 1
    asked = lax.all_to_all(request_table, "req", split_axis=0, concat_axis=0, tiled=True)
    wanted = jnp.maximum(asked, 0)
    tp_count = lax.axis_size("tp")
    half = tp_index % 2
    partner = [(i, i ^ 1) for i in range(tp_count)]
    arrival_index = holders * capacity + ranking

    def fetch_pages(cache):
        return cache.reshape(page_total, page_len, -1, HD)[wanted, :, kv_head]

    outgoing = lax.cond(
        half == 0, lambda: fetch_pages(cache_keys), lambda: fetch_pages(cache_values)
    )
    arrived = lax.all_to_all(outgoing, "req", split_axis=0, concat_axis=0, tiled=True)
    swapped = lax.ppermute(arrived, "tp", partner)
    attention = sparse_attention(
        queries,
        arrived.reshape(-1, page_len, HD),
        swapped.reshape(-1, page_len, HD),
        arrival_index,
        new_keys,
        new_values,
        half,
        kv_head,
        page_counts[0], last_fill[0], row_counts[0], page_total,
    )
    tp_size = lax.axis_size("tp")
    joined = jnp.concatenate([out_weight, ple_gate_weight, ple_proj_weight.T], axis=1)
    full_joined = lax.all_gather(joined, "tp", axis=0, tiled=True)
    full_weight = full_joined[:, : out_weight.shape[1]]
    full_gate_weight = full_joined[:, out_weight.shape[1] : out_weight.shape[1] + ple_gate_weight.shape[1]]
    full_proj_weight_t = full_joined[:, out_weight.shape[1] + ple_gate_weight.shape[1] :]
    hidden_parts = hidden.reshape(tp_size, -1, hidden.shape[1])
    gain_rows = jnp.zeros((8, hidden.shape[1]), hidden.dtype).at[0].set(attn_gain).at[1].set(ple_gain)
    with_gains = jnp.concatenate(
        [hidden_parts, jnp.broadcast_to(gain_rows[None], (tp_size, 8, hidden.shape[1]))], axis=1
    )
    row_hidden_gains = rows_to_columns(with_gains.reshape(-1, hidden.shape[1]), "tp")
    row_hidden = row_hidden_gains[: hidden_parts.shape[1]]
    full_attn_gain = row_hidden_gains[hidden_parts.shape[1]]
    full_ple_gain = row_hidden_gains[hidden_parts.shape[1] + 1]
    row_attention = rows_to_columns(attention, "tp")
    part_rows = row_attention.shape[0]
    row_ple = lax.dynamic_slice_in_dim(ple_input, tp_index * part_rows, part_rows, 0)
    projected = jnp.dot(row_attention, full_weight, preferred_element_type=jnp.float32)
    squares = jnp.sum(projected * projected, axis=1)
    normed = (
        projected
        * lax.rsqrt(squares / D + 1e-06)[:, None]
        * full_attn_gain.astype(jnp.float32)[None, :]
    )
    mixed_state = (row_hidden.astype(jnp.float32) + normed).astype(jnp.bfloat16)
    gate = jnp.dot(mixed_state, full_gate_weight, preferred_element_type=jnp.float32)
    activated = (jax.nn.gelu(gate, approximate=True) * row_ple.astype(jnp.float32)).astype(
        jnp.bfloat16
    )
    lifted = lax.dot_general(
        activated, full_proj_weight_t, (((1,), (1,)), ((), ())), preferred_element_type=jnp.float32
    )
    lift_squares = jnp.sum(lifted * lifted, axis=1)
    lift_normed = (
        lifted
        * lax.rsqrt(lift_squares / D + 1e-06)[:, None]
        * full_ple_gain.astype(jnp.float32)[None, :]
    )
    row_out = (mixed_state.astype(jnp.float32) + lift_normed).astype(jnp.bfloat16)
    return columns_to_rows(row_out, "tp")


def solution(mesh):
    return jax.shard_map(
        shards,
        mesh=mesh,
        in_specs=(
            P("req", "tp"),
            P("req", "tp"),
            P("req", None),
            P("req", None),
            P("req", None, None),
            P("req", None, None),
            P("tp", None),
            P("tp"),
            P("req", None),
            P("tp", None),
            P(None, "tp"),
            P("tp"),
            P("req", None),
            P("req", None),
            P("req", None),
            P("req", None),
            P("req", None),
        ),
        out_specs=P("req", "tp"),
        check_vma=False,
    )
```

```python
import math

import jax
import jax.numpy as jnp
from jax import lax
from jax.experimental import pallas as pl
from jax.experimental.pallas import tpu as pltpu
from jax.sharding import PartitionSpec as P

D = 2048
HD = 256


def slot_lookup(positions, counts):
    starts = jnp.cumsum(counts) - counts
    owning = jnp.sum((positions[:, None] >= starts[None, :]).astype(jnp.int32), axis=1) - 1
    return (owning, starts)


def table_pick(table, owning):
    onehot = owning[:, None] == jnp.arange(table.shape[0], dtype=jnp.int32)[None, :]
    return jnp.sum(jnp.where(onehot, table[None, :], 0), axis=1)


def attend_masks(counts_of_pages, fill_row, counts_of_rows, page_len, page_total, row_total):
    key_index = jnp.arange(page_total * page_len, dtype=jnp.int32)
    page_ref = key_index // page_len
    within = key_index % page_len
    page_owner, page_starts = slot_lookup(page_ref, counts_of_pages)
    context_len = (counts_of_pages - 1) * page_len + fill_row
    position = (page_ref - table_pick(page_starts, page_owner)) * page_len + within
    valid = position < table_pick(context_len, page_owner)
    row_index = jnp.arange(row_total, dtype=jnp.int32)
    row_owner = slot_lookup(row_index, counts_of_rows)[0]
    context_mask = (row_owner[:, None] == page_owner[None, :]) & valid[None, :]
    causal = (row_owner[:, None] == row_owner[None, :]) & (row_index[None, :] <= row_index[:, None])
    return jnp.concatenate([context_mask, causal], axis=1)


ROW_BLOCK = 128
KEY_CHUNK = 256


def pick(table, index):
    onehot = index[:, None] == jnp.arange(table.shape[0], dtype=jnp.int32)[None, :]
    return jnp.sum(jnp.where(onehot, table[None, :], 0), axis=1)


def attention_kernel(
    ranges_ref,
    slots_ref,
    meta_ref,
    q_ref,
    own_ref,
    partner_ref,
    fresh_k_ref,
    fresh_v_ref,
    kown_ref,
    kpos_ref,
    rown_ref,
    o_ref,
    s_scr,
    acc_scr,
):
    block = pl.program_id(0)
    ctx_lo = ranges_ref[block, 0]
    ctx_n = ranges_ref[block, 1]
    new_lo = ranges_ref[block, 2]
    total = ctx_n + ranges_ref[block, 3]
    ctx_chunks = ranges_ref[block, 4]
    keys_are_own = meta_ref[0] == 0
    heads = q_ref.shape[1] // HD
    page_len = own_ref.shape[1]
    per_chunk = KEY_CHUNK // page_len
    q = q_ref[...]
    stacked = jnp.concatenate([q[:, h * HD:(h + 1) * HD] for h in range(heads)], axis=0)
    row_owner = rown_ref[...]
    row_index = block * ROW_BLOCK + lax.broadcasted_iota(jnp.int32, (ROW_BLOCK, 1), 0)
    scale = 1.0 / math.sqrt(HD)

    def chunk_of(t):
        return jnp.where(t < ctx_n, ctx_lo + t, ctx_chunks + new_lo + t - ctx_n)

    def load_chunk(c, want_keys, fresh_ref):
        pick_own = keys_are_own == want_keys

        def cached():
            pages = []
            for i in range(per_chunk):
                slot = slots_ref[c * per_chunk + i]
                pages.append(jnp.where(pick_own, own_ref[slot], partner_ref[slot]))
            return jnp.concatenate(pages, axis=0)

        def fresh():
            start = pl.multiple_of((c - ctx_chunks) * KEY_CHUNK, KEY_CHUNK)
            return fresh_ref[pl.ds(start, KEY_CHUNK), :]

        return lax.cond(c < ctx_chunks, cached, fresh)

    def scores_pass(t, highest):
        c = chunk_of(t)
        keys = load_chunk(c, True, fresh_k_ref)
        s = lax.dot_general(
            stacked, keys, (((1,), (1,)), ((), ())), preferred_element_type=jnp.float32
        ) * scale
        seen = (kown_ref[c] == row_owner) & (kpos_ref[c] <= row_index)
        seen = jnp.concatenate([seen] * heads, axis=0)
        s = jnp.where(seen, s, -1e30)
        s_scr[c] = s
        return jnp.maximum(highest, jnp.max(s, axis=1, keepdims=True))

    highest = lax.fori_loop(
        0, total, scores_pass, jnp.full((heads * ROW_BLOCK, 1), -1e30, jnp.float32)
    )

    def exp_pass(t, summed):
        c = chunk_of(t)
        e = jnp.exp(s_scr[c] - highest)
        s_scr[c] = e
        return summed + jnp.sum(e, axis=1, keepdims=True)

    summed = lax.fori_loop(0, total, exp_pass, jnp.zeros((heads * ROW_BLOCK, 1), jnp.float32))
    inverse = 1.0 / summed
    acc_scr[...] = jnp.zeros(acc_scr.shape, jnp.float32)

    def value_pass(t, carry):
        c = chunk_of(t)
        w = (s_scr[c] * inverse).astype(jnp.bfloat16)
        values = load_chunk(c, False, fresh_v_ref)
        acc_scr[...] += jnp.dot(w, values, preferred_element_type=jnp.float32)
        return carry

    lax.fori_loop(0, total, value_pass, 0)
    for h in range(heads):
        o_ref[:, h * HD:(h + 1) * HD] = acc_scr[h * ROW_BLOCK:(h + 1) * ROW_BLOCK, :].astype(
            jnp.bfloat16
        )


def attention_tables(
    slots, half, kv_head, page_counts, last_fill, row_counts, page_total, page_len, row_total
):
    ctx_total = page_total * page_len
    key_total = ctx_total + row_total
    blocks = row_total // ROW_BLOCK
    chunks = key_total // KEY_CHUNK
    ctx_chunks = ctx_total // KEY_CHUNK
    key_index = jnp.arange(ctx_total, dtype=jnp.int32)
    page_ref = key_index // page_len
    page_owner, page_starts = slot_lookup(page_ref, page_counts)
    context_len = (page_counts - 1) * page_len + last_fill
    position = (page_ref - table_pick(page_starts, page_owner)) * page_len + key_index % page_len
    valid = position < table_pick(context_len, page_owner)
    row_index = jnp.arange(row_total, dtype=jnp.int32)
    row_owner, row_starts = slot_lookup(row_index, row_counts)
    key_owner = jnp.concatenate([jnp.where(valid, page_owner, -1), row_owner])
    key_pos = jnp.concatenate([jnp.full((ctx_total,), -1, jnp.int32), row_index])
    first = row_owner[::ROW_BLOCK]
    last = row_owner[ROW_BLOCK - 1::ROW_BLOCK]
    ctx_from = pick(page_starts, first) * page_len
    ctx_to = (pick(page_starts, last) + pick(page_counts, last)) * page_len
    ctx_lo = ctx_from // KEY_CHUNK
    ctx_n = (ctx_to + KEY_CHUNK - 1) // KEY_CHUNK - ctx_lo
    new_from = pick(row_starts, first)
    new_to = jnp.arange(1, blocks + 1, dtype=jnp.int32) * ROW_BLOCK
    new_lo = new_from // KEY_CHUNK
    new_n = (new_to + KEY_CHUNK - 1) // KEY_CHUNK - new_lo
    ranges = jnp.stack(
        [ctx_lo, ctx_n, new_lo, new_n, jnp.full((blocks,), ctx_chunks, jnp.int32)], axis=1
    ).astype(jnp.int32)
    meta = jnp.stack([half, kv_head]).astype(jnp.int32)
    return (
        ranges,
        slots.astype(jnp.int32),
        meta,
        key_owner.reshape(chunks, 1, KEY_CHUNK),
        key_pos.reshape(chunks, 1, KEY_CHUNK),
        row_owner.reshape(row_total, 1),
    )


def sparse_attention(queries, own_pages, partner_pages, new_keys, new_values, tables):
    ranges, slots, meta, key_owner, key_pos, row_owner = tables
    row_total = queries.shape[0]
    heads = queries.shape[1] // HD
    blocks = row_total // ROW_BLOCK
    whole = lambda b, r, s, m: (0, 0, 0)
    return pl.pallas_call(
        attention_kernel,
        grid_spec=pltpu.PrefetchScalarGridSpec(
            num_scalar_prefetch=3,
            grid=(blocks,),
            in_specs=[
                pl.BlockSpec((ROW_BLOCK, heads * HD), lambda b, r, s, m: (b, 0)),
                pl.BlockSpec(own_pages.shape, whole),
                pl.BlockSpec(partner_pages.shape, whole),
                pl.BlockSpec((row_total, HD), lambda b, r, s, m: (0, m[1])),
                pl.BlockSpec((row_total, HD), lambda b, r, s, m: (0, m[1])),
                pl.BlockSpec(key_owner.shape, whole),
                pl.BlockSpec(key_pos.shape, whole),
                pl.BlockSpec((ROW_BLOCK, 1), lambda b, r, s, m: (b, 0)),
            ],
            out_specs=pl.BlockSpec((ROW_BLOCK, heads * HD), lambda b, r, s, m: (b, 0)),
            scratch_shapes=[
                pltpu.VMEM((key_owner.shape[0], heads * ROW_BLOCK, KEY_CHUNK), jnp.float32),
                pltpu.VMEM((heads * ROW_BLOCK, HD), jnp.float32),
            ],
        ),
        out_shape=jax.ShapeDtypeStruct((row_total, heads * HD), jnp.bfloat16),
    )(
        ranges,
        slots,
        meta,
        queries,
        own_pages,
        partner_pages,
        new_keys,
        new_values,
        key_owner,
        key_pos,
        row_owner,
    )


def rows_to_columns(x, axis_name):
    count = lax.axis_size(axis_name)
    me = lax.axis_index(axis_name)
    parts = x.reshape(count, x.shape[0] // count, x.shape[1])
    received = [parts[me]]
    for shift in range(1, count):
        outgoing = lax.dynamic_index_in_dim(parts, (me + shift) % count, 0, keepdims=False)
        perm = [(i, (i + shift) % count) for i in range(count)]
        received.append(lax.ppermute(outgoing, axis_name, perm))
    order = (me - jnp.arange(count, dtype=jnp.int32)) % count
    blocks = jnp.stack(received)[order]
    return jnp.transpose(blocks, (1, 0, 2)).reshape(parts.shape[1], count * x.shape[1])


def columns_to_rows(x, axis_name):
    count = lax.axis_size(axis_name)
    me = lax.axis_index(axis_name)
    width = x.shape[1] // count
    received = [lax.dynamic_slice_in_dim(x, me * width, width, 1)]
    for shift in range(1, count):
        outgoing = lax.dynamic_slice_in_dim(x, ((me + shift) % count) * width, width, 1)
        perm = [(i, (i + shift) % count) for i in range(count)]
        received.append(lax.ppermute(outgoing, axis_name, perm))
    order = (me - jnp.arange(count, dtype=jnp.int32)) % count
    return jnp.stack(received)[order].reshape(count * x.shape[0], width)


def shards(
    hidden,
    queries,
    new_keys,
    new_values,
    cache_keys,
    cache_values,
    out_weight,
    attn_gain,
    ple_input,
    ple_gate_weight,
    ple_proj_weight,
    ple_gain,
    page_holder,
    page_slot,
    page_counts,
    last_fill,
    row_counts,
):
    row_total = hidden.shape[0]
    page_total = cache_keys.shape[0]
    page_len = cache_keys.shape[1]
    req_count = lax.axis_size("req")
    tp_index = lax.axis_index("tp")
    local_heads = queries.shape[1] // HD
    kv_head = tp_index // 2
    capacity = max(2, page_total // req_count)
    holders = page_holder[:, 0]
    places = page_slot[:, 0]
    ref_index = jnp.arange(page_total, dtype=jnp.int32)
    earlier = (holders[:, None] == holders[None, :]) & (ref_index[:, None] > ref_index[None, :])
    ranking = jnp.sum(earlier.astype(jnp.int32), axis=1)
    matched = (holders[:, None, None] == jnp.arange(req_count, dtype=jnp.int32)[None, :, None]) & (
        ranking[:, None, None] == jnp.arange(capacity, dtype=jnp.int32)[None, None, :]
    )
    request_table = jnp.sum(jnp.where(matched, places[:, None, None] + 1, 0), axis=0) - 1
    asked = lax.all_to_all(request_table, "req", split_axis=0, concat_axis=0, tiled=True)
    tp_count = lax.axis_size("tp")
    half = tp_index % 2
    partner = [(i, i ^ 1) for i in range(tp_count)]
    arrival_index = holders * capacity + ranking
    tables = attention_tables(
        arrival_index, half, kv_head, page_counts[0], last_fill[0], row_counts[0],
        page_total, page_len, row_total,
    )
    asked, tables = lax.optimization_barrier((asked, tables))
    wanted = jnp.maximum(asked, 0)
    own_cache = jnp.where(half == 0, cache_keys, cache_values)
    outgoing = lax.dynamic_slice_in_dim(own_cache, kv_head * HD, HD, 2)[wanted]
    arrived = lax.all_to_all(outgoing, "req", split_axis=0, concat_axis=0, tiled=True)
    swapped = lax.ppermute(arrived, "tp", partner)
    attention = sparse_attention(
        queries,
        arrived.reshape(-1, page_len, HD),
        swapped.reshape(-1, page_len, HD),
        new_keys,
        new_values,
        tables,
    )
    tp_size = lax.axis_size("tp")
    joined = jnp.concatenate([out_weight, ple_gate_weight, ple_proj_weight.T], axis=1)
    full_joined = lax.all_gather(joined, "tp", axis=0, tiled=True)
    full_weight = full_joined[:, : out_weight.shape[1]]
    full_gate_weight = full_joined[:, out_weight.shape[1] : out_weight.shape[1] + ple_gate_weight.shape[1]]
    full_proj_weight_t = full_joined[:, out_weight.shape[1] + ple_gate_weight.shape[1] :]
    hidden_parts = hidden.reshape(tp_size, -1, hidden.shape[1])
    gain_rows = jnp.zeros((8, hidden.shape[1]), hidden.dtype).at[0].set(attn_gain).at[1].set(ple_gain)
    with_gains = jnp.concatenate(
        [hidden_parts, jnp.broadcast_to(gain_rows[None], (tp_size, 8, hidden.shape[1]))], axis=1
    )
    row_hidden_gains = rows_to_columns(with_gains.reshape(-1, hidden.shape[1]), "tp")
    row_hidden = row_hidden_gains[: hidden_parts.shape[1]]
    full_attn_gain = row_hidden_gains[hidden_parts.shape[1]]
    full_ple_gain = row_hidden_gains[hidden_parts.shape[1] + 1]
    row_attention = rows_to_columns(attention, "tp")
    part_rows = row_attention.shape[0]
    row_ple = lax.dynamic_slice_in_dim(ple_input, tp_index * part_rows, part_rows, 0)
    projected = jnp.dot(row_attention, full_weight, preferred_element_type=jnp.float32)
    squares = jnp.sum(projected * projected, axis=1)
    normed = (
        projected
        * lax.rsqrt(squares / D + 1e-06)[:, None]
        * full_attn_gain.astype(jnp.float32)[None, :]
    )
    mixed_state = (row_hidden.astype(jnp.float32) + normed).astype(jnp.bfloat16)
    gate = jnp.dot(mixed_state, full_gate_weight, preferred_element_type=jnp.float32)
    activated = (jax.nn.gelu(gate, approximate=True) * row_ple.astype(jnp.float32)).astype(
        jnp.bfloat16
    )
    lifted = lax.dot_general(
        activated, full_proj_weight_t, (((1,), (1,)), ((), ())), preferred_element_type=jnp.float32
    )
    lift_squares = jnp.sum(lifted * lifted, axis=1)
    lift_normed = (
        lifted
        * lax.rsqrt(lift_squares / D + 1e-06)[:, None]
        * full_ple_gain.astype(jnp.float32)[None, :]
    )
    row_out = (mixed_state.astype(jnp.float32) + lift_normed).astype(jnp.bfloat16)
    return columns_to_rows(row_out, "tp")


def solution(mesh):
    return jax.shard_map(
        shards,
        mesh=mesh,
        in_specs=(
            P("req", "tp"),
            P("req", "tp"),
            P("req", None),
            P("req", None),
            P("req", None, None),
            P("req", None, None),
            P("tp", None),
            P("tp"),
            P("req", None),
            P("tp", None),
            P(None, "tp"),
            P("tp"),
            P("req", None),
            P("req", None),
            P("req", None),
            P("req", None),
            P("req", None),
        ),
        out_specs=P("req", "tp"),
        check_vma=False,
    )
```

```python
import math

import jax
import jax.numpy as jnp
from jax import lax
from jax.experimental import pallas as pl
from jax.experimental.pallas import tpu as pltpu
from jax.sharding import PartitionSpec as P

D = 2048
HD = 256


def slot_lookup(positions, counts):
    starts = jnp.cumsum(counts) - counts
    owning = jnp.sum((positions[:, None] >= starts[None, :]).astype(jnp.int32), axis=1) - 1
    return (owning, starts)


def table_pick(table, owning):
    onehot = owning[:, None] == jnp.arange(table.shape[0], dtype=jnp.int32)[None, :]
    return jnp.sum(jnp.where(onehot, table[None, :], 0), axis=1)


def attend_masks(counts_of_pages, fill_row, counts_of_rows, page_len, page_total, row_total):
    key_index = jnp.arange(page_total * page_len, dtype=jnp.int32)
    page_ref = key_index // page_len
    within = key_index % page_len
    page_owner, page_starts = slot_lookup(page_ref, counts_of_pages)
    context_len = (counts_of_pages - 1) * page_len + fill_row
    position = (page_ref - table_pick(page_starts, page_owner)) * page_len + within
    valid = position < table_pick(context_len, page_owner)
    row_index = jnp.arange(row_total, dtype=jnp.int32)
    row_owner = slot_lookup(row_index, counts_of_rows)[0]
    context_mask = (row_owner[:, None] == page_owner[None, :]) & valid[None, :]
    causal = (row_owner[:, None] == row_owner[None, :]) & (row_index[None, :] <= row_index[:, None])
    return jnp.concatenate([context_mask, causal], axis=1)


ROW_BLOCK = 128
KEY_CHUNK = 256


def pick(table, index):
    onehot = index[:, None] == jnp.arange(table.shape[0], dtype=jnp.int32)[None, :]
    return jnp.sum(jnp.where(onehot, table[None, :], 0), axis=1)


def attention_kernel(
    ranges_ref,
    slots_ref,
    meta_ref,
    q_ref,
    own_ref,
    partner_ref,
    fresh_k_ref,
    fresh_v_ref,
    kown_ref,
    kpos_ref,
    rown_ref,
    o_ref,
    s_scr,
    acc_scr,
):
    block = pl.program_id(0)
    ctx_lo = ranges_ref[block, 0]
    ctx_n = ranges_ref[block, 1]
    new_lo = ranges_ref[block, 2]
    total = ctx_n + ranges_ref[block, 3]
    ctx_chunks = ranges_ref[block, 4]
    keys_are_own = meta_ref[0] == 0
    heads = q_ref.shape[1] // HD
    page_len = own_ref.shape[1]
    per_chunk = KEY_CHUNK // page_len
    q = q_ref[...]
    stacked = jnp.concatenate([q[:, h * HD:(h + 1) * HD] for h in range(heads)], axis=0)
    row_owner = rown_ref[...]
    row_index = block * ROW_BLOCK + lax.broadcasted_iota(jnp.int32, (ROW_BLOCK, 1), 0)
    scale = 1.0 / math.sqrt(HD)

    def chunk_of(t):
        return jnp.where(t < ctx_n, ctx_lo + t, ctx_chunks + new_lo + t - ctx_n)

    def load_chunk(c, want_keys, fresh_ref):
        pick_own = keys_are_own == want_keys

        def cached():
            pages = []
            for i in range(per_chunk):
                slot = slots_ref[c * per_chunk + i]
                pages.append(jnp.where(pick_own, own_ref[slot], partner_ref[slot]))
            return jnp.concatenate(pages, axis=0)

        def fresh():
            start = pl.multiple_of((c - ctx_chunks) * KEY_CHUNK, KEY_CHUNK)
            return fresh_ref[pl.ds(start, KEY_CHUNK), :]

        return lax.cond(c < ctx_chunks, cached, fresh)

    def scores_pass(t, highest):
        c = chunk_of(t)
        keys = load_chunk(c, True, fresh_k_ref)
        s = lax.dot_general(
            stacked, keys, (((1,), (1,)), ((), ())), preferred_element_type=jnp.float32
        ) * scale
        seen = (kown_ref[c] == row_owner) & (kpos_ref[c] <= row_index)
        seen = jnp.concatenate([seen] * heads, axis=0)
        s = jnp.where(seen, s, -1e30)
        s_scr[c] = s
        return jnp.maximum(highest, jnp.max(s, axis=1, keepdims=True))

    highest = lax.fori_loop(
        0, total, scores_pass, jnp.full((heads * ROW_BLOCK, 1), -1e30, jnp.float32)
    )

    def exp_pass(t, summed):
        c = chunk_of(t)
        e = jnp.exp(s_scr[c] - highest)
        s_scr[c] = e
        return summed + jnp.sum(e, axis=1, keepdims=True)

    summed = lax.fori_loop(0, total, exp_pass, jnp.zeros((heads * ROW_BLOCK, 1), jnp.float32))
    inverse = 1.0 / summed
    acc_scr[...] = jnp.zeros(acc_scr.shape, jnp.float32)

    def value_pass(t, carry):
        c = chunk_of(t)
        w = (s_scr[c] * inverse).astype(jnp.bfloat16)
        values = load_chunk(c, False, fresh_v_ref)
        acc_scr[...] += jnp.dot(w, values, preferred_element_type=jnp.float32)
        return carry

    lax.fori_loop(0, total, value_pass, 0)
    for h in range(heads):
        o_ref[:, h * HD:(h + 1) * HD] = acc_scr[h * ROW_BLOCK:(h + 1) * ROW_BLOCK, :].astype(
            jnp.bfloat16
        )


def sparse_attention(
    queries, own_pages, partner_pages, slots, new_keys, new_values, half, kv_head,
    page_counts, last_fill, row_counts, page_total,
):
    row_total = queries.shape[0]
    page_len = own_pages.shape[1]
    ctx_total = page_total * page_len
    key_total = ctx_total + row_total
    heads = queries.shape[1] // HD
    blocks = row_total // ROW_BLOCK
    chunks = key_total // KEY_CHUNK
    ctx_chunks = ctx_total // KEY_CHUNK
    key_index = jnp.arange(ctx_total, dtype=jnp.int32)
    page_ref = key_index // page_len
    page_owner, page_starts = slot_lookup(page_ref, page_counts)
    context_len = (page_counts - 1) * page_len + last_fill
    position = (page_ref - table_pick(page_starts, page_owner)) * page_len + key_index % page_len
    valid = position < table_pick(context_len, page_owner)
    row_index = jnp.arange(row_total, dtype=jnp.int32)
    row_owner, row_starts = slot_lookup(row_index, row_counts)
    key_owner = jnp.concatenate([jnp.where(valid, page_owner, -1), row_owner])
    key_pos = jnp.concatenate([jnp.full((ctx_total,), -1, jnp.int32), row_index])
    first = row_owner[::ROW_BLOCK]
    last = row_owner[ROW_BLOCK - 1::ROW_BLOCK]
    ctx_from = pick(page_starts, first) * page_len
    ctx_to = (pick(page_starts, last) + pick(page_counts, last)) * page_len
    ctx_lo = ctx_from // KEY_CHUNK
    ctx_n = (ctx_to + KEY_CHUNK - 1) // KEY_CHUNK - ctx_lo
    new_from = pick(row_starts, first)
    new_to = jnp.arange(1, blocks + 1, dtype=jnp.int32) * ROW_BLOCK
    new_lo = new_from // KEY_CHUNK
    new_n = (new_to + KEY_CHUNK - 1) // KEY_CHUNK - new_lo
    ranges = jnp.stack(
        [ctx_lo, ctx_n, new_lo, new_n, jnp.full((blocks,), ctx_chunks, jnp.int32)], axis=1
    ).astype(jnp.int32)
    meta = jnp.stack([half, kv_head]).astype(jnp.int32)
    whole = lambda b, r, s, m: (0, 0, 0)
    return pl.pallas_call(
        attention_kernel,
        grid_spec=pltpu.PrefetchScalarGridSpec(
            num_scalar_prefetch=3,
            grid=(blocks,),
            in_specs=[
                pl.BlockSpec((ROW_BLOCK, heads * HD), lambda b, r, s, m: (b, 0)),
                pl.BlockSpec(own_pages.shape, whole),
                pl.BlockSpec(partner_pages.shape, whole),
                pl.BlockSpec((row_total, HD), lambda b, r, s, m: (0, m[1])),
                pl.BlockSpec((row_total, HD), lambda b, r, s, m: (0, m[1])),
                pl.BlockSpec((chunks, 1, KEY_CHUNK), whole),
                pl.BlockSpec((chunks, 1, KEY_CHUNK), whole),
                pl.BlockSpec((ROW_BLOCK, 1), lambda b, r, s, m: (b, 0)),
            ],
            out_specs=pl.BlockSpec((ROW_BLOCK, heads * HD), lambda b, r, s, m: (b, 0)),
            scratch_shapes=[
                pltpu.VMEM((chunks, heads * ROW_BLOCK, KEY_CHUNK), jnp.float32),
                pltpu.VMEM((heads * ROW_BLOCK, HD), jnp.float32),
            ],
        ),
        out_shape=jax.ShapeDtypeStruct((row_total, heads * HD), jnp.bfloat16),
    )(
        ranges,
        slots.astype(jnp.int32),
        meta,
        queries,
        own_pages,
        partner_pages,
        new_keys,
        new_values,
        key_owner.reshape(chunks, 1, KEY_CHUNK),
        key_pos.reshape(chunks, 1, KEY_CHUNK),
        row_owner.reshape(row_total, 1),
    )


def rows_to_columns(x, axis_name):
    count = lax.axis_size(axis_name)
    me = lax.axis_index(axis_name)
    parts = x.reshape(count, x.shape[0] // count, x.shape[1])
    received = [parts[me]]
    for shift in range(1, count):
        outgoing = lax.dynamic_index_in_dim(parts, (me + shift) % count, 0, keepdims=False)
        perm = [(i, (i + shift) % count) for i in range(count)]
        received.append(lax.ppermute(outgoing, axis_name, perm))
    order = (me - jnp.arange(count, dtype=jnp.int32)) % count
    blocks = jnp.stack(received)[order]
    return jnp.transpose(blocks, (1, 0, 2)).reshape(parts.shape[1], count * x.shape[1])


def columns_to_rows(x, axis_name):
    count = lax.axis_size(axis_name)
    me = lax.axis_index(axis_name)
    width = x.shape[1] // count
    received = [lax.dynamic_slice_in_dim(x, me * width, width, 1)]
    for shift in range(1, count):
        outgoing = lax.dynamic_slice_in_dim(x, ((me + shift) % count) * width, width, 1)
        perm = [(i, (i + shift) % count) for i in range(count)]
        received.append(lax.ppermute(outgoing, axis_name, perm))
    order = (me - jnp.arange(count, dtype=jnp.int32)) % count
    return jnp.stack(received)[order].reshape(count * x.shape[0], width)


def shards(
    hidden,
    queries,
    new_keys,
    new_values,
    cache_keys,
    cache_values,
    out_weight,
    attn_gain,
    ple_input,
    ple_gate_weight,
    ple_proj_weight,
    ple_gain,
    page_holder,
    page_slot,
    page_counts,
    last_fill,
    row_counts,
):
    row_total = hidden.shape[0]
    page_total = cache_keys.shape[0]
    page_len = cache_keys.shape[1]
    req_count = lax.axis_size("req")
    tp_index = lax.axis_index("tp")
    local_heads = queries.shape[1] // HD
    kv_head = tp_index // 2
    capacity = max(2, page_total // req_count)
    holders = page_holder[:, 0]
    places = page_slot[:, 0]
    ref_index = jnp.arange(page_total, dtype=jnp.int32)
    earlier = (holders[:, None] == holders[None, :]) & (ref_index[:, None] > ref_index[None, :])
    ranking = jnp.sum(earlier.astype(jnp.int32), axis=1)
    matched = (holders[:, None, None] == jnp.arange(req_count, dtype=jnp.int32)[None, :, None]) & (
        ranking[:, None, None] == jnp.arange(capacity, dtype=jnp.int32)[None, None, :]
    )
    request_table = jnp.sum(jnp.where(matched, places[:, None, None] + 1, 0), axis=0) - 1
    asked = lax.all_to_all(request_table, "req", split_axis=0, concat_axis=0, tiled=True)
    wanted = jnp.maximum(asked, 0)
    tp_count = lax.axis_size("tp")
    half = tp_index % 2
    partner = [(i, i ^ 1) for i in range(tp_count)]
    arrival_index = holders * capacity + ranking

    own_cache = jnp.where(half == 0, cache_keys, cache_values)
    outgoing = lax.dynamic_slice_in_dim(own_cache, kv_head * HD, HD, 2)[wanted]
    arrived = lax.all_to_all(outgoing, "req", split_axis=0, concat_axis=0, tiled=True)
    swapped = lax.ppermute(arrived, "tp", partner)
    attention = sparse_attention(
        queries,
        arrived.reshape(-1, page_len, HD),
        swapped.reshape(-1, page_len, HD),
        arrival_index,
        new_keys,
        new_values,
        half,
        kv_head,
        page_counts[0], last_fill[0], row_counts[0], page_total,
    )
    tp_size = lax.axis_size("tp")
    full_weight = lax.all_gather(out_weight, "tp", axis=0, tiled=True)
    full_gate_weight = lax.all_gather(ple_gate_weight, "tp", axis=0, tiled=True)
    full_proj_weight = lax.all_gather(ple_proj_weight, "tp", axis=1, tiled=True)
    hidden_parts = hidden.reshape(tp_size, -1, hidden.shape[1])
    gain_rows = jnp.zeros((8, hidden.shape[1]), hidden.dtype).at[0].set(attn_gain).at[1].set(ple_gain)
    with_gains = jnp.concatenate(
        [hidden_parts, jnp.broadcast_to(gain_rows[None], (tp_size, 8, hidden.shape[1]))], axis=1
    )
    row_hidden_gains = rows_to_columns(with_gains.reshape(-1, hidden.shape[1]), "tp")
    row_hidden = row_hidden_gains[: hidden_parts.shape[1]]
    full_attn_gain = row_hidden_gains[hidden_parts.shape[1]]
    full_ple_gain = row_hidden_gains[hidden_parts.shape[1] + 1]
    row_attention = rows_to_columns(attention, "tp")
    part_rows = row_attention.shape[0]
    row_ple = lax.dynamic_slice_in_dim(ple_input, tp_index * part_rows, part_rows, 0)
    projected = jnp.dot(row_attention, full_weight, preferred_element_type=jnp.float32)
    squares = jnp.sum(projected * projected, axis=1)
    normed = (
        projected
        * lax.rsqrt(squares / D + 1e-06)[:, None]
        * full_attn_gain.astype(jnp.float32)[None, :]
    )
    mixed_state = (row_hidden.astype(jnp.float32) + normed).astype(jnp.bfloat16)
    gate = jnp.dot(mixed_state, full_gate_weight, preferred_element_type=jnp.float32)
    activated = (jax.nn.gelu(gate, approximate=True) * row_ple.astype(jnp.float32)).astype(
        jnp.bfloat16
    )
    lifted = jnp.dot(activated, full_proj_weight, preferred_element_type=jnp.float32)
    lift_squares = jnp.sum(lifted * lifted, axis=1)
    lift_normed = (
        lifted
        * lax.rsqrt(lift_squares / D + 1e-06)[:, None]
        * full_ple_gain.astype(jnp.float32)[None, :]
    )
    row_out = (mixed_state.astype(jnp.float32) + lift_normed).astype(jnp.bfloat16)
    return columns_to_rows(row_out, "tp")


def solution(mesh):
    return jax.shard_map(
        shards,
        mesh=mesh,
        in_specs=(
            P("req", "tp"),
            P("req", "tp"),
            P("req", None),
            P("req", None),
            P("req", None, None),
            P("req", None, None),
            P("tp", None),
            P("tp"),
            P("req", None),
            P("tp", None),
            P(None, "tp"),
            P("tp"),
            P("req", None),
            P("req", None),
            P("req", None),
            P("req", None),
            P("req", None),
        ),
        out_specs=P("req", "tp"),
        check_vma=False,
    )
```

```python
import math

import jax
import jax.numpy as jnp
from jax import lax
from jax.experimental import pallas as pl
from jax.experimental.pallas import tpu as pltpu
from jax.sharding import PartitionSpec as P

D = 2048
HD = 256


def slot_lookup(positions, counts):
    starts = jnp.cumsum(counts) - counts
    owning = jnp.sum((positions[:, None] >= starts[None, :]).astype(jnp.int32), axis=1) - 1
    return (owning, starts)


def table_pick(table, owning):
    onehot = owning[:, None] == jnp.arange(table.shape[0], dtype=jnp.int32)[None, :]
    return jnp.sum(jnp.where(onehot, table[None, :], 0), axis=1)


def attend_masks(counts_of_pages, fill_row, counts_of_rows, page_len, page_total, row_total):
    key_index = jnp.arange(page_total * page_len, dtype=jnp.int32)
    page_ref = key_index // page_len
    within = key_index % page_len
    page_owner, page_starts = slot_lookup(page_ref, counts_of_pages)
    context_len = (counts_of_pages - 1) * page_len + fill_row
    position = (page_ref - table_pick(page_starts, page_owner)) * page_len + within
    valid = position < table_pick(context_len, page_owner)
    row_index = jnp.arange(row_total, dtype=jnp.int32)
    row_owner = slot_lookup(row_index, counts_of_rows)[0]
    context_mask = (row_owner[:, None] == page_owner[None, :]) & valid[None, :]
    causal = (row_owner[:, None] == row_owner[None, :]) & (row_index[None, :] <= row_index[:, None])
    return jnp.concatenate([context_mask, causal], axis=1)


ROW_BLOCK = 128
KEY_CHUNK = 256


def pick(table, index):
    onehot = index[:, None] == jnp.arange(table.shape[0], dtype=jnp.int32)[None, :]
    return jnp.sum(jnp.where(onehot, table[None, :], 0), axis=1)


def attention_kernel(
    ranges_ref,
    slots_ref,
    meta_ref,
    q_ref,
    own_ref,
    partner_ref,
    fresh_k_ref,
    fresh_v_ref,
    kown_ref,
    kpos_ref,
    rown_ref,
    o_ref,
    s_scr,
    acc_scr,
):
    block = pl.program_id(0)
    ctx_lo = ranges_ref[block, 0]
    ctx_n = ranges_ref[block, 1]
    new_lo = ranges_ref[block, 2]
    total = ctx_n + ranges_ref[block, 3]
    ctx_chunks = ranges_ref[block, 4]
    keys_are_own = meta_ref[0] == 0
    heads = q_ref.shape[1] // HD
    page_len = own_ref.shape[1]
    per_chunk = KEY_CHUNK // page_len
    q = q_ref[...]
    stacked = jnp.concatenate([q[:, h * HD:(h + 1) * HD] for h in range(heads)], axis=0)
    row_owner = rown_ref[...]
    row_index = block * ROW_BLOCK + lax.broadcasted_iota(jnp.int32, (ROW_BLOCK, 1), 0)
    scale = 1.0 / math.sqrt(HD)

    def chunk_of(t):
        return jnp.where(t < ctx_n, ctx_lo + t, ctx_chunks + new_lo + t - ctx_n)

    def load_chunk(c, want_keys, fresh_ref):
        pick_own = keys_are_own == want_keys

        def cached():
            pages = []
            for i in range(per_chunk):
                slot = slots_ref[c * per_chunk + i]
                pages.append(jnp.where(pick_own, own_ref[slot], partner_ref[slot]))
            return jnp.concatenate(pages, axis=0)

        def fresh():
            start = pl.multiple_of((c - ctx_chunks) * KEY_CHUNK, KEY_CHUNK)
            return fresh_ref[pl.ds(start, KEY_CHUNK), :]

        return lax.cond(c < ctx_chunks, cached, fresh)

    def scores_pass(t, highest):
        c = chunk_of(t)
        keys = load_chunk(c, True, fresh_k_ref)
        s = lax.dot_general(
            stacked, keys, (((1,), (1,)), ((), ())), preferred_element_type=jnp.float32
        ) * scale
        seen = (kown_ref[c] == row_owner) & (kpos_ref[c] <= row_index)
        seen = jnp.concatenate([seen] * heads, axis=0)
        s = jnp.where(seen, s, -1e30)
        s_scr[c] = s
        return jnp.maximum(highest, jnp.max(s, axis=1, keepdims=True))

    highest = lax.fori_loop(
        0, total, scores_pass, jnp.full((heads * ROW_BLOCK, 1), -1e30, jnp.float32)
    )

    def exp_pass(t, summed):
        c = chunk_of(t)
        e = jnp.exp(s_scr[c] - highest)
        s_scr[c] = e
        return summed + jnp.sum(e, axis=1, keepdims=True)

    summed = lax.fori_loop(0, total, exp_pass, jnp.zeros((heads * ROW_BLOCK, 1), jnp.float32))
    inverse = 1.0 / summed
    acc_scr[...] = jnp.zeros(acc_scr.shape, jnp.float32)

    def value_pass(t, carry):
        c = chunk_of(t)
        w = (s_scr[c] * inverse).astype(jnp.bfloat16)
        values = load_chunk(c, False, fresh_v_ref)
        acc_scr[...] += jnp.dot(w, values, preferred_element_type=jnp.float32)
        return carry

    lax.fori_loop(0, total, value_pass, 0)
    for h in range(heads):
        o_ref[:, h * HD:(h + 1) * HD] = acc_scr[h * ROW_BLOCK:(h + 1) * ROW_BLOCK, :].astype(
            jnp.bfloat16
        )


def sparse_attention(
    queries, own_pages, partner_pages, slots, new_keys, new_values, half, kv_head,
    page_counts, last_fill, row_counts, page_total,
):
    row_total = queries.shape[0]
    page_len = own_pages.shape[1]
    ctx_total = page_total * page_len
    key_total = ctx_total + row_total
    heads = queries.shape[1] // HD
    blocks = row_total // ROW_BLOCK
    chunks = key_total // KEY_CHUNK
    ctx_chunks = ctx_total // KEY_CHUNK
    key_index = jnp.arange(ctx_total, dtype=jnp.int32)
    page_ref = key_index // page_len
    page_owner, page_starts = slot_lookup(page_ref, page_counts)
    context_len = (page_counts - 1) * page_len + last_fill
    position = (page_ref - table_pick(page_starts, page_owner)) * page_len + key_index % page_len
    valid = position < table_pick(context_len, page_owner)
    row_index = jnp.arange(row_total, dtype=jnp.int32)
    row_owner, row_starts = slot_lookup(row_index, row_counts)
    key_owner = jnp.concatenate([jnp.where(valid, page_owner, -1), row_owner])
    key_pos = jnp.concatenate([jnp.full((ctx_total,), -1, jnp.int32), row_index])
    first = row_owner[::ROW_BLOCK]
    last = row_owner[ROW_BLOCK - 1::ROW_BLOCK]
    ctx_from = pick(page_starts, first) * page_len
    ctx_to = (pick(page_starts, last) + pick(page_counts, last)) * page_len
    ctx_lo = ctx_from // KEY_CHUNK
    ctx_n = (ctx_to + KEY_CHUNK - 1) // KEY_CHUNK - ctx_lo
    new_from = pick(row_starts, first)
    new_to = jnp.arange(1, blocks + 1, dtype=jnp.int32) * ROW_BLOCK
    new_lo = new_from // KEY_CHUNK
    new_n = (new_to + KEY_CHUNK - 1) // KEY_CHUNK - new_lo
    ranges = jnp.stack(
        [ctx_lo, ctx_n, new_lo, new_n, jnp.full((blocks,), ctx_chunks, jnp.int32)], axis=1
    ).astype(jnp.int32)
    meta = jnp.stack([half, kv_head]).astype(jnp.int32)
    whole = lambda b, r, s, m: (0, 0, 0)
    return pl.pallas_call(
        attention_kernel,
        grid_spec=pltpu.PrefetchScalarGridSpec(
            num_scalar_prefetch=3,
            grid=(blocks,),
            in_specs=[
                pl.BlockSpec((ROW_BLOCK, heads * HD), lambda b, r, s, m: (b, 0)),
                pl.BlockSpec(own_pages.shape, whole),
                pl.BlockSpec(partner_pages.shape, whole),
                pl.BlockSpec((row_total, HD), lambda b, r, s, m: (0, m[1])),
                pl.BlockSpec((row_total, HD), lambda b, r, s, m: (0, m[1])),
                pl.BlockSpec((chunks, 1, KEY_CHUNK), whole),
                pl.BlockSpec((chunks, 1, KEY_CHUNK), whole),
                pl.BlockSpec((ROW_BLOCK, 1), lambda b, r, s, m: (b, 0)),
            ],
            out_specs=pl.BlockSpec((ROW_BLOCK, heads * HD), lambda b, r, s, m: (b, 0)),
            scratch_shapes=[
                pltpu.VMEM((chunks, heads * ROW_BLOCK, KEY_CHUNK), jnp.float32),
                pltpu.VMEM((heads * ROW_BLOCK, HD), jnp.float32),
            ],
        ),
        out_shape=jax.ShapeDtypeStruct((row_total, heads * HD), jnp.bfloat16),
    )(
        ranges,
        slots.astype(jnp.int32),
        meta,
        queries,
        own_pages,
        partner_pages,
        new_keys,
        new_values,
        key_owner.reshape(chunks, 1, KEY_CHUNK),
        key_pos.reshape(chunks, 1, KEY_CHUNK),
        row_owner.reshape(row_total, 1),
    )


def rows_to_columns(x, axis_name):
    count = lax.axis_size(axis_name)
    me = lax.axis_index(axis_name)
    parts = x.reshape(count, x.shape[0] // count, x.shape[1])
    received = [parts[me]]
    for shift in range(1, count):
        outgoing = lax.dynamic_index_in_dim(parts, (me + shift) % count, 0, keepdims=False)
        perm = [(i, (i + shift) % count) for i in range(count)]
        received.append(lax.ppermute(outgoing, axis_name, perm))
    order = (me - jnp.arange(count, dtype=jnp.int32)) % count
    blocks = jnp.stack(received)[order]
    return jnp.transpose(blocks, (1, 0, 2)).reshape(parts.shape[1], count * x.shape[1])


def columns_to_rows(x, axis_name):
    count = lax.axis_size(axis_name)
    me = lax.axis_index(axis_name)
    width = x.shape[1] // count
    received = [lax.dynamic_slice_in_dim(x, me * width, width, 1)]
    for shift in range(1, count):
        outgoing = lax.dynamic_slice_in_dim(x, ((me + shift) % count) * width, width, 1)
        perm = [(i, (i + shift) % count) for i in range(count)]
        received.append(lax.ppermute(outgoing, axis_name, perm))
    order = (me - jnp.arange(count, dtype=jnp.int32)) % count
    return jnp.stack(received)[order].reshape(count * x.shape[0], width)


def shards(
    hidden,
    queries,
    new_keys,
    new_values,
    cache_keys,
    cache_values,
    out_weight,
    attn_gain,
    ple_input,
    ple_gate_weight,
    ple_proj_weight,
    ple_gain,
    page_holder,
    page_slot,
    page_counts,
    last_fill,
    row_counts,
):
    row_total = hidden.shape[0]
    page_total = cache_keys.shape[0]
    page_len = cache_keys.shape[1]
    req_count = lax.axis_size("req")
    tp_index = lax.axis_index("tp")
    local_heads = queries.shape[1] // HD
    kv_head = tp_index // 2
    capacity = max(2, page_total // req_count)
    holders = page_holder[:, 0]
    places = page_slot[:, 0]
    ref_index = jnp.arange(page_total, dtype=jnp.int32)
    earlier = (holders[:, None] == holders[None, :]) & (ref_index[:, None] > ref_index[None, :])
    ranking = jnp.sum(earlier.astype(jnp.int32), axis=1)
    matched = (holders[:, None, None] == jnp.arange(req_count, dtype=jnp.int32)[None, :, None]) & (
        ranking[:, None, None] == jnp.arange(capacity, dtype=jnp.int32)[None, None, :]
    )
    request_table = jnp.sum(jnp.where(matched, places[:, None, None] + 1, 0), axis=0) - 1
    asked = lax.all_to_all(request_table, "req", split_axis=0, concat_axis=0, tiled=True)
    wanted = jnp.maximum(asked, 0)
    tp_count = lax.axis_size("tp")
    half = tp_index % 2
    partner = [(i, i ^ 1) for i in range(tp_count)]
    arrival_index = holders * capacity + ranking

    own_cache = jnp.where(half == 0, cache_keys, cache_values)
    outgoing = lax.dynamic_slice_in_dim(own_cache, kv_head * HD, HD, 2)[wanted]
    arrived = lax.all_to_all(outgoing, "req", split_axis=0, concat_axis=0, tiled=True)
    swapped = lax.ppermute(arrived, "tp", partner)
    attention = sparse_attention(
        queries,
        arrived.reshape(-1, page_len, HD),
        swapped.reshape(-1, page_len, HD),
        arrival_index,
        new_keys,
        new_values,
        half,
        kv_head,
        page_counts[0], last_fill[0], row_counts[0], page_total,
    )
    tp_size = lax.axis_size("tp")
    full_weight = lax.all_gather(out_weight, "tp", axis=0, tiled=True)
    ple_joined = lax.all_gather(
        jnp.concatenate([ple_gate_weight, ple_proj_weight.T], axis=1), "tp", axis=0, tiled=True
    )
    full_gate_weight = ple_joined[:, : ple_gate_weight.shape[1]]
    full_proj_weight_t = ple_joined[:, ple_gate_weight.shape[1] :]
    hidden_parts = hidden.reshape(tp_size, -1, hidden.shape[1])
    gain_rows = jnp.zeros((8, hidden.shape[1]), hidden.dtype).at[0].set(attn_gain).at[1].set(ple_gain)
    with_gains = jnp.concatenate(
        [hidden_parts, jnp.broadcast_to(gain_rows[None], (tp_size, 8, hidden.shape[1]))], axis=1
    )
    row_hidden_gains = rows_to_columns(with_gains.reshape(-1, hidden.shape[1]), "tp")
    row_hidden = row_hidden_gains[: hidden_parts.shape[1]]
    full_attn_gain = row_hidden_gains[hidden_parts.shape[1]]
    full_ple_gain = row_hidden_gains[hidden_parts.shape[1] + 1]
    row_attention = rows_to_columns(attention, "tp")
    part_rows = row_attention.shape[0]
    row_ple = lax.dynamic_slice_in_dim(ple_input, tp_index * part_rows, part_rows, 0)
    projected = jnp.dot(row_attention, full_weight, preferred_element_type=jnp.float32)
    squares = jnp.sum(projected * projected, axis=1)
    normed = (
        projected
        * lax.rsqrt(squares / D + 1e-06)[:, None]
        * full_attn_gain.astype(jnp.float32)[None, :]
    )
    mixed_state = (row_hidden.astype(jnp.float32) + normed).astype(jnp.bfloat16)
    gate = jnp.dot(mixed_state, full_gate_weight, preferred_element_type=jnp.float32)
    activated = (jax.nn.gelu(gate, approximate=True) * row_ple.astype(jnp.float32)).astype(
        jnp.bfloat16
    )
    lifted = lax.dot_general(
        activated, full_proj_weight_t, (((1,), (1,)), ((), ())), preferred_element_type=jnp.float32
    )
    lift_squares = jnp.sum(lifted * lifted, axis=1)
    lift_normed = (
        lifted
        * lax.rsqrt(lift_squares / D + 1e-06)[:, None]
        * full_ple_gain.astype(jnp.float32)[None, :]
    )
    row_out = (mixed_state.astype(jnp.float32) + lift_normed).astype(jnp.bfloat16)
    return columns_to_rows(row_out, "tp")


def solution(mesh):
    return jax.shard_map(
        shards,
        mesh=mesh,
        in_specs=(
            P("req", "tp"),
            P("req", "tp"),
            P("req", None),
            P("req", None),
            P("req", None, None),
            P("req", None, None),
            P("tp", None),
            P("tp"),
            P("req", None),
            P("tp", None),
            P(None, "tp"),
            P("tp"),
            P("req", None),
            P("req", None),
            P("req", None),
            P("req", None),
            P("req", None),
        ),
        out_specs=P("req", "tp"),
        check_vma=False,
    )
```

```python
import math

import jax
import jax.numpy as jnp
from jax import lax
from jax.experimental import pallas as pl
from jax.experimental.pallas import tpu as pltpu
from jax.sharding import PartitionSpec as P

D = 2048
HD = 256


def slot_lookup(positions, counts):
    starts = jnp.cumsum(counts) - counts
    owning = jnp.sum((positions[:, None] >= starts[None, :]).astype(jnp.int32), axis=1) - 1
    return (owning, starts)


def table_pick(table, owning):
    onehot = owning[:, None] == jnp.arange(table.shape[0], dtype=jnp.int32)[None, :]
    return jnp.sum(jnp.where(onehot, table[None, :], 0), axis=1)


def attend_masks(counts_of_pages, fill_row, counts_of_rows, page_len, page_total, row_total):
    key_index = jnp.arange(page_total * page_len, dtype=jnp.int32)
    page_ref = key_index // page_len
    within = key_index % page_len
    page_owner, page_starts = slot_lookup(page_ref, counts_of_pages)
    context_len = (counts_of_pages - 1) * page_len + fill_row
    position = (page_ref - table_pick(page_starts, page_owner)) * page_len + within
    valid = position < table_pick(context_len, page_owner)
    row_index = jnp.arange(row_total, dtype=jnp.int32)
    row_owner = slot_lookup(row_index, counts_of_rows)[0]
    context_mask = (row_owner[:, None] == page_owner[None, :]) & valid[None, :]
    causal = (row_owner[:, None] == row_owner[None, :]) & (row_index[None, :] <= row_index[:, None])
    return jnp.concatenate([context_mask, causal], axis=1)


ROW_BLOCK = 128
KEY_CHUNK = 256


def pick(table, index):
    onehot = index[:, None] == jnp.arange(table.shape[0], dtype=jnp.int32)[None, :]
    return jnp.sum(jnp.where(onehot, table[None, :], 0), axis=1)


def attention_kernel(
    ranges_ref,
    slots_ref,
    meta_ref,
    q_ref,
    own_ref,
    partner_ref,
    fresh_k_ref,
    fresh_v_ref,
    kown_ref,
    kpos_ref,
    rown_ref,
    o_ref,
    s_scr,
    acc_scr,
):
    block = pl.program_id(0)
    ctx_lo = ranges_ref[block, 0]
    ctx_n = ranges_ref[block, 1]
    new_lo = ranges_ref[block, 2]
    total = ctx_n + ranges_ref[block, 3]
    ctx_chunks = ranges_ref[block, 4]
    keys_are_own = meta_ref[0] == 0
    heads = q_ref.shape[1] // HD
    page_len = own_ref.shape[1]
    per_chunk = KEY_CHUNK // page_len
    q = q_ref[...]
    stacked = jnp.concatenate([q[:, h * HD:(h + 1) * HD] for h in range(heads)], axis=0)
    row_owner = rown_ref[...]
    row_index = block * ROW_BLOCK + lax.broadcasted_iota(jnp.int32, (ROW_BLOCK, 1), 0)
    scale = 1.0 / math.sqrt(HD)

    def chunk_of(t):
        return jnp.where(t < ctx_n, ctx_lo + t, ctx_chunks + new_lo + t - ctx_n)

    def load_chunk(c, want_keys, fresh_ref):
        pick_own = keys_are_own == want_keys

        def cached():
            pages = []
            for i in range(per_chunk):
                slot = slots_ref[c * per_chunk + i]
                pages.append(jnp.where(pick_own, own_ref[slot], partner_ref[slot]))
            return jnp.concatenate(pages, axis=0)

        def fresh():
            start = pl.multiple_of((c - ctx_chunks) * KEY_CHUNK, KEY_CHUNK)
            return fresh_ref[pl.ds(start, KEY_CHUNK), :]

        return lax.cond(c < ctx_chunks, cached, fresh)

    def scores_pass(t, highest):
        c = chunk_of(t)
        keys = load_chunk(c, True, fresh_k_ref)
        s = lax.dot_general(
            stacked, keys, (((1,), (1,)), ((), ())), preferred_element_type=jnp.float32
        ) * scale
        seen = (kown_ref[c] == row_owner) & (kpos_ref[c] <= row_index)
        seen = jnp.concatenate([seen] * heads, axis=0)
        s = jnp.where(seen, s, -1e30)
        s_scr[c] = s
        return jnp.maximum(highest, jnp.max(s, axis=1, keepdims=True))

    highest = lax.fori_loop(
        0, total, scores_pass, jnp.full((heads * ROW_BLOCK, 1), -1e30, jnp.float32)
    )

    acc_scr[...] = jnp.zeros(acc_scr.shape, jnp.float32)

    def value_pass(t, summed):
        c = chunk_of(t)
        e = jnp.exp(s_scr[c] - highest)
        values = load_chunk(c, False, fresh_v_ref)
        acc_scr[...] += jnp.dot(e.astype(jnp.bfloat16), values, preferred_element_type=jnp.float32)
        return summed + jnp.sum(e, axis=1, keepdims=True)

    summed = lax.fori_loop(0, total, value_pass, jnp.zeros((heads * ROW_BLOCK, 1), jnp.float32))
    acc_scr[...] = acc_scr[...] / summed
    for h in range(heads):
        o_ref[:, h * HD:(h + 1) * HD] = acc_scr[h * ROW_BLOCK:(h + 1) * ROW_BLOCK, :].astype(
            jnp.bfloat16
        )


def sparse_attention(
    queries, own_pages, partner_pages, slots, new_keys, new_values, half, kv_head,
    page_counts, last_fill, row_counts, page_total,
):
    row_total = queries.shape[0]
    page_len = own_pages.shape[1]
    ctx_total = page_total * page_len
    key_total = ctx_total + row_total
    heads = queries.shape[1] // HD
    blocks = row_total // ROW_BLOCK
    chunks = key_total // KEY_CHUNK
    ctx_chunks = ctx_total // KEY_CHUNK
    key_index = jnp.arange(ctx_total, dtype=jnp.int32)
    page_ref = key_index // page_len
    page_owner, page_starts = slot_lookup(page_ref, page_counts)
    context_len = (page_counts - 1) * page_len + last_fill
    position = (page_ref - table_pick(page_starts, page_owner)) * page_len + key_index % page_len
    valid = position < table_pick(context_len, page_owner)
    row_index = jnp.arange(row_total, dtype=jnp.int32)
    row_owner, row_starts = slot_lookup(row_index, row_counts)
    key_owner = jnp.concatenate([jnp.where(valid, page_owner, -1), row_owner])
    key_pos = jnp.concatenate([jnp.full((ctx_total,), -1, jnp.int32), row_index])
    first = row_owner[::ROW_BLOCK]
    last = row_owner[ROW_BLOCK - 1::ROW_BLOCK]
    ctx_from = pick(page_starts, first) * page_len
    ctx_to = (pick(page_starts, last) + pick(page_counts, last)) * page_len
    ctx_lo = ctx_from // KEY_CHUNK
    ctx_n = (ctx_to + KEY_CHUNK - 1) // KEY_CHUNK - ctx_lo
    new_from = pick(row_starts, first)
    new_to = jnp.arange(1, blocks + 1, dtype=jnp.int32) * ROW_BLOCK
    new_lo = new_from // KEY_CHUNK
    new_n = (new_to + KEY_CHUNK - 1) // KEY_CHUNK - new_lo
    ranges = jnp.stack(
        [ctx_lo, ctx_n, new_lo, new_n, jnp.full((blocks,), ctx_chunks, jnp.int32)], axis=1
    ).astype(jnp.int32)
    meta = jnp.stack([half, kv_head]).astype(jnp.int32)
    whole = lambda b, r, s, m: (0, 0, 0)
    return pl.pallas_call(
        attention_kernel,
        grid_spec=pltpu.PrefetchScalarGridSpec(
            num_scalar_prefetch=3,
            grid=(blocks,),
            in_specs=[
                pl.BlockSpec((ROW_BLOCK, heads * HD), lambda b, r, s, m: (b, 0)),
                pl.BlockSpec(own_pages.shape, whole),
                pl.BlockSpec(partner_pages.shape, whole),
                pl.BlockSpec((row_total, HD), lambda b, r, s, m: (0, m[1])),
                pl.BlockSpec((row_total, HD), lambda b, r, s, m: (0, m[1])),
                pl.BlockSpec((chunks, 1, KEY_CHUNK), whole),
                pl.BlockSpec((chunks, 1, KEY_CHUNK), whole),
                pl.BlockSpec((ROW_BLOCK, 1), lambda b, r, s, m: (b, 0)),
            ],
            out_specs=pl.BlockSpec((ROW_BLOCK, heads * HD), lambda b, r, s, m: (b, 0)),
            scratch_shapes=[
                pltpu.VMEM((chunks, heads * ROW_BLOCK, KEY_CHUNK), jnp.float32),
                pltpu.VMEM((heads * ROW_BLOCK, HD), jnp.float32),
            ],
        ),
        out_shape=jax.ShapeDtypeStruct((row_total, heads * HD), jnp.bfloat16),
    )(
        ranges,
        slots.astype(jnp.int32),
        meta,
        queries,
        own_pages,
        partner_pages,
        new_keys,
        new_values,
        key_owner.reshape(chunks, 1, KEY_CHUNK),
        key_pos.reshape(chunks, 1, KEY_CHUNK),
        row_owner.reshape(row_total, 1),
    )


def rows_to_columns(x, axis_name):
    count = lax.axis_size(axis_name)
    me = lax.axis_index(axis_name)
    parts = x.reshape(count, x.shape[0] // count, x.shape[1])
    received = [parts[me]]
    for shift in range(1, count):
        outgoing = lax.dynamic_index_in_dim(parts, (me + shift) % count, 0, keepdims=False)
        perm = [(i, (i + shift) % count) for i in range(count)]
        received.append(lax.ppermute(outgoing, axis_name, perm))
    order = (me - jnp.arange(count, dtype=jnp.int32)) % count
    blocks = jnp.stack(received)[order]
    return jnp.transpose(blocks, (1, 0, 2)).reshape(parts.shape[1], count * x.shape[1])


def columns_to_rows(x, axis_name):
    count = lax.axis_size(axis_name)
    me = lax.axis_index(axis_name)
    width = x.shape[1] // count
    received = [lax.dynamic_slice_in_dim(x, me * width, width, 1)]
    for shift in range(1, count):
        outgoing = lax.dynamic_slice_in_dim(x, ((me + shift) % count) * width, width, 1)
        perm = [(i, (i + shift) % count) for i in range(count)]
        received.append(lax.ppermute(outgoing, axis_name, perm))
    order = (me - jnp.arange(count, dtype=jnp.int32)) % count
    return jnp.stack(received)[order].reshape(count * x.shape[0], width)


def shards(
    hidden,
    queries,
    new_keys,
    new_values,
    cache_keys,
    cache_values,
    out_weight,
    attn_gain,
    ple_input,
    ple_gate_weight,
    ple_proj_weight,
    ple_gain,
    page_holder,
    page_slot,
    page_counts,
    last_fill,
    row_counts,
):
    row_total = hidden.shape[0]
    page_total = cache_keys.shape[0]
    page_len = cache_keys.shape[1]
    req_count = lax.axis_size("req")
    tp_index = lax.axis_index("tp")
    local_heads = queries.shape[1] // HD
    kv_head = tp_index // 2
    capacity = max(2, page_total // req_count)
    holders = page_holder[:, 0]
    places = page_slot[:, 0]
    ref_index = jnp.arange(page_total, dtype=jnp.int32)
    earlier = (holders[:, None] == holders[None, :]) & (ref_index[:, None] > ref_index[None, :])
    ranking = jnp.sum(earlier.astype(jnp.int32), axis=1)
    matched = (holders[:, None, None] == jnp.arange(req_count, dtype=jnp.int32)[None, :, None]) & (
        ranking[:, None, None] == jnp.arange(capacity, dtype=jnp.int32)[None, None, :]
    )
    request_table = jnp.sum(jnp.where(matched, places[:, None, None] + 1, 0), axis=0) - 1
    asked = lax.all_to_all(request_table, "req", split_axis=0, concat_axis=0, tiled=True)
    wanted = jnp.maximum(asked, 0)
    tp_count = lax.axis_size("tp")
    half = tp_index % 2
    partner = [(i, i ^ 1) for i in range(tp_count)]
    arrival_index = holders * capacity + ranking

    own_cache = jnp.where(half == 0, cache_keys, cache_values)
    outgoing = lax.dynamic_slice_in_dim(own_cache, kv_head * HD, HD, 2)[wanted]
    arrived = lax.all_to_all(outgoing, "req", split_axis=0, concat_axis=0, tiled=True)
    swapped = lax.ppermute(arrived, "tp", partner)
    attention = sparse_attention(
        queries,
        arrived.reshape(-1, page_len, HD),
        swapped.reshape(-1, page_len, HD),
        arrival_index,
        new_keys,
        new_values,
        half,
        kv_head,
        page_counts[0], last_fill[0], row_counts[0], page_total,
    )
    tp_size = lax.axis_size("tp")
    full_weight = lax.all_gather(out_weight, "tp", axis=0, tiled=True)
    ple_joined = lax.all_gather(
        jnp.concatenate([ple_gate_weight, ple_proj_weight.T], axis=1), "tp", axis=0, tiled=True
    )
    full_gate_weight = ple_joined[:, : ple_gate_weight.shape[1]]
    full_proj_weight_t = ple_joined[:, ple_gate_weight.shape[1] :]
    hidden_parts = hidden.reshape(tp_size, -1, hidden.shape[1])
    gain_rows = jnp.zeros((8, hidden.shape[1]), hidden.dtype).at[0].set(attn_gain).at[1].set(ple_gain)
    with_gains = jnp.concatenate(
        [hidden_parts, jnp.broadcast_to(gain_rows[None], (tp_size, 8, hidden.shape[1]))], axis=1
    )
    row_hidden_gains = rows_to_columns(with_gains.reshape(-1, hidden.shape[1]), "tp")
    row_hidden = row_hidden_gains[: hidden_parts.shape[1]]
    full_attn_gain = row_hidden_gains[hidden_parts.shape[1]]
    full_ple_gain = row_hidden_gains[hidden_parts.shape[1] + 1]
    row_attention = rows_to_columns(attention, "tp")
    part_rows = row_attention.shape[0]
    row_ple = lax.dynamic_slice_in_dim(ple_input, tp_index * part_rows, part_rows, 0)
    projected = jnp.dot(row_attention, full_weight, preferred_element_type=jnp.float32)
    squares = jnp.sum(projected * projected, axis=1)
    normed = (
        projected
        * lax.rsqrt(squares / D + 1e-06)[:, None]
        * full_attn_gain.astype(jnp.float32)[None, :]
    )
    mixed_state = (row_hidden.astype(jnp.float32) + normed).astype(jnp.bfloat16)
    gate = jnp.dot(mixed_state, full_gate_weight, preferred_element_type=jnp.float32)
    activated = (jax.nn.gelu(gate, approximate=True) * row_ple.astype(jnp.float32)).astype(
        jnp.bfloat16
    )
    lifted = lax.dot_general(
        activated, full_proj_weight_t, (((1,), (1,)), ((), ())), preferred_element_type=jnp.float32
    )
    lift_squares = jnp.sum(lifted * lifted, axis=1)
    lift_normed = (
        lifted
        * lax.rsqrt(lift_squares / D + 1e-06)[:, None]
        * full_ple_gain.astype(jnp.float32)[None, :]
    )
    row_out = (mixed_state.astype(jnp.float32) + lift_normed).astype(jnp.bfloat16)
    return columns_to_rows(row_out, "tp")


def solution(mesh):
    return jax.shard_map(
        shards,
        mesh=mesh,
        in_specs=(
            P("req", "tp"),
            P("req", "tp"),
            P("req", None),
            P("req", None),
            P("req", None, None),
            P("req", None, None),
            P("tp", None),
            P("tp"),
            P("req", None),
            P("tp", None),
            P(None, "tp"),
            P("tp"),
            P("req", None),
            P("req", None),
            P("req", None),
            P("req", None),
            P("req", None),
        ),
        out_specs=P("req", "tp"),
        check_vma=False,
    )
```

```python
import math

import jax
import jax.numpy as jnp
from jax import lax
from jax.experimental import pallas as pl
from jax.experimental.pallas import tpu as pltpu
from jax.sharding import PartitionSpec as P

D = 2048
HD = 256


def slot_lookup(positions, counts):
    starts = jnp.cumsum(counts) - counts
    owning = jnp.sum((positions[:, None] >= starts[None, :]).astype(jnp.int32), axis=1) - 1
    return (owning, starts)


def table_pick(table, owning):
    onehot = owning[:, None] == jnp.arange(table.shape[0], dtype=jnp.int32)[None, :]
    return jnp.sum(jnp.where(onehot, table[None, :], 0), axis=1)


def attend_masks(counts_of_pages, fill_row, counts_of_rows, page_len, page_total, row_total):
    key_index = jnp.arange(page_total * page_len, dtype=jnp.int32)
    page_ref = key_index // page_len
    within = key_index % page_len
    page_owner, page_starts = slot_lookup(page_ref, counts_of_pages)
    context_len = (counts_of_pages - 1) * page_len + fill_row
    position = (page_ref - table_pick(page_starts, page_owner)) * page_len + within
    valid = position < table_pick(context_len, page_owner)
    row_index = jnp.arange(row_total, dtype=jnp.int32)
    row_owner = slot_lookup(row_index, counts_of_rows)[0]
    context_mask = (row_owner[:, None] == page_owner[None, :]) & valid[None, :]
    causal = (row_owner[:, None] == row_owner[None, :]) & (row_index[None, :] <= row_index[:, None])
    return jnp.concatenate([context_mask, causal], axis=1)


ROW_BLOCK = 128
KEY_CHUNK = 256


def pick(table, index):
    onehot = index[:, None] == jnp.arange(table.shape[0], dtype=jnp.int32)[None, :]
    return jnp.sum(jnp.where(onehot, table[None, :], 0), axis=1)


def attention_kernel(
    ranges_ref,
    slots_ref,
    meta_ref,
    order_ref,
    q_ref,
    own_ref,
    partner_ref,
    fresh_k_ref,
    fresh_v_ref,
    kown_ref,
    kpos_ref,
    rown_ref,
    o_ref,
    s_scr,
    acc_scr,
):
    block = order_ref[pl.program_id(0)]
    ctx_lo = ranges_ref[block, 0]
    ctx_n = ranges_ref[block, 1]
    new_lo = ranges_ref[block, 2]
    total = ctx_n + ranges_ref[block, 3]
    ctx_chunks = ranges_ref[block, 4]
    keys_are_own = meta_ref[0] == 0
    heads = q_ref.shape[1] // HD
    page_len = own_ref.shape[1]
    per_chunk = KEY_CHUNK // page_len
    q = q_ref[...]
    stacked = jnp.concatenate([q[:, h * HD:(h + 1) * HD] for h in range(heads)], axis=0)
    row_owner = rown_ref[...]
    row_index = block * ROW_BLOCK + lax.broadcasted_iota(jnp.int32, (ROW_BLOCK, 1), 0)
    scale = 1.0 / math.sqrt(HD)

    def chunk_of(t):
        return jnp.where(t < ctx_n, ctx_lo + t, ctx_chunks + new_lo + t - ctx_n)

    def load_chunk(c, want_keys, fresh_ref):
        pick_own = keys_are_own == want_keys

        def cached():
            pages = []
            for i in range(per_chunk):
                slot = slots_ref[c * per_chunk + i]
                pages.append(jnp.where(pick_own, own_ref[slot], partner_ref[slot]))
            return jnp.concatenate(pages, axis=0)

        def fresh():
            start = pl.multiple_of((c - ctx_chunks) * KEY_CHUNK, KEY_CHUNK)
            return fresh_ref[pl.ds(start, KEY_CHUNK), :]

        return lax.cond(c < ctx_chunks, cached, fresh)

    def scores_pass(t, highest):
        c = chunk_of(t)
        keys = load_chunk(c, True, fresh_k_ref)
        s = lax.dot_general(
            stacked, keys, (((1,), (1,)), ((), ())), preferred_element_type=jnp.float32
        ) * scale
        seen = (kown_ref[c] == row_owner) & (kpos_ref[c] <= row_index)
        seen = jnp.concatenate([seen] * heads, axis=0)
        s = jnp.where(seen, s, -1e30)
        s_scr[c] = s
        return jnp.maximum(highest, jnp.max(s, axis=1, keepdims=True))

    highest = lax.fori_loop(
        0, total, scores_pass, jnp.full((heads * ROW_BLOCK, 1), -1e30, jnp.float32)
    )

    def exp_pass(t, summed):
        c = chunk_of(t)
        e = jnp.exp(s_scr[c] - highest)
        s_scr[c] = e
        return summed + jnp.sum(e, axis=1, keepdims=True)

    summed = lax.fori_loop(0, total, exp_pass, jnp.zeros((heads * ROW_BLOCK, 1), jnp.float32))
    inverse = 1.0 / summed
    acc_scr[...] = jnp.zeros(acc_scr.shape, jnp.float32)

    def value_pass(t, carry):
        c = chunk_of(t)
        w = (s_scr[c] * inverse).astype(jnp.bfloat16)
        values = load_chunk(c, False, fresh_v_ref)
        acc_scr[...] += jnp.dot(w, values, preferred_element_type=jnp.float32)
        return carry

    lax.fori_loop(0, total, value_pass, 0)
    for h in range(heads):
        o_ref[:, h * HD:(h + 1) * HD] = acc_scr[h * ROW_BLOCK:(h + 1) * ROW_BLOCK, :].astype(
            jnp.bfloat16
        )


def sparse_attention(
    queries, own_pages, partner_pages, slots, new_keys, new_values, half, kv_head,
    page_counts, last_fill, row_counts, page_total, order,
):
    row_total = queries.shape[0]
    page_len = own_pages.shape[1]
    ctx_total = page_total * page_len
    key_total = ctx_total + row_total
    heads = queries.shape[1] // HD
    blocks = row_total // ROW_BLOCK
    chunks = key_total // KEY_CHUNK
    ctx_chunks = ctx_total // KEY_CHUNK
    key_index = jnp.arange(ctx_total, dtype=jnp.int32)
    page_ref = key_index // page_len
    page_owner, page_starts = slot_lookup(page_ref, page_counts)
    context_len = (page_counts - 1) * page_len + last_fill
    position = (page_ref - table_pick(page_starts, page_owner)) * page_len + key_index % page_len
    valid = position < table_pick(context_len, page_owner)
    row_index = jnp.arange(row_total, dtype=jnp.int32)
    row_owner, row_starts = slot_lookup(row_index, row_counts)
    key_owner = jnp.concatenate([jnp.where(valid, page_owner, -1), row_owner])
    key_pos = jnp.concatenate([jnp.full((ctx_total,), -1, jnp.int32), row_index])
    first = row_owner[::ROW_BLOCK]
    last = row_owner[ROW_BLOCK - 1::ROW_BLOCK]
    ctx_from = pick(page_starts, first) * page_len
    ctx_to = (pick(page_starts, last) + pick(page_counts, last)) * page_len
    ctx_lo = ctx_from // KEY_CHUNK
    ctx_n = (ctx_to + KEY_CHUNK - 1) // KEY_CHUNK - ctx_lo
    new_from = pick(row_starts, first)
    new_to = jnp.arange(1, blocks + 1, dtype=jnp.int32) * ROW_BLOCK
    new_lo = new_from // KEY_CHUNK
    new_n = (new_to + KEY_CHUNK - 1) // KEY_CHUNK - new_lo
    ranges = jnp.stack(
        [ctx_lo, ctx_n, new_lo, new_n, jnp.full((blocks,), ctx_chunks, jnp.int32)], axis=1
    ).astype(jnp.int32)
    meta = jnp.stack([half, kv_head]).astype(jnp.int32)
    whole = lambda b, r, s, m, o: (0, 0, 0)
    by_order = lambda b, r, s, m, o: (o[b], 0)
    by_head = lambda b, r, s, m, o: (0, m[1])
    operands = (
        ranges,
        slots.astype(jnp.int32),
        meta,
        order.astype(jnp.int32),
        queries,
        own_pages,
        partner_pages,
        new_keys,
        new_values,
        key_owner.reshape(chunks, 1, KEY_CHUNK),
        key_pos.reshape(chunks, 1, KEY_CHUNK),
        row_owner.reshape(row_total, 1),
    )
    return pl.pallas_call(
        attention_kernel,
        grid_spec=pltpu.PrefetchScalarGridSpec(
            num_scalar_prefetch=4,
            grid=(order.shape[0],),
            in_specs=[
                pl.BlockSpec((ROW_BLOCK, heads * HD), by_order),
                pl.BlockSpec(own_pages.shape, whole),
                pl.BlockSpec(partner_pages.shape, whole),
                pl.BlockSpec((row_total, HD), by_head),
                pl.BlockSpec((row_total, HD), by_head),
                pl.BlockSpec((chunks, 1, KEY_CHUNK), whole),
                pl.BlockSpec((chunks, 1, KEY_CHUNK), whole),
                pl.BlockSpec((ROW_BLOCK, 1), by_order),
            ],
            out_specs=pl.BlockSpec((ROW_BLOCK, heads * HD), lambda b, r, s, m, o: (b, 0)),
            scratch_shapes=[
                pltpu.VMEM((chunks, heads * ROW_BLOCK, KEY_CHUNK), jnp.float32),
                pltpu.VMEM((heads * ROW_BLOCK, HD), jnp.float32),
            ],
        ),
        out_shape=jax.ShapeDtypeStruct((order.shape[0] * ROW_BLOCK, heads * HD), jnp.bfloat16),
    )(*operands)


def rows_to_columns(x, axis_name):
    count = lax.axis_size(axis_name)
    me = lax.axis_index(axis_name)
    parts = x.reshape(count, x.shape[0] // count, x.shape[1])
    received = [parts[me]]
    for shift in range(1, count):
        outgoing = lax.dynamic_index_in_dim(parts, (me + shift) % count, 0, keepdims=False)
        perm = [(i, (i + shift) % count) for i in range(count)]
        received.append(lax.ppermute(outgoing, axis_name, perm))
    order = (me - jnp.arange(count, dtype=jnp.int32)) % count
    blocks = jnp.stack(received)[order]
    return jnp.transpose(blocks, (1, 0, 2)).reshape(parts.shape[1], count * x.shape[1])


def columns_to_rows(x, axis_name):
    count = lax.axis_size(axis_name)
    me = lax.axis_index(axis_name)
    width = x.shape[1] // count
    received = [lax.dynamic_slice_in_dim(x, me * width, width, 1)]
    for shift in range(1, count):
        outgoing = lax.dynamic_slice_in_dim(x, ((me + shift) % count) * width, width, 1)
        perm = [(i, (i + shift) % count) for i in range(count)]
        received.append(lax.ppermute(outgoing, axis_name, perm))
    order = (me - jnp.arange(count, dtype=jnp.int32)) % count
    return jnp.stack(received)[order].reshape(count * x.shape[0], width)


def shards(
    hidden,
    queries,
    new_keys,
    new_values,
    cache_keys,
    cache_values,
    out_weight,
    attn_gain,
    ple_input,
    ple_gate_weight,
    ple_proj_weight,
    ple_gain,
    page_holder,
    page_slot,
    page_counts,
    last_fill,
    row_counts,
):
    row_total = hidden.shape[0]
    page_total = cache_keys.shape[0]
    page_len = cache_keys.shape[1]
    req_count = lax.axis_size("req")
    tp_index = lax.axis_index("tp")
    local_heads = queries.shape[1] // HD
    kv_head = tp_index // 2
    capacity = max(2, page_total // req_count)
    holders = page_holder[:, 0]
    places = page_slot[:, 0]
    ref_index = jnp.arange(page_total, dtype=jnp.int32)
    earlier = (holders[:, None] == holders[None, :]) & (ref_index[:, None] > ref_index[None, :])
    ranking = jnp.sum(earlier.astype(jnp.int32), axis=1)
    matched = (holders[:, None, None] == jnp.arange(req_count, dtype=jnp.int32)[None, :, None]) & (
        ranking[:, None, None] == jnp.arange(capacity, dtype=jnp.int32)[None, None, :]
    )
    request_table = jnp.sum(jnp.where(matched, places[:, None, None] + 1, 0), axis=0) - 1
    asked = lax.all_to_all(request_table, "req", split_axis=0, concat_axis=0, tiled=True)
    wanted = jnp.maximum(asked, 0)
    tp_count = lax.axis_size("tp")
    half = tp_index % 2
    partner = [(i, i ^ 1) for i in range(tp_count)]
    arrival_index = holders * capacity + ranking

    own_cache = jnp.where(half == 0, cache_keys, cache_values)
    outgoing = lax.dynamic_slice_in_dim(own_cache, kv_head * HD, HD, 2)[wanted]
    arrived = lax.all_to_all(outgoing, "req", split_axis=0, concat_axis=0, tiled=True)
    swapped = lax.ppermute(arrived, "tp", partner)
    assert row_total == ROW_BLOCK * tp_count
    sends = (tp_index + jnp.arange(1, tp_count, dtype=jnp.int32)) % tp_count

    def attend(order):
        return sparse_attention(
            queries,
            arrived.reshape(-1, page_len, HD),
            swapped.reshape(-1, page_len, HD),
            arrival_index,
            new_keys,
            new_values,
            half,
            kv_head,
            page_counts[0],
            last_fill[0],
            row_counts[0],
            page_total,
            order,
        )

    sent_blocks = attend(sends)
    own_block = attend(tp_index.reshape(1).astype(jnp.int32))
    tp_size = lax.axis_size("tp")
    full_weight = lax.all_gather(out_weight, "tp", axis=0, tiled=True)
    ple_joined = lax.all_gather(
        jnp.concatenate([ple_gate_weight, ple_proj_weight.T], axis=1), "tp", axis=0, tiled=True
    )
    full_gate_weight = ple_joined[:, : ple_gate_weight.shape[1]]
    full_proj_weight_t = ple_joined[:, ple_gate_weight.shape[1] :]
    hidden_parts = hidden.reshape(tp_size, -1, hidden.shape[1])
    gain_rows = jnp.zeros((8, hidden.shape[1]), hidden.dtype).at[0].set(attn_gain).at[1].set(ple_gain)
    with_gains = jnp.concatenate(
        [hidden_parts, jnp.broadcast_to(gain_rows[None], (tp_size, 8, hidden.shape[1]))], axis=1
    )
    row_hidden_gains = rows_to_columns(with_gains.reshape(-1, hidden.shape[1]), "tp")
    row_hidden = row_hidden_gains[: hidden_parts.shape[1]]
    full_attn_gain = row_hidden_gains[hidden_parts.shape[1]]
    full_ple_gain = row_hidden_gains[hidden_parts.shape[1] + 1]
    received = [own_block]
    for shift in range(1, tp_count):
        perm = [(i, (i + shift) % tp_count) for i in range(tp_count)]
        piece = sent_blocks[(shift - 1) * ROW_BLOCK : shift * ROW_BLOCK]
        received.append(lax.ppermute(piece, "tp", perm))
    source_order = (tp_index - jnp.arange(tp_count, dtype=jnp.int32)) % tp_count
    row_attention = jnp.transpose(jnp.stack(received)[source_order], (1, 0, 2)).reshape(
        ROW_BLOCK, tp_count * own_block.shape[1]
    )
    part_rows = row_attention.shape[0]
    row_ple = lax.dynamic_slice_in_dim(ple_input, tp_index * part_rows, part_rows, 0)
    projected = jnp.dot(row_attention, full_weight, preferred_element_type=jnp.float32)
    squares = jnp.sum(projected * projected, axis=1)
    normed = (
        projected
        * lax.rsqrt(squares / D + 1e-06)[:, None]
        * full_attn_gain.astype(jnp.float32)[None, :]
    )
    mixed_state = (row_hidden.astype(jnp.float32) + normed).astype(jnp.bfloat16)
    gate = jnp.dot(mixed_state, full_gate_weight, preferred_element_type=jnp.float32)
    activated = (jax.nn.gelu(gate, approximate=True) * row_ple.astype(jnp.float32)).astype(
        jnp.bfloat16
    )
    lifted = lax.dot_general(
        activated, full_proj_weight_t, (((1,), (1,)), ((), ())), preferred_element_type=jnp.float32
    )
    lift_squares = jnp.sum(lifted * lifted, axis=1)
    lift_normed = (
        lifted
        * lax.rsqrt(lift_squares / D + 1e-06)[:, None]
        * full_ple_gain.astype(jnp.float32)[None, :]
    )
    row_out = (mixed_state.astype(jnp.float32) + lift_normed).astype(jnp.bfloat16)
    return columns_to_rows(row_out, "tp")


def solution(mesh):
    return jax.shard_map(
        shards,
        mesh=mesh,
        in_specs=(
            P("req", "tp"),
            P("req", "tp"),
            P("req", None),
            P("req", None),
            P("req", None, None),
            P("req", None, None),
            P("tp", None),
            P("tp"),
            P("req", None),
            P("tp", None),
            P(None, "tp"),
            P("tp"),
            P("req", None),
            P("req", None),
            P("req", None),
            P("req", None),
            P("req", None),
        ),
        out_specs=P("req", "tp"),
        check_vma=False,
    )
```

```python
import math

import jax
import jax.numpy as jnp
from jax import lax
from jax.experimental import pallas as pl
from jax.experimental.pallas import tpu as pltpu
from jax.sharding import PartitionSpec as P

D = 2048
HD = 256


def slot_lookup(positions, counts):
    starts = jnp.cumsum(counts) - counts
    owning = jnp.sum((positions[:, None] >= starts[None, :]).astype(jnp.int32), axis=1) - 1
    return (owning, starts)


def table_pick(table, owning):
    onehot = owning[:, None] == jnp.arange(table.shape[0], dtype=jnp.int32)[None, :]
    return jnp.sum(jnp.where(onehot, table[None, :], 0), axis=1)


def attend_masks(counts_of_pages, fill_row, counts_of_rows, page_len, page_total, row_total):
    key_index = jnp.arange(page_total * page_len, dtype=jnp.int32)
    page_ref = key_index // page_len
    within = key_index % page_len
    page_owner, page_starts = slot_lookup(page_ref, counts_of_pages)
    context_len = (counts_of_pages - 1) * page_len + fill_row
    position = (page_ref - table_pick(page_starts, page_owner)) * page_len + within
    valid = position < table_pick(context_len, page_owner)
    row_index = jnp.arange(row_total, dtype=jnp.int32)
    row_owner = slot_lookup(row_index, counts_of_rows)[0]
    context_mask = (row_owner[:, None] == page_owner[None, :]) & valid[None, :]
    causal = (row_owner[:, None] == row_owner[None, :]) & (row_index[None, :] <= row_index[:, None])
    return jnp.concatenate([context_mask, causal], axis=1)


ROW_BLOCK = 128
KEY_CHUNK = 256


def pick(table, index):
    onehot = index[:, None] == jnp.arange(table.shape[0], dtype=jnp.int32)[None, :]
    return jnp.sum(jnp.where(onehot, table[None, :], 0), axis=1)


def attention_kernel(
    ranges_ref,
    slots_ref,
    meta_ref,
    q_ref,
    own_ref,
    partner_ref,
    fresh_k_ref,
    fresh_v_ref,
    kown_ref,
    kpos_ref,
    rown_ref,
    o_ref,
    s_scr,
    acc_scr,
):
    block = pl.program_id(0)
    ctx_lo = ranges_ref[block, 0]
    ctx_n = ranges_ref[block, 1]
    new_lo = ranges_ref[block, 2]
    total = ctx_n + ranges_ref[block, 3]
    ctx_chunks = ranges_ref[block, 4]
    keys_are_own = meta_ref[0] == 0
    heads = q_ref.shape[1] // HD
    page_len = own_ref.shape[1]
    per_chunk = KEY_CHUNK // page_len
    q = q_ref[...]
    stacked = jnp.concatenate([q[:, h * HD:(h + 1) * HD] for h in range(heads)], axis=0)
    row_owner = rown_ref[...]
    row_index = block * ROW_BLOCK + lax.broadcasted_iota(jnp.int32, (ROW_BLOCK, 1), 0)
    scale = 1.0 / math.sqrt(HD)

    def chunk_of(t):
        return jnp.where(t < ctx_n, ctx_lo + t, ctx_chunks + new_lo + t - ctx_n)

    def load_chunk(c, want_keys, fresh_ref):
        pick_own = keys_are_own == want_keys

        def cached():
            pages = []
            for i in range(per_chunk):
                slot = slots_ref[c * per_chunk + i]
                pages.append(jnp.where(pick_own, own_ref[slot], partner_ref[slot]))
            return jnp.concatenate(pages, axis=0)

        def fresh():
            start = pl.multiple_of((c - ctx_chunks) * KEY_CHUNK, KEY_CHUNK)
            return fresh_ref[pl.ds(start, KEY_CHUNK), :]

        return lax.cond(c < ctx_chunks, cached, fresh)

    def scores_pass(t, highest):
        c = chunk_of(t)
        keys = load_chunk(c, True, fresh_k_ref)
        s = lax.dot_general(
            stacked, keys, (((1,), (1,)), ((), ())), preferred_element_type=jnp.float32
        ) * scale
        seen = (kown_ref[c] == row_owner) & (kpos_ref[c] <= row_index)
        s = jnp.where(seen[None], s.reshape(heads, ROW_BLOCK, KEY_CHUNK), -1e30).reshape(
            heads * ROW_BLOCK, KEY_CHUNK
        )
        s_scr[c] = s
        return jnp.maximum(highest, jnp.max(s, axis=1, keepdims=True))

    highest = lax.fori_loop(
        0, total, scores_pass, jnp.full((heads * ROW_BLOCK, 1), -1e30, jnp.float32)
    )

    def exp_pass(t, summed):
        c = chunk_of(t)
        e = jnp.exp(s_scr[c] - highest)
        s_scr[c] = e
        return summed + jnp.sum(e, axis=1, keepdims=True)

    summed = lax.fori_loop(0, total, exp_pass, jnp.zeros((heads * ROW_BLOCK, 1), jnp.float32))
    inverse = 1.0 / summed
    acc_scr[...] = jnp.zeros(acc_scr.shape, jnp.float32)

    def value_pass(t, carry):
        c = chunk_of(t)
        w = (s_scr[c] * inverse).astype(jnp.bfloat16)
        values = load_chunk(c, False, fresh_v_ref)
        acc_scr[...] += jnp.dot(w, values, preferred_element_type=jnp.float32)
        return carry

    lax.fori_loop(0, total, value_pass, 0)
    for h in range(heads):
        o_ref[:, h * HD:(h + 1) * HD] = acc_scr[h * ROW_BLOCK:(h + 1) * ROW_BLOCK, :].astype(
            jnp.bfloat16
        )


def sparse_attention(
    queries, own_pages, partner_pages, slots, new_keys, new_values, half, kv_head,
    page_counts, last_fill, row_counts, page_total,
):
    row_total = queries.shape[0]
    page_len = own_pages.shape[1]
    ctx_total = page_total * page_len
    key_total = ctx_total + row_total
    heads = queries.shape[1] // HD
    blocks = row_total // ROW_BLOCK
    chunks = key_total // KEY_CHUNK
    ctx_chunks = ctx_total // KEY_CHUNK
    key_index = jnp.arange(ctx_total, dtype=jnp.int32)
    page_ref = key_index // page_len
    page_owner, page_starts = slot_lookup(page_ref, page_counts)
    context_len = (page_counts - 1) * page_len + last_fill
    position = (page_ref - table_pick(page_starts, page_owner)) * page_len + key_index % page_len
    valid = position < table_pick(context_len, page_owner)
    row_index = jnp.arange(row_total, dtype=jnp.int32)
    row_owner, row_starts = slot_lookup(row_index, row_counts)
    key_owner = jnp.concatenate([jnp.where(valid, page_owner, -1), row_owner])
    key_pos = jnp.concatenate([jnp.full((ctx_total,), -1, jnp.int32), row_index])
    first = row_owner[::ROW_BLOCK]
    last = row_owner[ROW_BLOCK - 1::ROW_BLOCK]
    ctx_from = pick(page_starts, first) * page_len
    ctx_to = (pick(page_starts, last) + pick(page_counts, last)) * page_len
    ctx_lo = ctx_from // KEY_CHUNK
    ctx_n = (ctx_to + KEY_CHUNK - 1) // KEY_CHUNK - ctx_lo
    new_from = pick(row_starts, first)
    new_to = jnp.arange(1, blocks + 1, dtype=jnp.int32) * ROW_BLOCK
    new_lo = new_from // KEY_CHUNK
    new_n = (new_to + KEY_CHUNK - 1) // KEY_CHUNK - new_lo
    ranges = jnp.stack(
        [ctx_lo, ctx_n, new_lo, new_n, jnp.full((blocks,), ctx_chunks, jnp.int32)], axis=1
    ).astype(jnp.int32)
    meta = jnp.stack([half, kv_head]).astype(jnp.int32)
    whole = lambda b, r, s, m: (0, 0, 0)
    return pl.pallas_call(
        attention_kernel,
        grid_spec=pltpu.PrefetchScalarGridSpec(
            num_scalar_prefetch=3,
            grid=(blocks,),
            in_specs=[
                pl.BlockSpec((ROW_BLOCK, heads * HD), lambda b, r, s, m: (b, 0)),
                pl.BlockSpec(own_pages.shape, whole),
                pl.BlockSpec(partner_pages.shape, whole),
                pl.BlockSpec((row_total, HD), lambda b, r, s, m: (0, m[1])),
                pl.BlockSpec((row_total, HD), lambda b, r, s, m: (0, m[1])),
                pl.BlockSpec((chunks, 1, KEY_CHUNK), whole),
                pl.BlockSpec((chunks, 1, KEY_CHUNK), whole),
                pl.BlockSpec((ROW_BLOCK, 1), lambda b, r, s, m: (b, 0)),
            ],
            out_specs=pl.BlockSpec((ROW_BLOCK, heads * HD), lambda b, r, s, m: (b, 0)),
            scratch_shapes=[
                pltpu.VMEM((chunks, heads * ROW_BLOCK, KEY_CHUNK), jnp.float32),
                pltpu.VMEM((heads * ROW_BLOCK, HD), jnp.float32),
            ],
        ),
        out_shape=jax.ShapeDtypeStruct((row_total, heads * HD), jnp.bfloat16),
    )(
        ranges,
        slots.astype(jnp.int32),
        meta,
        queries,
        own_pages,
        partner_pages,
        new_keys,
        new_values,
        key_owner.reshape(chunks, 1, KEY_CHUNK),
        key_pos.reshape(chunks, 1, KEY_CHUNK),
        row_owner.reshape(row_total, 1),
    )


def rows_to_columns(x, axis_name):
    count = lax.axis_size(axis_name)
    me = lax.axis_index(axis_name)
    parts = x.reshape(count, x.shape[0] // count, x.shape[1])
    received = [parts[me]]
    for shift in range(1, count):
        outgoing = lax.dynamic_index_in_dim(parts, (me + shift) % count, 0, keepdims=False)
        perm = [(i, (i + shift) % count) for i in range(count)]
        received.append(lax.ppermute(outgoing, axis_name, perm))
    order = (me - jnp.arange(count, dtype=jnp.int32)) % count
    blocks = jnp.stack(received)[order]
    return jnp.transpose(blocks, (1, 0, 2)).reshape(parts.shape[1], count * x.shape[1])


def columns_to_rows(x, axis_name):
    count = lax.axis_size(axis_name)
    me = lax.axis_index(axis_name)
    width = x.shape[1] // count
    received = [lax.dynamic_slice_in_dim(x, me * width, width, 1)]
    for shift in range(1, count):
        outgoing = lax.dynamic_slice_in_dim(x, ((me + shift) % count) * width, width, 1)
        perm = [(i, (i + shift) % count) for i in range(count)]
        received.append(lax.ppermute(outgoing, axis_name, perm))
    order = (me - jnp.arange(count, dtype=jnp.int32)) % count
    return jnp.stack(received)[order].reshape(count * x.shape[0], width)


def shards(
    hidden,
    queries,
    new_keys,
    new_values,
    cache_keys,
    cache_values,
    out_weight,
    attn_gain,
    ple_input,
    ple_gate_weight,
    ple_proj_weight,
    ple_gain,
    page_holder,
    page_slot,
    page_counts,
    last_fill,
    row_counts,
):
    row_total = hidden.shape[0]
    page_total = cache_keys.shape[0]
    page_len = cache_keys.shape[1]
    req_count = lax.axis_size("req")
    tp_index = lax.axis_index("tp")
    local_heads = queries.shape[1] // HD
    kv_head = tp_index // 2
    capacity = max(2, page_total // req_count)
    holders = page_holder[:, 0]
    places = page_slot[:, 0]
    ref_index = jnp.arange(page_total, dtype=jnp.int32)
    earlier = (holders[:, None] == holders[None, :]) & (ref_index[:, None] > ref_index[None, :])
    ranking = jnp.sum(earlier.astype(jnp.int32), axis=1)
    matched = (holders[:, None, None] == jnp.arange(req_count, dtype=jnp.int32)[None, :, None]) & (
        ranking[:, None, None] == jnp.arange(capacity, dtype=jnp.int32)[None, None, :]
    )
    request_table = jnp.sum(jnp.where(matched, places[:, None, None] + 1, 0), axis=0) - 1
    asked = lax.all_to_all(request_table, "req", split_axis=0, concat_axis=0, tiled=True)
    wanted = jnp.maximum(asked, 0)
    tp_count = lax.axis_size("tp")
    half = tp_index % 2
    partner = [(i, i ^ 1) for i in range(tp_count)]
    arrival_index = holders * capacity + ranking

    own_cache = jnp.where(half == 0, cache_keys, cache_values)
    outgoing = lax.dynamic_slice_in_dim(own_cache, kv_head * HD, HD, 2)[wanted]
    arrived = lax.all_to_all(outgoing, "req", split_axis=0, concat_axis=0, tiled=True)
    swapped = lax.ppermute(arrived, "tp", partner)
    attention = sparse_attention(
        queries,
        arrived.reshape(-1, page_len, HD),
        swapped.reshape(-1, page_len, HD),
        arrival_index,
        new_keys,
        new_values,
        half,
        kv_head,
        page_counts[0], last_fill[0], row_counts[0], page_total,
    )
    tp_size = lax.axis_size("tp")
    full_weight = lax.all_gather(out_weight, "tp", axis=0, tiled=True)
    ple_joined = lax.all_gather(
        jnp.concatenate([ple_gate_weight, ple_proj_weight.T], axis=1), "tp", axis=0, tiled=True
    )
    full_gate_weight = ple_joined[:, : ple_gate_weight.shape[1]]
    full_proj_weight_t = ple_joined[:, ple_gate_weight.shape[1] :]
    hidden_parts = hidden.reshape(tp_size, -1, hidden.shape[1])
    gain_rows = jnp.zeros((8, hidden.shape[1]), hidden.dtype).at[0].set(attn_gain).at[1].set(ple_gain)
    with_gains = jnp.concatenate(
        [hidden_parts, jnp.broadcast_to(gain_rows[None], (tp_size, 8, hidden.shape[1]))], axis=1
    )
    row_hidden_gains = rows_to_columns(with_gains.reshape(-1, hidden.shape[1]), "tp")
    row_hidden = row_hidden_gains[: hidden_parts.shape[1]]
    full_attn_gain = row_hidden_gains[hidden_parts.shape[1]]
    full_ple_gain = row_hidden_gains[hidden_parts.shape[1] + 1]
    parts = attention.reshape(tp_size, -1, attention.shape[1])
    width = attention.shape[1]
    projected = jnp.dot(
        parts[tp_index],
        lax.dynamic_slice_in_dim(full_weight, tp_index * width, width, 0),
        preferred_element_type=jnp.float32,
    )
    for shift in range(1, tp_size):
        outgoing = lax.dynamic_index_in_dim(parts, (tp_index + shift) % tp_size, 0, keepdims=False)
        perm = [(i, (i + shift) % tp_size) for i in range(tp_size)]
        piece = lax.ppermute(outgoing, "tp", perm)
        source = (tp_index - shift) % tp_size
        projected = projected + jnp.dot(
            piece,
            lax.dynamic_slice_in_dim(full_weight, source * width, width, 0),
            preferred_element_type=jnp.float32,
        )
    part_rows = parts.shape[1]
    row_ple = lax.dynamic_slice_in_dim(ple_input, tp_index * part_rows, part_rows, 0)
    squares = jnp.sum(projected * projected, axis=1)
    normed = (
        projected
        * lax.rsqrt(squares / D + 1e-06)[:, None]
        * full_attn_gain.astype(jnp.float32)[None, :]
    )
    mixed_state = (row_hidden.astype(jnp.float32) + normed).astype(jnp.bfloat16)
    gate = jnp.dot(mixed_state, full_gate_weight, preferred_element_type=jnp.float32)
    activated = (jax.nn.gelu(gate, approximate=True) * row_ple.astype(jnp.float32)).astype(
        jnp.bfloat16
    )
    lifted = lax.dot_general(
        activated, full_proj_weight_t, (((1,), (1,)), ((), ())), preferred_element_type=jnp.float32
    )
    lift_squares = jnp.sum(lifted * lifted, axis=1)
    lift_normed = (
        lifted
        * lax.rsqrt(lift_squares / D + 1e-06)[:, None]
        * full_ple_gain.astype(jnp.float32)[None, :]
    )
    row_out = (mixed_state.astype(jnp.float32) + lift_normed).astype(jnp.bfloat16)
    return columns_to_rows(row_out, "tp")


def solution(mesh):
    return jax.shard_map(
        shards,
        mesh=mesh,
        in_specs=(
            P("req", "tp"),
            P("req", "tp"),
            P("req", None),
            P("req", None),
            P("req", None, None),
            P("req", None, None),
            P("tp", None),
            P("tp"),
            P("req", None),
            P("tp", None),
            P(None, "tp"),
            P("tp"),
            P("req", None),
            P("req", None),
            P("req", None),
            P("req", None),
            P("req", None),
        ),
        out_specs=P("req", "tp"),
        check_vma=False,
    )
```

```python
import math

import jax
import jax.numpy as jnp
from jax import lax
from jax.experimental import pallas as pl
from jax.experimental.pallas import tpu as pltpu
from jax.sharding import PartitionSpec as P

D = 2048
HD = 256


def slot_lookup(positions, counts):
    starts = jnp.cumsum(counts) - counts
    owning = jnp.sum((positions[:, None] >= starts[None, :]).astype(jnp.int32), axis=1) - 1
    return (owning, starts)


def table_pick(table, owning):
    onehot = owning[:, None] == jnp.arange(table.shape[0], dtype=jnp.int32)[None, :]
    return jnp.sum(jnp.where(onehot, table[None, :], 0), axis=1)


def attend_masks(counts_of_pages, fill_row, counts_of_rows, page_len, page_total, row_total):
    key_index = jnp.arange(page_total * page_len, dtype=jnp.int32)
    page_ref = key_index // page_len
    within = key_index % page_len
    page_owner, page_starts = slot_lookup(page_ref, counts_of_pages)
    context_len = (counts_of_pages - 1) * page_len + fill_row
    position = (page_ref - table_pick(page_starts, page_owner)) * page_len + within
    valid = position < table_pick(context_len, page_owner)
    row_index = jnp.arange(row_total, dtype=jnp.int32)
    row_owner = slot_lookup(row_index, counts_of_rows)[0]
    context_mask = (row_owner[:, None] == page_owner[None, :]) & valid[None, :]
    causal = (row_owner[:, None] == row_owner[None, :]) & (row_index[None, :] <= row_index[:, None])
    return jnp.concatenate([context_mask, causal], axis=1)


ROW_BLOCK = 128
KEY_CHUNK = 256


def pick(table, index):
    onehot = index[:, None] == jnp.arange(table.shape[0], dtype=jnp.int32)[None, :]
    return jnp.sum(jnp.where(onehot, table[None, :], 0), axis=1)


def attention_kernel(
    ranges_ref,
    slots_ref,
    meta_ref,
    q_ref,
    own_ref,
    partner_ref,
    fresh_k_ref,
    fresh_v_ref,
    kown_ref,
    kpos_ref,
    rown_ref,
    o_ref,
    s_scr,
    acc_scr,
):
    block = pl.program_id(0)
    ctx_lo = ranges_ref[block, 0]
    ctx_n = ranges_ref[block, 1]
    new_lo = ranges_ref[block, 2]
    total = ctx_n + ranges_ref[block, 3]
    ctx_chunks = ranges_ref[block, 4]
    keys_are_own = meta_ref[0] == 0
    heads = q_ref.shape[1] // HD
    page_len = own_ref.shape[1]
    per_chunk = KEY_CHUNK // page_len
    q = q_ref[...]
    stacked = jnp.concatenate([q[:, h * HD:(h + 1) * HD] for h in range(heads)], axis=0)
    row_owner = rown_ref[...]
    row_index = block * ROW_BLOCK + lax.broadcasted_iota(jnp.int32, (ROW_BLOCK, 1), 0)
    scale = 1.0 / math.sqrt(HD)

    def chunk_of(t):
        return jnp.where(t < ctx_n, ctx_lo + t, ctx_chunks + new_lo + t - ctx_n)

    def load_chunk(c, want_keys, fresh_ref):
        pick_own = keys_are_own == want_keys

        def cached():
            pages = []
            for i in range(per_chunk):
                slot = slots_ref[c * per_chunk + i]
                pages.append(jnp.where(pick_own, own_ref[slot], partner_ref[slot]))
            return jnp.concatenate(pages, axis=0)

        def fresh():
            start = pl.multiple_of((c - ctx_chunks) * KEY_CHUNK, KEY_CHUNK)
            return fresh_ref[pl.ds(start, KEY_CHUNK), :]

        return lax.cond(c < ctx_chunks, cached, fresh)

    def scores_pass(t, highest):
        c = chunk_of(t)
        keys = load_chunk(c, True, fresh_k_ref)
        s = lax.dot_general(
            stacked, keys, (((1,), (1,)), ((), ())), preferred_element_type=jnp.float32
        ) * scale
        seen = (kown_ref[c] == row_owner) & (kpos_ref[c] <= row_index)
        s = jnp.where(seen[None], s.reshape(heads, ROW_BLOCK, KEY_CHUNK), -1e30).reshape(
            heads * ROW_BLOCK, KEY_CHUNK
        )
        s_scr[c] = s
        return jnp.maximum(highest, jnp.max(s, axis=1, keepdims=True))

    highest = lax.fori_loop(
        0, total, scores_pass, jnp.full((heads * ROW_BLOCK, 1), -1e30, jnp.float32)
    )

    def exp_pass(t, summed):
        c = chunk_of(t)
        e = jnp.exp(s_scr[c] - highest)
        s_scr[c] = e
        return summed + jnp.sum(e, axis=1, keepdims=True)

    summed = lax.fori_loop(0, total, exp_pass, jnp.zeros((heads * ROW_BLOCK, 1), jnp.float32))
    inverse = 1.0 / summed
    acc_scr[...] = jnp.zeros(acc_scr.shape, jnp.float32)

    def value_pass(t, carry):
        c = chunk_of(t)
        w = (s_scr[c] * inverse).astype(jnp.bfloat16)
        values = load_chunk(c, False, fresh_v_ref)
        acc_scr[...] += jnp.dot(w, values, preferred_element_type=jnp.float32)
        return carry

    lax.fori_loop(0, total, value_pass, 0)
    for h in range(heads):
        o_ref[:, h * HD:(h + 1) * HD] = acc_scr[h * ROW_BLOCK:(h + 1) * ROW_BLOCK, :].astype(
            jnp.bfloat16
        )


def sparse_attention(
    queries, own_pages, partner_pages, slots, new_keys, new_values, half, kv_head,
    page_counts, last_fill, row_counts, page_total,
):
    row_total = queries.shape[0]
    page_len = own_pages.shape[1]
    ctx_total = page_total * page_len
    key_total = ctx_total + row_total
    heads = queries.shape[1] // HD
    blocks = row_total // ROW_BLOCK
    chunks = key_total // KEY_CHUNK
    ctx_chunks = ctx_total // KEY_CHUNK
    key_index = jnp.arange(ctx_total, dtype=jnp.int32)
    page_ref = key_index // page_len
    page_owner, page_starts = slot_lookup(page_ref, page_counts)
    context_len = (page_counts - 1) * page_len + last_fill
    position = (page_ref - table_pick(page_starts, page_owner)) * page_len + key_index % page_len
    valid = position < table_pick(context_len, page_owner)
    row_index = jnp.arange(row_total, dtype=jnp.int32)
    row_owner, row_starts = slot_lookup(row_index, row_counts)
    key_owner = jnp.concatenate([jnp.where(valid, page_owner, -1), row_owner])
    key_pos = jnp.concatenate([jnp.full((ctx_total,), -1, jnp.int32), row_index])
    first = row_owner[::ROW_BLOCK]
    last = row_owner[ROW_BLOCK - 1::ROW_BLOCK]
    ctx_from = pick(page_starts, first) * page_len
    ctx_to = (pick(page_starts, last) + pick(page_counts, last)) * page_len
    ctx_lo = ctx_from // KEY_CHUNK
    ctx_n = (ctx_to + KEY_CHUNK - 1) // KEY_CHUNK - ctx_lo
    new_from = pick(row_starts, first)
    new_to = jnp.arange(1, blocks + 1, dtype=jnp.int32) * ROW_BLOCK
    new_lo = new_from // KEY_CHUNK
    new_n = (new_to + KEY_CHUNK - 1) // KEY_CHUNK - new_lo
    ranges = jnp.stack(
        [ctx_lo, ctx_n, new_lo, new_n, jnp.full((blocks,), ctx_chunks, jnp.int32)], axis=1
    ).astype(jnp.int32)
    meta = jnp.stack([half, kv_head]).astype(jnp.int32)
    whole = lambda b, r, s, m: (0, 0, 0)
    return pl.pallas_call(
        attention_kernel,
        grid_spec=pltpu.PrefetchScalarGridSpec(
            num_scalar_prefetch=3,
            grid=(blocks,),
            in_specs=[
                pl.BlockSpec((ROW_BLOCK, heads * HD), lambda b, r, s, m: (b, 0)),
                pl.BlockSpec(own_pages.shape, whole),
                pl.BlockSpec(partner_pages.shape, whole),
                pl.BlockSpec((row_total, HD), lambda b, r, s, m: (0, m[1])),
                pl.BlockSpec((row_total, HD), lambda b, r, s, m: (0, m[1])),
                pl.BlockSpec((chunks, 1, KEY_CHUNK), whole),
                pl.BlockSpec((chunks, 1, KEY_CHUNK), whole),
                pl.BlockSpec((ROW_BLOCK, 1), lambda b, r, s, m: (b, 0)),
            ],
            out_specs=pl.BlockSpec((ROW_BLOCK, heads * HD), lambda b, r, s, m: (b, 0)),
            scratch_shapes=[
                pltpu.VMEM((chunks, heads * ROW_BLOCK, KEY_CHUNK), jnp.float32),
                pltpu.VMEM((heads * ROW_BLOCK, HD), jnp.float32),
            ],
        ),
        out_shape=jax.ShapeDtypeStruct((row_total, heads * HD), jnp.bfloat16),
    )(
        ranges,
        slots.astype(jnp.int32),
        meta,
        queries,
        own_pages,
        partner_pages,
        new_keys,
        new_values,
        key_owner.reshape(chunks, 1, KEY_CHUNK),
        key_pos.reshape(chunks, 1, KEY_CHUNK),
        row_owner.reshape(row_total, 1),
    )


def rows_to_columns(x, axis_name):
    count = lax.axis_size(axis_name)
    me = lax.axis_index(axis_name)
    parts = x.reshape(count, x.shape[0] // count, x.shape[1])
    received = [parts[me]]
    for shift in range(1, count):
        outgoing = lax.dynamic_index_in_dim(parts, (me + shift) % count, 0, keepdims=False)
        perm = [(i, (i + shift) % count) for i in range(count)]
        received.append(lax.ppermute(outgoing, axis_name, perm))
    order = (me - jnp.arange(count, dtype=jnp.int32)) % count
    blocks = jnp.stack(received)[order]
    return jnp.transpose(blocks, (1, 0, 2)).reshape(parts.shape[1], count * x.shape[1])


def columns_to_rows(x, axis_name):
    count = lax.axis_size(axis_name)
    me = lax.axis_index(axis_name)
    width = x.shape[1] // count
    received = [lax.dynamic_slice_in_dim(x, me * width, width, 1)]
    for shift in range(1, count):
        outgoing = lax.dynamic_slice_in_dim(x, ((me + shift) % count) * width, width, 1)
        perm = [(i, (i + shift) % count) for i in range(count)]
        received.append(lax.ppermute(outgoing, axis_name, perm))
    order = (me - jnp.arange(count, dtype=jnp.int32)) % count
    return jnp.stack(received)[order].reshape(count * x.shape[0], width)


def shards(
    hidden,
    queries,
    new_keys,
    new_values,
    cache_keys,
    cache_values,
    out_weight,
    attn_gain,
    ple_input,
    ple_gate_weight,
    ple_proj_weight,
    ple_gain,
    page_holder,
    page_slot,
    page_counts,
    last_fill,
    row_counts,
):
    row_total = hidden.shape[0]
    page_total = cache_keys.shape[0]
    page_len = cache_keys.shape[1]
    req_count = lax.axis_size("req")
    tp_index = lax.axis_index("tp")
    local_heads = queries.shape[1] // HD
    kv_head = tp_index // 2
    capacity = max(2, page_total // req_count)
    holders = page_holder[:, 0]
    places = page_slot[:, 0]
    ref_index = jnp.arange(page_total, dtype=jnp.int32)
    earlier = (holders[:, None] == holders[None, :]) & (ref_index[:, None] > ref_index[None, :])
    ranking = jnp.sum(earlier.astype(jnp.int32), axis=1)
    matched = (holders[:, None, None] == jnp.arange(req_count, dtype=jnp.int32)[None, :, None]) & (
        ranking[:, None, None] == jnp.arange(capacity, dtype=jnp.int32)[None, None, :]
    )
    request_table = jnp.sum(jnp.where(matched, places[:, None, None] + 1, 0), axis=0) - 1
    asked = lax.all_to_all(request_table, "req", split_axis=0, concat_axis=0, tiled=True)
    wanted = jnp.maximum(asked, 0)
    tp_count = lax.axis_size("tp")
    half = tp_index % 2
    partner = [(i, i ^ 1) for i in range(tp_count)]
    arrival_index = holders * capacity + ranking

    own_cache = jnp.where(half == 0, cache_keys, cache_values)
    outgoing = lax.dynamic_slice_in_dim(own_cache, kv_head * HD, HD, 2)[wanted]
    arrived = lax.all_to_all(outgoing, "req", split_axis=0, concat_axis=0, tiled=True)
    swapped = lax.ppermute(arrived, "tp", partner)
    attention = sparse_attention(
        queries,
        arrived.reshape(-1, page_len, HD),
        swapped.reshape(-1, page_len, HD),
        arrival_index,
        new_keys,
        new_values,
        half,
        kv_head,
        page_counts[0], last_fill[0], row_counts[0], page_total,
    )
    tp_size = lax.axis_size("tp")
    full_weight = lax.all_gather(out_weight, "tp", axis=0, tiled=True)
    ple_joined = jnp.concatenate([ple_gate_weight, ple_proj_weight.T], axis=1)
    assert ple_joined.shape[1] == hidden.shape[1]
    hidden_parts = hidden.reshape(tp_size, -1, hidden.shape[1])
    gain_rows = jnp.zeros((8, hidden.shape[1]), hidden.dtype).at[0].set(attn_gain).at[1].set(ple_gain)
    with_all = jnp.concatenate(
        [
            hidden_parts,
            jnp.broadcast_to(gain_rows[None], (tp_size, 8, hidden.shape[1])),
            jnp.broadcast_to(ple_joined[None], (tp_size,) + ple_joined.shape),
        ],
        axis=1,
    )
    row_all = rows_to_columns(with_all.reshape(-1, hidden.shape[1]), "tp")
    part_rows = hidden_parts.shape[1]
    row_hidden = row_all[:part_rows]
    full_attn_gain = row_all[part_rows]
    full_ple_gain = row_all[part_rows + 1]
    ple_blocks = row_all[part_rows + 8 :].reshape(ple_joined.shape[0], tp_size, hidden.shape[1])
    ple_blocks = jnp.transpose(ple_blocks, (1, 0, 2)).reshape(-1, hidden.shape[1])
    full_gate_weight = ple_blocks[:, : ple_gate_weight.shape[1]]
    full_proj_weight_t = ple_blocks[:, ple_gate_weight.shape[1] :]
    parts = attention.reshape(tp_size, -1, attention.shape[1])
    width = attention.shape[1]
    projected = jnp.dot(
        parts[tp_index],
        lax.dynamic_slice_in_dim(full_weight, tp_index * width, width, 0),
        preferred_element_type=jnp.float32,
    )
    for shift in range(1, tp_size):
        outgoing = lax.dynamic_index_in_dim(parts, (tp_index + shift) % tp_size, 0, keepdims=False)
        perm = [(i, (i + shift) % tp_size) for i in range(tp_size)]
        piece = lax.ppermute(outgoing, "tp", perm)
        source = (tp_index - shift) % tp_size
        projected = projected + jnp.dot(
            piece,
            lax.dynamic_slice_in_dim(full_weight, source * width, width, 0),
            preferred_element_type=jnp.float32,
        )
    row_ple = lax.dynamic_slice_in_dim(ple_input, tp_index * part_rows, part_rows, 0)
    squares = jnp.sum(projected * projected, axis=1)
    normed = (
        projected
        * lax.rsqrt(squares / D + 1e-06)[:, None]
        * full_attn_gain.astype(jnp.float32)[None, :]
    )
    mixed_state = (row_hidden.astype(jnp.float32) + normed).astype(jnp.bfloat16)
    gate = jnp.dot(mixed_state, full_gate_weight, preferred_element_type=jnp.float32)
    activated = (jax.nn.gelu(gate, approximate=True) * row_ple.astype(jnp.float32)).astype(
        jnp.bfloat16
    )
    lifted = lax.dot_general(
        activated, full_proj_weight_t, (((1,), (1,)), ((), ())), preferred_element_type=jnp.float32
    )
    lift_squares = jnp.sum(lifted * lifted, axis=1)
    lift_normed = (
        lifted
        * lax.rsqrt(lift_squares / D + 1e-06)[:, None]
        * full_ple_gain.astype(jnp.float32)[None, :]
    )
    row_out = (mixed_state.astype(jnp.float32) + lift_normed).astype(jnp.bfloat16)
    return columns_to_rows(row_out, "tp")


def solution(mesh):
    return jax.shard_map(
        shards,
        mesh=mesh,
        in_specs=(
            P("req", "tp"),
            P("req", "tp"),
            P("req", None),
            P("req", None),
            P("req", None, None),
            P("req", None, None),
            P("tp", None),
            P("tp"),
            P("req", None),
            P("tp", None),
            P(None, "tp"),
            P("tp"),
            P("req", None),
            P("req", None),
            P("req", None),
            P("req", None),
            P("req", None),
        ),
        out_specs=P("req", "tp"),
        check_vma=False,
    )
```

```python
import functools
import math

import jax
import jax.numpy as jnp
from jax import lax
from jax.experimental import pallas as pl
from jax.experimental.pallas import tpu as pltpu
from jax.sharding import PartitionSpec as P

D = 2048
HD = 256


def slot_lookup(positions, counts):
    starts = jnp.cumsum(counts) - counts
    owning = jnp.sum((positions[:, None] >= starts[None, :]).astype(jnp.int32), axis=1) - 1
    return (owning, starts)


def table_pick(table, owning):
    onehot = owning[:, None] == jnp.arange(table.shape[0], dtype=jnp.int32)[None, :]
    return jnp.sum(jnp.where(onehot, table[None, :], 0), axis=1)


def attend_masks(counts_of_pages, fill_row, counts_of_rows, page_len, page_total, row_total):
    key_index = jnp.arange(page_total * page_len, dtype=jnp.int32)
    page_ref = key_index // page_len
    within = key_index % page_len
    page_owner, page_starts = slot_lookup(page_ref, counts_of_pages)
    context_len = (counts_of_pages - 1) * page_len + fill_row
    position = (page_ref - table_pick(page_starts, page_owner)) * page_len + within
    valid = position < table_pick(context_len, page_owner)
    row_index = jnp.arange(row_total, dtype=jnp.int32)
    row_owner = slot_lookup(row_index, counts_of_rows)[0]
    context_mask = (row_owner[:, None] == page_owner[None, :]) & valid[None, :]
    causal = (row_owner[:, None] == row_owner[None, :]) & (row_index[None, :] <= row_index[:, None])
    return jnp.concatenate([context_mask, causal], axis=1)


ROW_BLOCK = 64
KEY_CHUNK = 256


def pick(table, index):
    onehot = index[:, None] == jnp.arange(table.shape[0], dtype=jnp.int32)[None, :]
    return jnp.sum(jnp.where(onehot, table[None, :], 0), axis=1)


def attention_kernel(
    scalars_ref,
    q_ref,
    own_ref,
    partner_ref,
    fresh_k_ref,
    fresh_v_ref,
    kinfo_ref,
    rown_ref,
    o_ref,
    s_scr,
    acc_scr,
    *,
    slot_base,
    meta_base,
):
    block = pl.program_id(0)
    ctx_lo = scalars_ref[block * 5]
    ctx_n = scalars_ref[block * 5 + 1]
    new_lo = scalars_ref[block * 5 + 2]
    total = ctx_n + scalars_ref[block * 5 + 3]
    ctx_chunks = scalars_ref[block * 5 + 4]
    keys_are_own = scalars_ref[meta_base] == 0
    heads = q_ref.shape[1] // HD
    page_len = own_ref.shape[1]
    per_chunk = KEY_CHUNK // page_len
    q = q_ref[...]
    stacked = jnp.concatenate([q[:, h * HD:(h + 1) * HD] for h in range(heads)], axis=0)
    row_owner = rown_ref[...]
    row_index = block * ROW_BLOCK + lax.broadcasted_iota(jnp.int32, (ROW_BLOCK, 1), 0)
    scale = 1.0 / math.sqrt(HD)

    def chunk_of(t):
        return jnp.where(t < ctx_n, ctx_lo + t, ctx_chunks + new_lo + t - ctx_n)

    def load_chunk(c, want_keys, fresh_ref):
        pick_own = keys_are_own == want_keys

        def cached():
            pages = []
            for i in range(per_chunk):
                slot = scalars_ref[slot_base + c * per_chunk + i]
                pages.append(jnp.where(pick_own, own_ref[slot], partner_ref[slot]))
            return jnp.concatenate(pages, axis=0)

        def fresh():
            start = pl.multiple_of((c - ctx_chunks) * KEY_CHUNK, KEY_CHUNK)
            return fresh_ref[pl.ds(start, KEY_CHUNK), :]

        return lax.cond(c < ctx_chunks, cached, fresh)

    def scores_pass(t, highest):
        c = chunk_of(t)
        keys = load_chunk(c, True, fresh_k_ref)
        s = lax.dot_general(
            stacked, keys, (((1,), (1,)), ((), ())), preferred_element_type=jnp.float32
        ) * scale
        info = kinfo_ref[c]
        seen = (info[0:1] == row_owner) & (info[1:2] <= row_index)
        s = jnp.where(seen[None], s.reshape(heads, ROW_BLOCK, KEY_CHUNK), -1e30).reshape(
            heads * ROW_BLOCK, KEY_CHUNK
        )
        s_scr[c] = s
        return jnp.maximum(highest, jnp.max(s, axis=1, keepdims=True))

    highest = lax.fori_loop(
        0, total, scores_pass, jnp.full((heads * ROW_BLOCK, 1), -1e30, jnp.float32)
    )

    def exp_pass(t, summed):
        c = chunk_of(t)
        e = jnp.exp(s_scr[c] - highest)
        s_scr[c] = e
        return summed + jnp.sum(e, axis=1, keepdims=True)

    summed = lax.fori_loop(0, total, exp_pass, jnp.zeros((heads * ROW_BLOCK, 1), jnp.float32))
    inverse = 1.0 / summed
    acc_scr[...] = jnp.zeros(acc_scr.shape, jnp.float32)

    def value_pass(t, carry):
        c = chunk_of(t)
        w = (s_scr[c] * inverse).astype(jnp.bfloat16)
        values = load_chunk(c, False, fresh_v_ref)
        acc_scr[...] += jnp.dot(w, values, preferred_element_type=jnp.float32)
        return carry

    lax.fori_loop(0, total, value_pass, 0)
    for h in range(heads):
        o_ref[:, h * HD:(h + 1) * HD] = acc_scr[h * ROW_BLOCK:(h + 1) * ROW_BLOCK, :].astype(
            jnp.bfloat16
        )


def sparse_attention(
    queries, own_pages, partner_pages, slots, new_keys, new_values, half, kv_head,
    page_counts, last_fill, row_counts, page_total,
):
    row_total = queries.shape[0]
    page_len = own_pages.shape[1]
    ctx_total = page_total * page_len
    key_total = ctx_total + row_total
    heads = queries.shape[1] // HD
    blocks = row_total // ROW_BLOCK
    chunks = key_total // KEY_CHUNK
    ctx_chunks = ctx_total // KEY_CHUNK
    key_index = jnp.arange(ctx_total, dtype=jnp.int32)
    page_ref = key_index // page_len
    page_owner, page_starts = slot_lookup(page_ref, page_counts)
    context_len = (page_counts - 1) * page_len + last_fill
    position = (page_ref - table_pick(page_starts, page_owner)) * page_len + key_index % page_len
    valid = position < table_pick(context_len, page_owner)
    row_index = jnp.arange(row_total, dtype=jnp.int32)
    row_owner, row_starts = slot_lookup(row_index, row_counts)
    key_owner = jnp.concatenate([jnp.where(valid, page_owner, -1), row_owner])
    key_pos = jnp.concatenate([jnp.full((ctx_total,), -1, jnp.int32), row_index])
    first = row_owner[::ROW_BLOCK]
    last = row_owner[ROW_BLOCK - 1::ROW_BLOCK]
    ctx_from = pick(page_starts, first) * page_len
    ctx_to = (pick(page_starts, last) + pick(page_counts, last)) * page_len
    ctx_lo = ctx_from // KEY_CHUNK
    ctx_n = (ctx_to + KEY_CHUNK - 1) // KEY_CHUNK - ctx_lo
    new_from = pick(row_starts, first)
    new_to = jnp.arange(1, blocks + 1, dtype=jnp.int32) * ROW_BLOCK
    new_lo = new_from // KEY_CHUNK
    new_n = (new_to + KEY_CHUNK - 1) // KEY_CHUNK - new_lo
    ranges = jnp.stack(
        [ctx_lo, ctx_n, new_lo, new_n, jnp.full((blocks,), ctx_chunks, jnp.int32)], axis=1
    ).astype(jnp.int32)
    meta = jnp.stack([half, kv_head]).astype(jnp.int32)
    slot_base = ranges.size
    meta_base = slot_base + slots.shape[0]
    scalars = jnp.concatenate([ranges.reshape(-1), slots.astype(jnp.int32), meta])
    key_info = jnp.stack(
        [key_owner.reshape(chunks, KEY_CHUNK), key_pos.reshape(chunks, KEY_CHUNK)], axis=1
    )
    whole = lambda b, s: (0, 0, 0)
    by_head = lambda b, s: (0, s[meta_base + 1])
    return pl.pallas_call(
        functools.partial(attention_kernel, slot_base=slot_base, meta_base=meta_base),
        grid_spec=pltpu.PrefetchScalarGridSpec(
            num_scalar_prefetch=1,
            grid=(blocks,),
            in_specs=[
                pl.BlockSpec((ROW_BLOCK, heads * HD), lambda b, s: (b, 0)),
                pl.BlockSpec(own_pages.shape, whole),
                pl.BlockSpec(partner_pages.shape, whole),
                pl.BlockSpec((row_total, HD), by_head),
                pl.BlockSpec((row_total, HD), by_head),
                pl.BlockSpec((chunks, 2, KEY_CHUNK), whole),
                pl.BlockSpec((ROW_BLOCK, 1), lambda b, s: (b, 0)),
            ],
            out_specs=pl.BlockSpec((ROW_BLOCK, heads * HD), lambda b, s: (b, 0)),
            scratch_shapes=[
                pltpu.VMEM((chunks, heads * ROW_BLOCK, KEY_CHUNK), jnp.float32),
                pltpu.VMEM((heads * ROW_BLOCK, HD), jnp.float32),
            ],
        ),
        out_shape=jax.ShapeDtypeStruct((row_total, heads * HD), jnp.bfloat16),
    )(
        scalars,
        queries,
        own_pages,
        partner_pages,
        new_keys,
        new_values,
        key_info,
        row_owner.reshape(row_total, 1),
    )


def rows_to_columns(x, axis_name):
    count = lax.axis_size(axis_name)
    me = lax.axis_index(axis_name)
    parts = x.reshape(count, x.shape[0] // count, x.shape[1])
    received = [parts[me]]
    for shift in range(1, count):
        outgoing = lax.dynamic_index_in_dim(parts, (me + shift) % count, 0, keepdims=False)
        perm = [(i, (i + shift) % count) for i in range(count)]
        received.append(lax.ppermute(outgoing, axis_name, perm))
    order = (me - jnp.arange(count, dtype=jnp.int32)) % count
    blocks = jnp.stack(received)[order]
    return jnp.transpose(blocks, (1, 0, 2)).reshape(parts.shape[1], count * x.shape[1])


def columns_to_rows(x, axis_name):
    count = lax.axis_size(axis_name)
    me = lax.axis_index(axis_name)
    width = x.shape[1] // count
    received = [lax.dynamic_slice_in_dim(x, me * width, width, 1)]
    for shift in range(1, count):
        outgoing = lax.dynamic_slice_in_dim(x, ((me + shift) % count) * width, width, 1)
        perm = [(i, (i + shift) % count) for i in range(count)]
        received.append(lax.ppermute(outgoing, axis_name, perm))
    order = (me - jnp.arange(count, dtype=jnp.int32)) % count
    return jnp.stack(received)[order].reshape(count * x.shape[0], width)


def shards(
    hidden,
    queries,
    new_keys,
    new_values,
    cache_keys,
    cache_values,
    out_weight,
    attn_gain,
    ple_input,
    ple_gate_weight,
    ple_proj_weight,
    ple_gain,
    page_holder,
    page_slot,
    page_counts,
    last_fill,
    row_counts,
):
    row_total = hidden.shape[0]
    page_total = cache_keys.shape[0]
    page_len = cache_keys.shape[1]
    req_count = lax.axis_size("req")
    tp_index = lax.axis_index("tp")
    local_heads = queries.shape[1] // HD
    kv_head = tp_index // 2
    capacity = max(2, page_total // req_count)
    holders = page_holder[:, 0]
    places = page_slot[:, 0]
    ref_index = jnp.arange(page_total, dtype=jnp.int32)
    earlier = (holders[:, None] == holders[None, :]) & (ref_index[:, None] > ref_index[None, :])
    ranking = jnp.sum(earlier.astype(jnp.int32), axis=1)
    matched = (holders[:, None, None] == jnp.arange(req_count, dtype=jnp.int32)[None, :, None]) & (
        ranking[:, None, None] == jnp.arange(capacity, dtype=jnp.int32)[None, None, :]
    )
    request_table = jnp.sum(jnp.where(matched, places[:, None, None] + 1, 0), axis=0) - 1
    asked = lax.all_to_all(request_table, "req", split_axis=0, concat_axis=0, tiled=True)
    wanted = jnp.maximum(asked, 0)
    tp_count = lax.axis_size("tp")
    half = tp_index % 2
    partner = [(i, i ^ 1) for i in range(tp_count)]
    arrival_index = holders * capacity + ranking

    own_cache = jnp.where(half == 0, cache_keys, cache_values)
    outgoing = lax.dynamic_slice_in_dim(own_cache, kv_head * HD, HD, 2)[wanted]
    arrived = lax.all_to_all(outgoing, "req", split_axis=0, concat_axis=0, tiled=True)
    swapped = lax.ppermute(arrived, "tp", partner)
    attention = sparse_attention(
        queries,
        arrived.reshape(-1, page_len, HD),
        swapped.reshape(-1, page_len, HD),
        arrival_index,
        new_keys,
        new_values,
        half,
        kv_head,
        page_counts[0], last_fill[0], row_counts[0], page_total,
    )
    tp_size = lax.axis_size("tp")
    full_weight = lax.all_gather(out_weight, "tp", axis=0, tiled=True)
    ple_joined = lax.all_gather(
        jnp.concatenate([ple_gate_weight, ple_proj_weight.T], axis=1), "tp", axis=0, tiled=True
    )
    full_gate_weight = ple_joined[:, : ple_gate_weight.shape[1]]
    full_proj_weight_t = ple_joined[:, ple_gate_weight.shape[1] :]
    hidden_parts = hidden.reshape(tp_size, -1, hidden.shape[1])
    gain_rows = jnp.zeros((8, hidden.shape[1]), hidden.dtype).at[0].set(attn_gain).at[1].set(ple_gain)
    with_gains = jnp.concatenate(
        [hidden_parts, jnp.broadcast_to(gain_rows[None], (tp_size, 8, hidden.shape[1]))], axis=1
    )
    row_hidden_gains = rows_to_columns(with_gains.reshape(-1, hidden.shape[1]), "tp")
    row_hidden = row_hidden_gains[: hidden_parts.shape[1]]
    full_attn_gain = row_hidden_gains[hidden_parts.shape[1]]
    full_ple_gain = row_hidden_gains[hidden_parts.shape[1] + 1]
    parts = attention.reshape(tp_size, -1, attention.shape[1])
    width = attention.shape[1]
    projected = jnp.dot(
        parts[tp_index],
        lax.dynamic_slice_in_dim(full_weight, tp_index * width, width, 0),
        preferred_element_type=jnp.float32,
    )
    for shift in range(1, tp_size):
        outgoing = lax.dynamic_index_in_dim(parts, (tp_index + shift) % tp_size, 0, keepdims=False)
        perm = [(i, (i + shift) % tp_size) for i in range(tp_size)]
        piece = lax.ppermute(outgoing, "tp", perm)
        source = (tp_index - shift) % tp_size
        projected = projected + jnp.dot(
            piece,
            lax.dynamic_slice_in_dim(full_weight, source * width, width, 0),
            preferred_element_type=jnp.float32,
        )
    part_rows = parts.shape[1]
    row_ple = lax.dynamic_slice_in_dim(ple_input, tp_index * part_rows, part_rows, 0)
    squares = jnp.sum(projected * projected, axis=1)
    normed = (
        projected
        * lax.rsqrt(squares / D + 1e-06)[:, None]
        * full_attn_gain.astype(jnp.float32)[None, :]
    )
    mixed_state = (row_hidden.astype(jnp.float32) + normed).astype(jnp.bfloat16)
    gate = jnp.dot(mixed_state, full_gate_weight, preferred_element_type=jnp.float32)
    activated = (jax.nn.gelu(gate, approximate=True) * row_ple.astype(jnp.float32)).astype(
        jnp.bfloat16
    )
    lifted = lax.dot_general(
        activated, full_proj_weight_t, (((1,), (1,)), ((), ())), preferred_element_type=jnp.float32
    )
    lift_squares = jnp.sum(lifted * lifted, axis=1)
    lift_normed = (
        lifted
        * lax.rsqrt(lift_squares / D + 1e-06)[:, None]
        * full_ple_gain.astype(jnp.float32)[None, :]
    )
    row_out = (mixed_state.astype(jnp.float32) + lift_normed).astype(jnp.bfloat16)
    return columns_to_rows(row_out, "tp")


def solution(mesh):
    return jax.shard_map(
        shards,
        mesh=mesh,
        in_specs=(
            P("req", "tp"),
            P("req", "tp"),
            P("req", None),
            P("req", None),
            P("req", None, None),
            P("req", None, None),
            P("tp", None),
            P("tp"),
            P("req", None),
            P("tp", None),
            P(None, "tp"),
            P("tp"),
            P("req", None),
            P("req", None),
            P("req", None),
            P("req", None),
            P("req", None),
        ),
        out_specs=P("req", "tp"),
        check_vma=False,
    )
```

```python
import functools
import math

import jax
import jax.numpy as jnp
from jax import lax
from jax.experimental import pallas as pl
from jax.experimental.pallas import tpu as pltpu
from jax.sharding import PartitionSpec as P

D = 2048
HD = 256


def slot_lookup(positions, counts):
    starts = jnp.cumsum(counts) - counts
    owning = jnp.sum((positions[:, None] >= starts[None, :]).astype(jnp.int32), axis=1) - 1
    return (owning, starts)


def table_pick(table, owning):
    onehot = owning[:, None] == jnp.arange(table.shape[0], dtype=jnp.int32)[None, :]
    return jnp.sum(jnp.where(onehot, table[None, :], 0), axis=1)


def attend_masks(counts_of_pages, fill_row, counts_of_rows, page_len, page_total, row_total):
    key_index = jnp.arange(page_total * page_len, dtype=jnp.int32)
    page_ref = key_index // page_len
    within = key_index % page_len
    page_owner, page_starts = slot_lookup(page_ref, counts_of_pages)
    context_len = (counts_of_pages - 1) * page_len + fill_row
    position = (page_ref - table_pick(page_starts, page_owner)) * page_len + within
    valid = position < table_pick(context_len, page_owner)
    row_index = jnp.arange(row_total, dtype=jnp.int32)
    row_owner = slot_lookup(row_index, counts_of_rows)[0]
    context_mask = (row_owner[:, None] == page_owner[None, :]) & valid[None, :]
    causal = (row_owner[:, None] == row_owner[None, :]) & (row_index[None, :] <= row_index[:, None])
    return jnp.concatenate([context_mask, causal], axis=1)


ROW_BLOCK = 256
KEY_CHUNK = 512


def pick(table, index):
    onehot = index[:, None] == jnp.arange(table.shape[0], dtype=jnp.int32)[None, :]
    return jnp.sum(jnp.where(onehot, table[None, :], 0), axis=1)


def attention_kernel(
    scalars_ref,
    q_ref,
    own_ref,
    partner_ref,
    fresh_k_ref,
    fresh_v_ref,
    kinfo_ref,
    rown_ref,
    o_ref,
    s_scr,
    acc_scr,
    *,
    slot_base,
    meta_base,
):
    block = pl.program_id(0)
    ctx_lo = scalars_ref[block * 5]
    ctx_n = scalars_ref[block * 5 + 1]
    new_lo = scalars_ref[block * 5 + 2]
    total = ctx_n + scalars_ref[block * 5 + 3]
    ctx_chunks = scalars_ref[block * 5 + 4]
    keys_are_own = scalars_ref[meta_base] == 0
    heads = q_ref.shape[1] // HD
    page_len = own_ref.shape[1]
    per_chunk = KEY_CHUNK // page_len
    q = q_ref[...]
    stacked = jnp.concatenate([q[:, h * HD:(h + 1) * HD] for h in range(heads)], axis=0)
    row_owner = rown_ref[...]
    row_index = block * ROW_BLOCK + lax.broadcasted_iota(jnp.int32, (ROW_BLOCK, 1), 0)
    scale = 1.0 / math.sqrt(HD)

    def chunk_of(t):
        return jnp.where(t < ctx_n, ctx_lo + t, ctx_chunks + new_lo + t - ctx_n)

    def load_chunk(c, want_keys, fresh_ref):
        pick_own = keys_are_own == want_keys

        def cached():
            pages = []
            for i in range(per_chunk):
                slot = scalars_ref[slot_base + c * per_chunk + i]
                pages.append(jnp.where(pick_own, own_ref[slot], partner_ref[slot]))
            return jnp.concatenate(pages, axis=0)

        def fresh():
            start = pl.multiple_of((c - ctx_chunks) * KEY_CHUNK, KEY_CHUNK)
            return fresh_ref[pl.ds(start, KEY_CHUNK), :]

        return lax.cond(c < ctx_chunks, cached, fresh)

    def scores_pass(t, highest):
        c = chunk_of(t)
        keys = load_chunk(c, True, fresh_k_ref)
        s = lax.dot_general(
            stacked, keys, (((1,), (1,)), ((), ())), preferred_element_type=jnp.float32
        ) * scale
        info = kinfo_ref[c]
        seen = (info[0:1] == row_owner) & (info[1:2] <= row_index)
        s = jnp.where(seen[None], s.reshape(heads, ROW_BLOCK, KEY_CHUNK), -1e30).reshape(
            heads * ROW_BLOCK, KEY_CHUNK
        )
        s_scr[c] = s
        return jnp.maximum(highest, jnp.max(s, axis=1, keepdims=True))

    highest = lax.fori_loop(
        0, total, scores_pass, jnp.full((heads * ROW_BLOCK, 1), -1e30, jnp.float32)
    )

    def exp_pass(t, summed):
        c = chunk_of(t)
        e = jnp.exp(s_scr[c] - highest)
        s_scr[c] = e
        return summed + jnp.sum(e, axis=1, keepdims=True)

    summed = lax.fori_loop(0, total, exp_pass, jnp.zeros((heads * ROW_BLOCK, 1), jnp.float32))
    inverse = 1.0 / summed
    acc_scr[...] = jnp.zeros(acc_scr.shape, jnp.float32)

    def value_pass(t, carry):
        c = chunk_of(t)
        w = (s_scr[c] * inverse).astype(jnp.bfloat16)
        values = load_chunk(c, False, fresh_v_ref)
        acc_scr[...] += jnp.dot(w, values, preferred_element_type=jnp.float32)
        return carry

    lax.fori_loop(0, total, value_pass, 0)
    for h in range(heads):
        o_ref[:, h * HD:(h + 1) * HD] = acc_scr[h * ROW_BLOCK:(h + 1) * ROW_BLOCK, :].astype(
            jnp.bfloat16
        )


def sparse_attention(
    queries, own_pages, partner_pages, slots, new_keys, new_values, half, kv_head,
    page_counts, last_fill, row_counts, page_total,
):
    row_total = queries.shape[0]
    page_len = own_pages.shape[1]
    ctx_total = page_total * page_len
    key_total = ctx_total + row_total
    heads = queries.shape[1] // HD
    blocks = row_total // ROW_BLOCK
    chunks = key_total // KEY_CHUNK
    ctx_chunks = ctx_total // KEY_CHUNK
    key_index = jnp.arange(ctx_total, dtype=jnp.int32)
    page_ref = key_index // page_len
    page_owner, page_starts = slot_lookup(page_ref, page_counts)
    context_len = (page_counts - 1) * page_len + last_fill
    position = (page_ref - table_pick(page_starts, page_owner)) * page_len + key_index % page_len
    valid = position < table_pick(context_len, page_owner)
    row_index = jnp.arange(row_total, dtype=jnp.int32)
    row_owner, row_starts = slot_lookup(row_index, row_counts)
    key_owner = jnp.concatenate([jnp.where(valid, page_owner, -1), row_owner])
    key_pos = jnp.concatenate([jnp.full((ctx_total,), -1, jnp.int32), row_index])
    first = row_owner[::ROW_BLOCK]
    last = row_owner[ROW_BLOCK - 1::ROW_BLOCK]
    ctx_from = pick(page_starts, first) * page_len
    ctx_to = (pick(page_starts, last) + pick(page_counts, last)) * page_len
    ctx_lo = ctx_from // KEY_CHUNK
    ctx_n = (ctx_to + KEY_CHUNK - 1) // KEY_CHUNK - ctx_lo
    new_from = pick(row_starts, first)
    new_to = jnp.arange(1, blocks + 1, dtype=jnp.int32) * ROW_BLOCK
    new_lo = new_from // KEY_CHUNK
    new_n = (new_to + KEY_CHUNK - 1) // KEY_CHUNK - new_lo
    ranges = jnp.stack(
        [ctx_lo, ctx_n, new_lo, new_n, jnp.full((blocks,), ctx_chunks, jnp.int32)], axis=1
    ).astype(jnp.int32)
    meta = jnp.stack([half, kv_head]).astype(jnp.int32)
    slot_base = ranges.size
    meta_base = slot_base + slots.shape[0]
    scalars = jnp.concatenate([ranges.reshape(-1), slots.astype(jnp.int32), meta])
    key_info = jnp.stack(
        [key_owner.reshape(chunks, KEY_CHUNK), key_pos.reshape(chunks, KEY_CHUNK)], axis=1
    )
    whole = lambda b, s: (0, 0, 0)
    by_head = lambda b, s: (0, s[meta_base + 1])
    return pl.pallas_call(
        functools.partial(attention_kernel, slot_base=slot_base, meta_base=meta_base),
        grid_spec=pltpu.PrefetchScalarGridSpec(
            num_scalar_prefetch=1,
            grid=(blocks,),
            in_specs=[
                pl.BlockSpec((ROW_BLOCK, heads * HD), lambda b, s: (b, 0)),
                pl.BlockSpec(own_pages.shape, whole),
                pl.BlockSpec(partner_pages.shape, whole),
                pl.BlockSpec((row_total, HD), by_head),
                pl.BlockSpec((row_total, HD), by_head),
                pl.BlockSpec((chunks, 2, KEY_CHUNK), whole),
                pl.BlockSpec((ROW_BLOCK, 1), lambda b, s: (b, 0)),
            ],
            out_specs=pl.BlockSpec((ROW_BLOCK, heads * HD), lambda b, s: (b, 0)),
            scratch_shapes=[
                pltpu.VMEM((chunks, heads * ROW_BLOCK, KEY_CHUNK), jnp.float32),
                pltpu.VMEM((heads * ROW_BLOCK, HD), jnp.float32),
            ],
        ),
        out_shape=jax.ShapeDtypeStruct((row_total, heads * HD), jnp.bfloat16),
    )(
        scalars,
        queries,
        own_pages,
        partner_pages,
        new_keys,
        new_values,
        key_info,
        row_owner.reshape(row_total, 1),
    )


def rows_to_columns(x, axis_name):
    count = lax.axis_size(axis_name)
    me = lax.axis_index(axis_name)
    parts = x.reshape(count, x.shape[0] // count, x.shape[1])
    received = [parts[me]]
    for shift in range(1, count):
        outgoing = lax.dynamic_index_in_dim(parts, (me + shift) % count, 0, keepdims=False)
        perm = [(i, (i + shift) % count) for i in range(count)]
        received.append(lax.ppermute(outgoing, axis_name, perm))
    order = (me - jnp.arange(count, dtype=jnp.int32)) % count
    blocks = jnp.stack(received)[order]
    return jnp.transpose(blocks, (1, 0, 2)).reshape(parts.shape[1], count * x.shape[1])


def columns_to_rows(x, axis_name):
    count = lax.axis_size(axis_name)
    me = lax.axis_index(axis_name)
    width = x.shape[1] // count
    received = [lax.dynamic_slice_in_dim(x, me * width, width, 1)]
    for shift in range(1, count):
        outgoing = lax.dynamic_slice_in_dim(x, ((me + shift) % count) * width, width, 1)
        perm = [(i, (i + shift) % count) for i in range(count)]
        received.append(lax.ppermute(outgoing, axis_name, perm))
    order = (me - jnp.arange(count, dtype=jnp.int32)) % count
    return jnp.stack(received)[order].reshape(count * x.shape[0], width)


def shards(
    hidden,
    queries,
    new_keys,
    new_values,
    cache_keys,
    cache_values,
    out_weight,
    attn_gain,
    ple_input,
    ple_gate_weight,
    ple_proj_weight,
    ple_gain,
    page_holder,
    page_slot,
    page_counts,
    last_fill,
    row_counts,
):
    row_total = hidden.shape[0]
    page_total = cache_keys.shape[0]
    page_len = cache_keys.shape[1]
    req_count = lax.axis_size("req")
    tp_index = lax.axis_index("tp")
    local_heads = queries.shape[1] // HD
    kv_head = tp_index // 2
    capacity = max(2, page_total // req_count)
    holders = page_holder[:, 0]
    places = page_slot[:, 0]
    ref_index = jnp.arange(page_total, dtype=jnp.int32)
    earlier = (holders[:, None] == holders[None, :]) & (ref_index[:, None] > ref_index[None, :])
    ranking = jnp.sum(earlier.astype(jnp.int32), axis=1)
    matched = (holders[:, None, None] == jnp.arange(req_count, dtype=jnp.int32)[None, :, None]) & (
        ranking[:, None, None] == jnp.arange(capacity, dtype=jnp.int32)[None, None, :]
    )
    request_table = jnp.sum(jnp.where(matched, places[:, None, None] + 1, 0), axis=0) - 1
    asked = lax.all_to_all(request_table, "req", split_axis=0, concat_axis=0, tiled=True)
    wanted = jnp.maximum(asked, 0)
    tp_count = lax.axis_size("tp")
    half = tp_index % 2
    partner = [(i, i ^ 1) for i in range(tp_count)]
    arrival_index = holders * capacity + ranking

    own_cache = jnp.where(half == 0, cache_keys, cache_values)
    outgoing = lax.dynamic_slice_in_dim(own_cache, kv_head * HD, HD, 2)[wanted]
    arrived = lax.all_to_all(outgoing, "req", split_axis=0, concat_axis=0, tiled=True)
    swapped = lax.ppermute(arrived, "tp", partner)
    attention = sparse_attention(
        queries,
        arrived.reshape(-1, page_len, HD),
        swapped.reshape(-1, page_len, HD),
        arrival_index,
        new_keys,
        new_values,
        half,
        kv_head,
        page_counts[0], last_fill[0], row_counts[0], page_total,
    )
    tp_size = lax.axis_size("tp")
    full_weight = lax.all_gather(out_weight, "tp", axis=0, tiled=True)
    ple_joined = lax.all_gather(
        jnp.concatenate([ple_gate_weight, ple_proj_weight.T], axis=1), "tp", axis=0, tiled=True
    )
    full_gate_weight = ple_joined[:, : ple_gate_weight.shape[1]]
    full_proj_weight_t = ple_joined[:, ple_gate_weight.shape[1] :]
    hidden_parts = hidden.reshape(tp_size, -1, hidden.shape[1])
    gain_rows = jnp.zeros((8, hidden.shape[1]), hidden.dtype).at[0].set(attn_gain).at[1].set(ple_gain)
    with_gains = jnp.concatenate(
        [hidden_parts, jnp.broadcast_to(gain_rows[None], (tp_size, 8, hidden.shape[1]))], axis=1
    )
    row_hidden_gains = rows_to_columns(with_gains.reshape(-1, hidden.shape[1]), "tp")
    row_hidden = row_hidden_gains[: hidden_parts.shape[1]]
    full_attn_gain = row_hidden_gains[hidden_parts.shape[1]]
    full_ple_gain = row_hidden_gains[hidden_parts.shape[1] + 1]
    parts = attention.reshape(tp_size, -1, attention.shape[1])
    width = attention.shape[1]
    projected = jnp.dot(
        parts[tp_index],
        lax.dynamic_slice_in_dim(full_weight, tp_index * width, width, 0),
        preferred_element_type=jnp.float32,
    )
    for shift in range(1, tp_size):
        outgoing = lax.dynamic_index_in_dim(parts, (tp_index + shift) % tp_size, 0, keepdims=False)
        perm = [(i, (i + shift) % tp_size) for i in range(tp_size)]
        piece = lax.ppermute(outgoing, "tp", perm)
        source = (tp_index - shift) % tp_size
        projected = projected + jnp.dot(
            piece,
            lax.dynamic_slice_in_dim(full_weight, source * width, width, 0),
            preferred_element_type=jnp.float32,
        )
    part_rows = parts.shape[1]
    row_ple = lax.dynamic_slice_in_dim(ple_input, tp_index * part_rows, part_rows, 0)
    squares = jnp.sum(projected * projected, axis=1)
    normed = (
        projected
        * lax.rsqrt(squares / D + 1e-06)[:, None]
        * full_attn_gain.astype(jnp.float32)[None, :]
    )
    mixed_state = (row_hidden.astype(jnp.float32) + normed).astype(jnp.bfloat16)
    gate = jnp.dot(mixed_state, full_gate_weight, preferred_element_type=jnp.float32)
    activated = (jax.nn.gelu(gate, approximate=True) * row_ple.astype(jnp.float32)).astype(
        jnp.bfloat16
    )
    lifted = lax.dot_general(
        activated, full_proj_weight_t, (((1,), (1,)), ((), ())), preferred_element_type=jnp.float32
    )
    lift_squares = jnp.sum(lifted * lifted, axis=1)
    lift_normed = (
        lifted
        * lax.rsqrt(lift_squares / D + 1e-06)[:, None]
        * full_ple_gain.astype(jnp.float32)[None, :]
    )
    row_out = (mixed_state.astype(jnp.float32) + lift_normed).astype(jnp.bfloat16)
    return columns_to_rows(row_out, "tp")


def solution(mesh):
    return jax.shard_map(
        shards,
        mesh=mesh,
        in_specs=(
            P("req", "tp"),
            P("req", "tp"),
            P("req", None),
            P("req", None),
            P("req", None, None),
            P("req", None, None),
            P("tp", None),
            P("tp"),
            P("req", None),
            P("tp", None),
            P(None, "tp"),
            P("tp"),
            P("req", None),
            P("req", None),
            P("req", None),
            P("req", None),
            P("req", None),
        ),
        out_specs=P("req", "tp"),
        check_vma=False,
    )
```

```python
import functools
import math

import jax
import jax.numpy as jnp
from jax import lax
from jax.experimental import pallas as pl
from jax.experimental.pallas import tpu as pltpu
from jax.sharding import PartitionSpec as P

D = 2048
HD = 256


def slot_lookup(positions, counts):
    starts = jnp.cumsum(counts) - counts
    owning = jnp.sum((positions[:, None] >= starts[None, :]).astype(jnp.int32), axis=1) - 1
    return (owning, starts)


def table_pick(table, owning):
    onehot = owning[:, None] == jnp.arange(table.shape[0], dtype=jnp.int32)[None, :]
    return jnp.sum(jnp.where(onehot, table[None, :], 0), axis=1)


def attend_masks(counts_of_pages, fill_row, counts_of_rows, page_len, page_total, row_total):
    key_index = jnp.arange(page_total * page_len, dtype=jnp.int32)
    page_ref = key_index // page_len
    within = key_index % page_len
    page_owner, page_starts = slot_lookup(page_ref, counts_of_pages)
    context_len = (counts_of_pages - 1) * page_len + fill_row
    position = (page_ref - table_pick(page_starts, page_owner)) * page_len + within
    valid = position < table_pick(context_len, page_owner)
    row_index = jnp.arange(row_total, dtype=jnp.int32)
    row_owner = slot_lookup(row_index, counts_of_rows)[0]
    context_mask = (row_owner[:, None] == page_owner[None, :]) & valid[None, :]
    causal = (row_owner[:, None] == row_owner[None, :]) & (row_index[None, :] <= row_index[:, None])
    return jnp.concatenate([context_mask, causal], axis=1)


ROW_BLOCK = 256
KEY_CHUNK = 512


def pick(table, index):
    onehot = index[:, None] == jnp.arange(table.shape[0], dtype=jnp.int32)[None, :]
    return jnp.sum(jnp.where(onehot, table[None, :], 0), axis=1)


def attention_kernel(
    scalars_ref,
    q_ref,
    own_ref,
    partner_ref,
    fresh_k_ref,
    fresh_v_ref,
    kinfo_ref,
    rown_ref,
    o_ref,
    s_scr,
    acc_scr,
    *,
    slot_base,
    meta_base,
):
    block = pl.program_id(0)
    ctx_lo = scalars_ref[block * 5]
    ctx_n = scalars_ref[block * 5 + 1]
    new_lo = scalars_ref[block * 5 + 2]
    total = ctx_n + scalars_ref[block * 5 + 3]
    ctx_chunks = scalars_ref[block * 5 + 4]
    keys_are_own = scalars_ref[meta_base] == 0
    heads = q_ref.shape[1] // HD
    page_len = own_ref.shape[1]
    per_chunk = KEY_CHUNK // page_len
    q = q_ref[...]
    stacked = jnp.concatenate([q[:, h * HD:(h + 1) * HD] for h in range(heads)], axis=0)
    row_owner = rown_ref[...]
    row_index = block * ROW_BLOCK + lax.broadcasted_iota(jnp.int32, (ROW_BLOCK, 1), 0)
    scale = 1.0 / math.sqrt(HD)

    def chunk_of(t):
        return jnp.where(t < ctx_n, ctx_lo + t, ctx_chunks + new_lo + t - ctx_n)

    def load_chunk(c, want_keys, fresh_ref):
        pick_own = keys_are_own == want_keys

        def cached():
            pages = []
            for i in range(per_chunk):
                slot = scalars_ref[slot_base + c * per_chunk + i]
                pages.append(jnp.where(pick_own, own_ref[slot], partner_ref[slot]))
            return jnp.concatenate(pages, axis=0)

        def fresh():
            start = pl.multiple_of((c - ctx_chunks) * KEY_CHUNK, KEY_CHUNK)
            return fresh_ref[pl.ds(start, KEY_CHUNK), :]

        return lax.cond(c < ctx_chunks, cached, fresh)

    def scores_pass(t, highest):
        c = chunk_of(t)
        keys = load_chunk(c, True, fresh_k_ref)
        s = lax.dot_general(
            stacked, keys, (((1,), (1,)), ((), ())), preferred_element_type=jnp.float32
        ) * scale
        info = kinfo_ref[c]
        seen = (info[0:1] == row_owner) & (info[1:2] <= row_index)
        s = jnp.where(seen[None], s.reshape(heads, ROW_BLOCK, KEY_CHUNK), -1e30).reshape(
            heads * ROW_BLOCK, KEY_CHUNK
        )
        s_scr[c] = s
        return jnp.maximum(highest, jnp.max(s, axis=1, keepdims=True))

    highest = lax.fori_loop(
        0, total, scores_pass, jnp.full((heads * ROW_BLOCK, 1), -1e30, jnp.float32)
    )

    def exp_pass(t, summed):
        c = chunk_of(t)
        e = jnp.exp(s_scr[c] - highest)
        s_scr[c] = e
        return summed + jnp.sum(e, axis=1, keepdims=True)

    summed = lax.fori_loop(0, total, exp_pass, jnp.zeros((heads * ROW_BLOCK, 1), jnp.float32))
    inverse = 1.0 / summed
    acc_scr[...] = jnp.zeros(acc_scr.shape, jnp.float32)

    def value_pass(t, carry):
        c = chunk_of(t)
        w = (s_scr[c] * inverse).astype(jnp.bfloat16)
        values = load_chunk(c, False, fresh_v_ref)
        acc_scr[...] += jnp.dot(w, values, preferred_element_type=jnp.float32)
        return carry

    lax.fori_loop(0, total, value_pass, 0)
    for h in range(heads):
        o_ref[:, h * HD:(h + 1) * HD] = acc_scr[h * ROW_BLOCK:(h + 1) * ROW_BLOCK, :].astype(
            jnp.bfloat16
        )


def sparse_attention(
    queries, own_pages, partner_pages, slots, new_keys, new_values, half, kv_head,
    page_counts, last_fill, row_counts, page_total,
):
    row_total = queries.shape[0]
    page_len = own_pages.shape[1]
    ctx_total = page_total * page_len
    key_total = ctx_total + row_total
    heads = queries.shape[1] // HD
    blocks = row_total // ROW_BLOCK
    chunks = key_total // KEY_CHUNK
    ctx_chunks = ctx_total // KEY_CHUNK
    key_index = jnp.arange(ctx_total, dtype=jnp.int32)
    page_ref = key_index // page_len
    page_owner, page_starts = slot_lookup(page_ref, page_counts)
    context_len = (page_counts - 1) * page_len + last_fill
    position = (page_ref - table_pick(page_starts, page_owner)) * page_len + key_index % page_len
    valid = position < table_pick(context_len, page_owner)
    row_index = jnp.arange(row_total, dtype=jnp.int32)
    row_owner, row_starts = slot_lookup(row_index, row_counts)
    key_owner = jnp.concatenate([jnp.where(valid, page_owner, -1), row_owner])
    key_pos = jnp.concatenate([jnp.full((ctx_total,), -1, jnp.int32), row_index])
    first = row_owner[::ROW_BLOCK]
    last = row_owner[ROW_BLOCK - 1::ROW_BLOCK]
    ctx_from = pick(page_starts, first) * page_len
    ctx_to = (pick(page_starts, last) + pick(page_counts, last)) * page_len
    ctx_lo = ctx_from // KEY_CHUNK
    ctx_n = (ctx_to + KEY_CHUNK - 1) // KEY_CHUNK - ctx_lo
    new_from = pick(row_starts, first)
    new_to = jnp.arange(1, blocks + 1, dtype=jnp.int32) * ROW_BLOCK
    new_lo = new_from // KEY_CHUNK
    new_n = (new_to + KEY_CHUNK - 1) // KEY_CHUNK - new_lo
    ranges = jnp.stack(
        [ctx_lo, ctx_n, new_lo, new_n, jnp.full((blocks,), ctx_chunks, jnp.int32)], axis=1
    ).astype(jnp.int32)
    meta = jnp.stack([half, kv_head]).astype(jnp.int32)
    slot_base = ranges.size
    meta_base = slot_base + slots.shape[0]
    scalars = jnp.concatenate([ranges.reshape(-1), slots.astype(jnp.int32), meta])
    key_info = jnp.stack(
        [key_owner.reshape(chunks, KEY_CHUNK), key_pos.reshape(chunks, KEY_CHUNK)], axis=1
    )
    whole = lambda b, s: (0, 0, 0)
    by_head = lambda b, s: (0, s[meta_base + 1])
    return pl.pallas_call(
        functools.partial(attention_kernel, slot_base=slot_base, meta_base=meta_base),
        grid_spec=pltpu.PrefetchScalarGridSpec(
            num_scalar_prefetch=1,
            grid=(blocks,),
            in_specs=[
                pl.BlockSpec((ROW_BLOCK, heads * HD), lambda b, s: (b, 0)),
                pl.BlockSpec(own_pages.shape, whole),
                pl.BlockSpec(partner_pages.shape, whole),
                pl.BlockSpec((row_total, HD), by_head),
                pl.BlockSpec((row_total, HD), by_head),
                pl.BlockSpec((chunks, 2, KEY_CHUNK), whole),
                pl.BlockSpec((ROW_BLOCK, 1), lambda b, s: (b, 0)),
            ],
            out_specs=pl.BlockSpec((ROW_BLOCK, heads * HD), lambda b, s: (b, 0)),
            scratch_shapes=[
                pltpu.VMEM((chunks, heads * ROW_BLOCK, KEY_CHUNK), jnp.float32),
                pltpu.VMEM((heads * ROW_BLOCK, HD), jnp.float32),
            ],
        ),
        out_shape=jax.ShapeDtypeStruct((row_total, heads * HD), jnp.bfloat16),
    )(
        scalars,
        queries,
        own_pages,
        partner_pages,
        new_keys,
        new_values,
        key_info,
        row_owner.reshape(row_total, 1),
    )


def rows_to_columns(x, axis_name):
    count = lax.axis_size(axis_name)
    me = lax.axis_index(axis_name)
    parts = x.reshape(count, x.shape[0] // count, x.shape[1])
    received = [parts[me]]
    for shift in range(1, count):
        outgoing = lax.dynamic_index_in_dim(parts, (me + shift) % count, 0, keepdims=False)
        perm = [(i, (i + shift) % count) for i in range(count)]
        received.append(lax.ppermute(outgoing, axis_name, perm))
    order = (me - jnp.arange(count, dtype=jnp.int32)) % count
    blocks = jnp.stack(received)[order]
    return jnp.transpose(blocks, (1, 0, 2)).reshape(parts.shape[1], count * x.shape[1])


def columns_to_rows(x, axis_name):
    count = lax.axis_size(axis_name)
    me = lax.axis_index(axis_name)
    width = x.shape[1] // count
    received = [lax.dynamic_slice_in_dim(x, me * width, width, 1)]
    for shift in range(1, count):
        outgoing = lax.dynamic_slice_in_dim(x, ((me + shift) % count) * width, width, 1)
        perm = [(i, (i + shift) % count) for i in range(count)]
        received.append(lax.ppermute(outgoing, axis_name, perm))
    order = (me - jnp.arange(count, dtype=jnp.int32)) % count
    return jnp.stack(received)[order].reshape(count * x.shape[0], width)


def shards(
    hidden,
    queries,
    new_keys,
    new_values,
    cache_keys,
    cache_values,
    out_weight,
    attn_gain,
    ple_input,
    ple_gate_weight,
    ple_proj_weight,
    ple_gain,
    page_holder,
    page_slot,
    page_counts,
    last_fill,
    row_counts,
):
    row_total = hidden.shape[0]
    page_total = cache_keys.shape[0]
    page_len = cache_keys.shape[1]
    req_count = lax.axis_size("req")
    tp_index = lax.axis_index("tp")
    local_heads = queries.shape[1] // HD
    kv_head = tp_index // 2
    capacity = max(2, page_total // req_count)
    holders = page_holder[:, 0]
    places = page_slot[:, 0]
    ref_index = jnp.arange(page_total, dtype=jnp.int32)
    earlier = (holders[:, None] == holders[None, :]) & (ref_index[:, None] > ref_index[None, :])
    ranking = jnp.sum(earlier.astype(jnp.int32), axis=1)
    matched = (holders[:, None, None] == jnp.arange(req_count, dtype=jnp.int32)[None, :, None]) & (
        ranking[:, None, None] == jnp.arange(capacity, dtype=jnp.int32)[None, None, :]
    )
    request_table = jnp.sum(jnp.where(matched, places[:, None, None] + 1, 0), axis=0) - 1
    asked = lax.all_to_all(request_table, "req", split_axis=0, concat_axis=0, tiled=True)
    wanted = jnp.maximum(asked, 0)
    tp_count = lax.axis_size("tp")
    half = tp_index % 2
    partner = [(i, i ^ 1) for i in range(tp_count)]
    arrival_index = holders * capacity + ranking

    own_cache = jnp.where(half == 0, cache_keys, cache_values)
    outgoing = lax.dynamic_slice_in_dim(own_cache, kv_head * HD, HD, 2)[wanted]
    arrived = lax.all_to_all(outgoing, "req", split_axis=0, concat_axis=0, tiled=True)
    swapped = lax.ppermute(arrived, "tp", partner)
    attention = sparse_attention(
        queries,
        arrived.reshape(-1, page_len, HD),
        swapped.reshape(-1, page_len, HD),
        arrival_index,
        new_keys,
        new_values,
        half,
        kv_head,
        page_counts[0], last_fill[0], row_counts[0], page_total,
    )
    tp_size = lax.axis_size("tp")
    joined = jnp.concatenate([out_weight, ple_gate_weight, ple_proj_weight.T], axis=1)
    full_joined = lax.all_gather(joined, "tp", axis=0, tiled=True)
    gate_from = out_weight.shape[1]
    proj_from = gate_from + ple_gate_weight.shape[1]
    full_weight = full_joined[:, :gate_from]
    full_gate_weight = full_joined[:, gate_from:proj_from]
    full_proj_weight_t = full_joined[:, proj_from:]
    hidden_parts = hidden.reshape(tp_size, -1, hidden.shape[1])
    gain_rows = jnp.zeros((8, hidden.shape[1]), hidden.dtype).at[0].set(attn_gain).at[1].set(ple_gain)
    with_gains = jnp.concatenate(
        [hidden_parts, jnp.broadcast_to(gain_rows[None], (tp_size, 8, hidden.shape[1]))], axis=1
    )
    row_hidden_gains = rows_to_columns(with_gains.reshape(-1, hidden.shape[1]), "tp")
    row_hidden = row_hidden_gains[: hidden_parts.shape[1]]
    full_attn_gain = row_hidden_gains[hidden_parts.shape[1]]
    full_ple_gain = row_hidden_gains[hidden_parts.shape[1] + 1]
    parts = attention.reshape(tp_size, -1, attention.shape[1])
    width = attention.shape[1]
    projected = jnp.dot(
        parts[tp_index],
        lax.dynamic_slice_in_dim(full_weight, tp_index * width, width, 0),
        preferred_element_type=jnp.float32,
    )
    for shift in range(1, tp_size):
        outgoing = lax.dynamic_index_in_dim(parts, (tp_index + shift) % tp_size, 0, keepdims=False)
        perm = [(i, (i + shift) % tp_size) for i in range(tp_size)]
        piece = lax.ppermute(outgoing, "tp", perm)
        source = (tp_index - shift) % tp_size
        projected = projected + jnp.dot(
            piece,
            lax.dynamic_slice_in_dim(full_weight, source * width, width, 0),
            preferred_element_type=jnp.float32,
        )
    part_rows = parts.shape[1]
    row_ple = lax.dynamic_slice_in_dim(ple_input, tp_index * part_rows, part_rows, 0)
    squares = jnp.sum(projected * projected, axis=1)
    normed = (
        projected
        * lax.rsqrt(squares / D + 1e-06)[:, None]
        * full_attn_gain.astype(jnp.float32)[None, :]
    )
    mixed_state = (row_hidden.astype(jnp.float32) + normed).astype(jnp.bfloat16)
    gate = jnp.dot(mixed_state, full_gate_weight, preferred_element_type=jnp.float32)
    activated = (jax.nn.gelu(gate, approximate=True) * row_ple.astype(jnp.float32)).astype(
        jnp.bfloat16
    )
    lifted = lax.dot_general(
        activated, full_proj_weight_t, (((1,), (1,)), ((), ())), preferred_element_type=jnp.float32
    )
    lift_squares = jnp.sum(lifted * lifted, axis=1)
    lift_normed = (
        lifted
        * lax.rsqrt(lift_squares / D + 1e-06)[:, None]
        * full_ple_gain.astype(jnp.float32)[None, :]
    )
    row_out = (mixed_state.astype(jnp.float32) + lift_normed).astype(jnp.bfloat16)
    return columns_to_rows(row_out, "tp")


def solution(mesh):
    return jax.shard_map(
        shards,
        mesh=mesh,
        in_specs=(
            P("req", "tp"),
            P("req", "tp"),
            P("req", None),
            P("req", None),
            P("req", None, None),
            P("req", None, None),
            P("tp", None),
            P("tp"),
            P("req", None),
            P("tp", None),
            P(None, "tp"),
            P("tp"),
            P("req", None),
            P("req", None),
            P("req", None),
            P("req", None),
            P("req", None),
        ),
        out_specs=P("req", "tp"),
        check_vma=False,
    )
```

```python
import functools
import math

import jax
import jax.numpy as jnp
from jax import lax
from jax.experimental import pallas as pl
from jax.experimental.pallas import tpu as pltpu
from jax.sharding import PartitionSpec as P

D = 2048
HD = 256


def slot_lookup(positions, counts):
    starts = jnp.cumsum(counts) - counts
    owning = jnp.sum((positions[:, None] >= starts[None, :]).astype(jnp.int32), axis=1) - 1
    return (owning, starts)


def table_pick(table, owning):
    onehot = owning[:, None] == jnp.arange(table.shape[0], dtype=jnp.int32)[None, :]
    return jnp.sum(jnp.where(onehot, table[None, :], 0), axis=1)


def attend_masks(counts_of_pages, fill_row, counts_of_rows, page_len, page_total, row_total):
    key_index = jnp.arange(page_total * page_len, dtype=jnp.int32)
    page_ref = key_index // page_len
    within = key_index % page_len
    page_owner, page_starts = slot_lookup(page_ref, counts_of_pages)
    context_len = (counts_of_pages - 1) * page_len + fill_row
    position = (page_ref - table_pick(page_starts, page_owner)) * page_len + within
    valid = position < table_pick(context_len, page_owner)
    row_index = jnp.arange(row_total, dtype=jnp.int32)
    row_owner = slot_lookup(row_index, counts_of_rows)[0]
    context_mask = (row_owner[:, None] == page_owner[None, :]) & valid[None, :]
    causal = (row_owner[:, None] == row_owner[None, :]) & (row_index[None, :] <= row_index[:, None])
    return jnp.concatenate([context_mask, causal], axis=1)


ROW_BLOCK = 256
KEY_CHUNK = 512


def pick(table, index):
    onehot = index[:, None] == jnp.arange(table.shape[0], dtype=jnp.int32)[None, :]
    return jnp.sum(jnp.where(onehot, table[None, :], 0), axis=1)


def attention_kernel(
    scalars_ref,
    q_ref,
    own_ref,
    partner_ref,
    fresh_k_ref,
    fresh_v_ref,
    kinfo_ref,
    rown_ref,
    o_ref,
    s_scr,
    acc_scr,
    *,
    slot_base,
    meta_base,
):
    block = pl.program_id(0)
    ctx_lo = scalars_ref[block * 5]
    ctx_n = scalars_ref[block * 5 + 1]
    new_lo = scalars_ref[block * 5 + 2]
    total = ctx_n + scalars_ref[block * 5 + 3]
    ctx_chunks = scalars_ref[block * 5 + 4]
    keys_are_own = scalars_ref[meta_base] == 0
    heads = q_ref.shape[1] // HD
    page_len = own_ref.shape[1]
    per_chunk = KEY_CHUNK // page_len
    q = q_ref[...]
    stacked = jnp.concatenate([q[:, h * HD:(h + 1) * HD] for h in range(heads)], axis=0)
    row_owner = rown_ref[...]
    row_index = block * ROW_BLOCK + lax.broadcasted_iota(jnp.int32, (ROW_BLOCK, 1), 0)
    scale = 1.0 / math.sqrt(HD)

    def chunk_of(t):
        return jnp.where(t < ctx_n, ctx_lo + t, ctx_chunks + new_lo + t - ctx_n)

    def load_chunk(c, want_keys, fresh_ref):
        pick_own = keys_are_own == want_keys

        def cached():
            pages = []
            for i in range(per_chunk):
                slot = scalars_ref[slot_base + c * per_chunk + i]
                pages.append(jnp.where(pick_own, own_ref[slot], partner_ref[slot]))
            return jnp.concatenate(pages, axis=0)

        def fresh():
            start = pl.multiple_of((c - ctx_chunks) * KEY_CHUNK, KEY_CHUNK)
            return fresh_ref[pl.ds(start, KEY_CHUNK), :]

        return lax.cond(c < ctx_chunks, cached, fresh)

    def scores_pass(t, highest):
        c = chunk_of(t)
        keys = load_chunk(c, True, fresh_k_ref)
        s = lax.dot_general(
            stacked, keys, (((1,), (1,)), ((), ())), preferred_element_type=jnp.float32
        ) * scale
        info = kinfo_ref[c]
        seen = (info[0:1] == row_owner) & (info[1:2] <= row_index)
        s = jnp.where(seen[None], s.reshape(heads, ROW_BLOCK, KEY_CHUNK), -1e30).reshape(
            heads * ROW_BLOCK, KEY_CHUNK
        )
        s_scr[c] = s
        return jnp.maximum(highest, jnp.max(s, axis=1, keepdims=True))

    highest = lax.fori_loop(
        0, total, scores_pass, jnp.full((heads * ROW_BLOCK, 1), -1e30, jnp.float32)
    )

    def exp_pass(t, summed):
        c = chunk_of(t)
        e = jnp.exp(s_scr[c] - highest)
        s_scr[c] = e
        return summed + jnp.sum(e, axis=1, keepdims=True)

    summed = lax.fori_loop(0, total, exp_pass, jnp.zeros((heads * ROW_BLOCK, 1), jnp.float32))
    inverse = 1.0 / summed
    acc_scr[...] = jnp.zeros(acc_scr.shape, jnp.float32)

    def value_pass(t, carry):
        c = chunk_of(t)
        w = (s_scr[c] * inverse).astype(jnp.bfloat16)
        values = load_chunk(c, False, fresh_v_ref)
        acc_scr[...] += jnp.dot(w, values, preferred_element_type=jnp.float32)
        return carry

    lax.fori_loop(0, total, value_pass, 0)
    for h in range(heads):
        o_ref[:, h * HD:(h + 1) * HD] = acc_scr[h * ROW_BLOCK:(h + 1) * ROW_BLOCK, :].astype(
            jnp.bfloat16
        )


def sparse_attention(
    queries, own_pages, partner_pages, slots, new_keys, new_values, half, kv_head,
    page_counts, last_fill, row_counts, page_total,
):
    row_total = queries.shape[0]
    page_len = own_pages.shape[1]
    ctx_total = page_total * page_len
    key_total = ctx_total + row_total
    heads = queries.shape[1] // HD
    blocks = row_total // ROW_BLOCK
    chunks = key_total // KEY_CHUNK
    ctx_chunks = ctx_total // KEY_CHUNK
    key_index = jnp.arange(ctx_total, dtype=jnp.int32)
    page_ref = key_index // page_len
    page_owner, page_starts = slot_lookup(page_ref, page_counts)
    context_len = (page_counts - 1) * page_len + last_fill
    position = (page_ref - table_pick(page_starts, page_owner)) * page_len + key_index % page_len
    valid = position < table_pick(context_len, page_owner)
    row_index = jnp.arange(row_total, dtype=jnp.int32)
    row_owner, row_starts = slot_lookup(row_index, row_counts)
    key_owner = jnp.concatenate([jnp.where(valid, page_owner, -1), row_owner])
    key_pos = jnp.concatenate([jnp.full((ctx_total,), -1, jnp.int32), row_index])
    first = row_owner[::ROW_BLOCK]
    last = row_owner[ROW_BLOCK - 1::ROW_BLOCK]
    ctx_from = pick(page_starts, first) * page_len
    ctx_to = (pick(page_starts, last) + pick(page_counts, last)) * page_len
    ctx_lo = ctx_from // KEY_CHUNK
    ctx_n = (ctx_to + KEY_CHUNK - 1) // KEY_CHUNK - ctx_lo
    new_from = pick(row_starts, first)
    new_to = jnp.arange(1, blocks + 1, dtype=jnp.int32) * ROW_BLOCK
    new_lo = new_from // KEY_CHUNK
    new_n = (new_to + KEY_CHUNK - 1) // KEY_CHUNK - new_lo
    ranges = jnp.stack(
        [ctx_lo, ctx_n, new_lo, new_n, jnp.full((blocks,), ctx_chunks, jnp.int32)], axis=1
    ).astype(jnp.int32)
    meta = jnp.stack([half, kv_head]).astype(jnp.int32)
    slot_base = ranges.size
    meta_base = slot_base + slots.shape[0]
    scalars = jnp.concatenate([ranges.reshape(-1), slots.astype(jnp.int32), meta])
    key_info = jnp.stack(
        [key_owner.reshape(chunks, KEY_CHUNK), key_pos.reshape(chunks, KEY_CHUNK)], axis=1
    )
    whole = lambda b, s: (0, 0, 0)
    by_head = lambda b, s: (0, s[meta_base + 1])
    return pl.pallas_call(
        functools.partial(attention_kernel, slot_base=slot_base, meta_base=meta_base),
        grid_spec=pltpu.PrefetchScalarGridSpec(
            num_scalar_prefetch=1,
            grid=(blocks,),
            in_specs=[
                pl.BlockSpec((ROW_BLOCK, heads * HD), lambda b, s: (b, 0)),
                pl.BlockSpec(own_pages.shape, whole),
                pl.BlockSpec(partner_pages.shape, whole),
                pl.BlockSpec((row_total, HD), by_head),
                pl.BlockSpec((row_total, HD), by_head),
                pl.BlockSpec((chunks, 2, KEY_CHUNK), whole),
                pl.BlockSpec((ROW_BLOCK, 1), lambda b, s: (b, 0)),
            ],
            out_specs=pl.BlockSpec((ROW_BLOCK, heads * HD), lambda b, s: (b, 0)),
            scratch_shapes=[
                pltpu.VMEM((chunks, heads * ROW_BLOCK, KEY_CHUNK), jnp.float32),
                pltpu.VMEM((heads * ROW_BLOCK, HD), jnp.float32),
            ],
        ),
        out_shape=jax.ShapeDtypeStruct((row_total, heads * HD), jnp.bfloat16),
    )(
        scalars,
        queries,
        own_pages,
        partner_pages,
        new_keys,
        new_values,
        key_info,
        row_owner.reshape(row_total, 1),
    )


def rows_to_columns(x, axis_name):
    count = lax.axis_size(axis_name)
    me = lax.axis_index(axis_name)
    parts = x.reshape(count, x.shape[0] // count, x.shape[1])
    received = [parts[me]]
    for shift in range(1, count):
        outgoing = lax.dynamic_index_in_dim(parts, (me + shift) % count, 0, keepdims=False)
        perm = [(i, (i + shift) % count) for i in range(count)]
        received.append(lax.ppermute(outgoing, axis_name, perm))
    order = (me - jnp.arange(count, dtype=jnp.int32)) % count
    blocks = jnp.stack(received)[order]
    return jnp.transpose(blocks, (1, 0, 2)).reshape(parts.shape[1], count * x.shape[1])


def columns_to_rows(x, axis_name):
    count = lax.axis_size(axis_name)
    me = lax.axis_index(axis_name)
    width = x.shape[1] // count
    received = [lax.dynamic_slice_in_dim(x, me * width, width, 1)]
    for shift in range(1, count):
        outgoing = lax.dynamic_slice_in_dim(x, ((me + shift) % count) * width, width, 1)
        perm = [(i, (i + shift) % count) for i in range(count)]
        received.append(lax.ppermute(outgoing, axis_name, perm))
    order = (me - jnp.arange(count, dtype=jnp.int32)) % count
    return jnp.stack(received)[order].reshape(count * x.shape[0], width)


def shards(
    hidden,
    queries,
    new_keys,
    new_values,
    cache_keys,
    cache_values,
    out_weight,
    attn_gain,
    ple_input,
    ple_gate_weight,
    ple_proj_weight,
    ple_gain,
    page_holder,
    page_slot,
    page_counts,
    last_fill,
    row_counts,
):
    row_total = hidden.shape[0]
    page_total = cache_keys.shape[0]
    page_len = cache_keys.shape[1]
    req_count = lax.axis_size("req")
    tp_index = lax.axis_index("tp")
    local_heads = queries.shape[1] // HD
    kv_head = tp_index // 2
    capacity = max(2, page_total // req_count)
    holders = page_holder[:, 0]
    places = page_slot[:, 0]
    ref_index = jnp.arange(page_total, dtype=jnp.int32)
    earlier = (holders[:, None] == holders[None, :]) & (ref_index[:, None] > ref_index[None, :])
    ranking = jnp.sum(earlier.astype(jnp.int32), axis=1)
    matched = (holders[:, None, None] == jnp.arange(req_count, dtype=jnp.int32)[None, :, None]) & (
        ranking[:, None, None] == jnp.arange(capacity, dtype=jnp.int32)[None, None, :]
    )
    request_table = jnp.sum(jnp.where(matched, places[:, None, None] + 1, 0), axis=0) - 1
    asked = lax.all_to_all(request_table, "req", split_axis=0, concat_axis=0, tiled=True)
    wanted = jnp.maximum(asked, 0)
    tp_count = lax.axis_size("tp")
    half = tp_index % 2
    partner = [(i, i ^ 1) for i in range(tp_count)]
    arrival_index = holders * capacity + ranking

    own_cache = jnp.where(half == 0, cache_keys, cache_values)
    outgoing = lax.dynamic_slice_in_dim(own_cache, kv_head * HD, HD, 2)[wanted]
    arrived = lax.all_to_all(outgoing, "req", split_axis=0, concat_axis=0, tiled=True)
    swapped = lax.ppermute(arrived, "tp", partner)
    attention = sparse_attention(
        queries,
        arrived.reshape(-1, page_len, HD),
        swapped.reshape(-1, page_len, HD),
        arrival_index,
        new_keys,
        new_values,
        half,
        kv_head,
        page_counts[0], last_fill[0], row_counts[0], page_total,
    )
    tp_size = lax.axis_size("tp")
    full_weight = lax.all_gather(out_weight, "tp", axis=0, tiled=True)
    ple_joined = lax.all_gather(
        jnp.concatenate([ple_gate_weight, ple_proj_weight.T], axis=1), "tp", axis=0, tiled=True
    )
    full_gate_weight = ple_joined[:, : ple_gate_weight.shape[1]]
    full_proj_weight_t = ple_joined[:, ple_gate_weight.shape[1] :]
    hidden_parts = hidden.reshape(tp_size, -1, hidden.shape[1])
    gain_rows = jnp.zeros((8, hidden.shape[1]), hidden.dtype).at[0].set(attn_gain).at[1].set(ple_gain)
    with_gains = jnp.concatenate(
        [hidden_parts, jnp.broadcast_to(gain_rows[None], (tp_size, 8, hidden.shape[1]))], axis=1
    )
    row_hidden_gains = rows_to_columns(with_gains.reshape(-1, hidden.shape[1]), "tp")
    row_hidden = row_hidden_gains[: hidden_parts.shape[1]]
    full_attn_gain = row_hidden_gains[hidden_parts.shape[1]]
    full_ple_gain = row_hidden_gains[hidden_parts.shape[1] + 1]
    parts = attention.reshape(tp_size, -1, attention.shape[1])
    width = attention.shape[1]
    projected = jnp.dot(
        parts[tp_index],
        lax.dynamic_slice_in_dim(full_weight, tp_index * width, width, 0),
        preferred_element_type=jnp.float32,
    )
    for shift in range(1, tp_size):
        outgoing = lax.dynamic_index_in_dim(parts, (tp_index + shift) % tp_size, 0, keepdims=False)
        perm = [(i, (i + shift) % tp_size) for i in range(tp_size)]
        piece = lax.ppermute(outgoing, "tp", perm)
        source = (tp_index - shift) % tp_size
        projected = projected + jnp.dot(
            piece,
            lax.dynamic_slice_in_dim(full_weight, source * width, width, 0),
            preferred_element_type=jnp.float32,
        )
    part_rows = parts.shape[1]
    row_ple = lax.dynamic_slice_in_dim(ple_input, tp_index * part_rows, part_rows, 0)
    squares = jnp.sum(projected * projected, axis=1)
    normed = (
        projected
        * lax.rsqrt(squares / D + 1e-06)[:, None]
        * full_attn_gain.astype(jnp.float32)[None, :]
    )
    mixed_state = (row_hidden.astype(jnp.float32) + normed).astype(jnp.bfloat16)
    gate = jnp.dot(
        lax.dynamic_slice_in_dim(mixed_state, tp_index * width, width, 1),
        ple_gate_weight,
        preferred_element_type=jnp.float32,
    )
    for shift in range(1, tp_size):
        source = (tp_index - shift) % tp_size
        gate = gate + jnp.dot(
            lax.dynamic_slice_in_dim(mixed_state, source * width, width, 1),
            lax.dynamic_slice_in_dim(full_gate_weight, source * width, width, 0),
            preferred_element_type=jnp.float32,
        )
    activated = (jax.nn.gelu(gate, approximate=True) * row_ple.astype(jnp.float32)).astype(
        jnp.bfloat16
    )
    lifted = lax.dot_general(
        activated, full_proj_weight_t, (((1,), (1,)), ((), ())), preferred_element_type=jnp.float32
    )
    lift_squares = jnp.sum(lifted * lifted, axis=1)
    lift_normed = (
        lifted
        * lax.rsqrt(lift_squares / D + 1e-06)[:, None]
        * full_ple_gain.astype(jnp.float32)[None, :]
    )
    row_out = (mixed_state.astype(jnp.float32) + lift_normed).astype(jnp.bfloat16)
    return columns_to_rows(row_out, "tp")


def solution(mesh):
    return jax.shard_map(
        shards,
        mesh=mesh,
        in_specs=(
            P("req", "tp"),
            P("req", "tp"),
            P("req", None),
            P("req", None),
            P("req", None, None),
            P("req", None, None),
            P("tp", None),
            P("tp"),
            P("req", None),
            P("tp", None),
            P(None, "tp"),
            P("tp"),
            P("req", None),
            P("req", None),
            P("req", None),
            P("req", None),
            P("req", None),
        ),
        out_specs=P("req", "tp"),
        check_vma=False,
    )
```

```python
import functools
import math

import jax
import jax.numpy as jnp
from jax import lax
from jax.experimental import pallas as pl
from jax.experimental.pallas import tpu as pltpu
from jax.sharding import PartitionSpec as P

D = 2048
HD = 256


def slot_lookup(positions, counts):
    starts = jnp.cumsum(counts) - counts
    owning = jnp.sum((positions[:, None] >= starts[None, :]).astype(jnp.int32), axis=1) - 1
    return (owning, starts)


def table_pick(table, owning):
    onehot = owning[:, None] == jnp.arange(table.shape[0], dtype=jnp.int32)[None, :]
    return jnp.sum(jnp.where(onehot, table[None, :], 0), axis=1)


def attend_masks(counts_of_pages, fill_row, counts_of_rows, page_len, page_total, row_total):
    key_index = jnp.arange(page_total * page_len, dtype=jnp.int32)
    page_ref = key_index // page_len
    within = key_index % page_len
    page_owner, page_starts = slot_lookup(page_ref, counts_of_pages)
    context_len = (counts_of_pages - 1) * page_len + fill_row
    position = (page_ref - table_pick(page_starts, page_owner)) * page_len + within
    valid = position < table_pick(context_len, page_owner)
    row_index = jnp.arange(row_total, dtype=jnp.int32)
    row_owner = slot_lookup(row_index, counts_of_rows)[0]
    context_mask = (row_owner[:, None] == page_owner[None, :]) & valid[None, :]
    causal = (row_owner[:, None] == row_owner[None, :]) & (row_index[None, :] <= row_index[:, None])
    return jnp.concatenate([context_mask, causal], axis=1)


ROW_BLOCK = 256
KEY_CHUNK = 512


def pick(table, index):
    onehot = index[:, None] == jnp.arange(table.shape[0], dtype=jnp.int32)[None, :]
    return jnp.sum(jnp.where(onehot, table[None, :], 0), axis=1)


def attention_kernel(
    scalars_ref,
    q_ref,
    own_ref,
    partner_ref,
    fresh_k_ref,
    fresh_v_ref,
    o_ref,
    s_scr,
    acc_scr,
    *,
    slot_base,
    meta_base,
    request_base,
    requests,
    ctx_total,
):
    block = pl.program_id(0)
    ctx_lo = scalars_ref[block * 5]
    ctx_n = scalars_ref[block * 5 + 1]
    new_lo = scalars_ref[block * 5 + 2]
    total = ctx_n + scalars_ref[block * 5 + 3]
    ctx_chunks = scalars_ref[block * 5 + 4]
    keys_are_own = scalars_ref[meta_base] == 0
    heads = q_ref.shape[1] // HD
    page_len = own_ref.shape[1]
    per_chunk = KEY_CHUNK // page_len
    q = q_ref[...]
    stacked = jnp.concatenate([q[:, h * HD:(h + 1) * HD] for h in range(heads)], axis=0)
    row_index = block * ROW_BLOCK + lax.broadcasted_iota(jnp.int32, (ROW_BLOCK, 1), 0)
    row_owner = jnp.full((ROW_BLOCK, 1), -1, jnp.int32)
    for s in range(requests):
        lo = scalars_ref[request_base + 4 * s + 2]
        hi = lo + scalars_ref[request_base + 4 * s + 3]
        row_owner = jnp.where((row_index >= lo) & (row_index < hi), s, row_owner)
    scale = 1.0 / math.sqrt(HD)

    def chunk_of(t):
        return jnp.where(t < ctx_n, ctx_lo + t, ctx_chunks + new_lo + t - ctx_n)

    def load_chunk(c, want_keys, fresh_ref):
        pick_own = keys_are_own == want_keys

        def cached():
            pages = []
            for i in range(per_chunk):
                slot = scalars_ref[slot_base + c * per_chunk + i]
                pages.append(jnp.where(pick_own, own_ref[slot], partner_ref[slot]))
            return jnp.concatenate(pages, axis=0)

        def fresh():
            start = pl.multiple_of((c - ctx_chunks) * KEY_CHUNK, KEY_CHUNK)
            return fresh_ref[pl.ds(start, KEY_CHUNK), :]

        return lax.cond(c < ctx_chunks, cached, fresh)

    def scores_pass(t, highest):
        c = chunk_of(t)
        keys = load_chunk(c, True, fresh_k_ref)
        s = lax.dot_general(
            stacked, keys, (((1,), (1,)), ((), ())), preferred_element_type=jnp.float32
        ) * scale
        key_index = c * KEY_CHUNK + lax.broadcasted_iota(jnp.int32, (1, KEY_CHUNK), 1)
        key_owner = jnp.full((1, KEY_CHUNK), -1, jnp.int32)
        for r in range(requests):
            ctx_lo_s = scalars_ref[request_base + 4 * r]
            ctx_hi_s = ctx_lo_s + scalars_ref[request_base + 4 * r + 1]
            new_lo_s = ctx_total + scalars_ref[request_base + 4 * r + 2]
            new_hi_s = new_lo_s + scalars_ref[request_base + 4 * r + 3]
            inside = ((key_index >= ctx_lo_s) & (key_index < ctx_hi_s)) | (
                (key_index >= new_lo_s) & (key_index < new_hi_s)
            )
            key_owner = jnp.where(inside, r, key_owner)
        key_pos = jnp.where(key_index >= ctx_total, key_index - ctx_total, -1)
        seen = (key_owner == row_owner) & (key_pos <= row_index)
        s = jnp.where(seen[None], s.reshape(heads, ROW_BLOCK, KEY_CHUNK), -1e30).reshape(
            heads * ROW_BLOCK, KEY_CHUNK
        )
        s_scr[c] = s
        return jnp.maximum(highest, jnp.max(s, axis=1, keepdims=True))

    highest = lax.fori_loop(
        0, total, scores_pass, jnp.full((heads * ROW_BLOCK, 1), -1e30, jnp.float32)
    )

    def exp_pass(t, summed):
        c = chunk_of(t)
        e = jnp.exp(s_scr[c] - highest)
        s_scr[c] = e
        return summed + jnp.sum(e, axis=1, keepdims=True)

    summed = lax.fori_loop(0, total, exp_pass, jnp.zeros((heads * ROW_BLOCK, 1), jnp.float32))
    inverse = 1.0 / summed
    acc_scr[...] = jnp.zeros(acc_scr.shape, jnp.float32)

    def value_pass(t, carry):
        c = chunk_of(t)
        w = (s_scr[c] * inverse).astype(jnp.bfloat16)
        values = load_chunk(c, False, fresh_v_ref)
        acc_scr[...] += jnp.dot(w, values, preferred_element_type=jnp.float32)
        return carry

    lax.fori_loop(0, total, value_pass, 0)
    for h in range(heads):
        o_ref[:, h * HD:(h + 1) * HD] = acc_scr[h * ROW_BLOCK:(h + 1) * ROW_BLOCK, :].astype(
            jnp.bfloat16
        )


def sparse_attention(
    queries, own_pages, partner_pages, slots, new_keys, new_values, half, kv_head,
    page_counts, last_fill, row_counts, page_total,
):
    row_total = queries.shape[0]
    page_len = own_pages.shape[1]
    ctx_total = page_total * page_len
    key_total = ctx_total + row_total
    heads = queries.shape[1] // HD
    blocks = row_total // ROW_BLOCK
    chunks = key_total // KEY_CHUNK
    ctx_chunks = ctx_total // KEY_CHUNK
    key_index = jnp.arange(ctx_total, dtype=jnp.int32)
    page_ref = key_index // page_len
    page_owner, page_starts = slot_lookup(page_ref, page_counts)
    context_len = (page_counts - 1) * page_len + last_fill
    position = (page_ref - table_pick(page_starts, page_owner)) * page_len + key_index % page_len
    valid = position < table_pick(context_len, page_owner)
    row_index = jnp.arange(row_total, dtype=jnp.int32)
    row_owner, row_starts = slot_lookup(row_index, row_counts)
    key_owner = jnp.concatenate([jnp.where(valid, page_owner, -1), row_owner])
    key_pos = jnp.concatenate([jnp.full((ctx_total,), -1, jnp.int32), row_index])
    first = row_owner[::ROW_BLOCK]
    last = row_owner[ROW_BLOCK - 1::ROW_BLOCK]
    ctx_from = pick(page_starts, first) * page_len
    ctx_to = (pick(page_starts, last) + pick(page_counts, last)) * page_len
    ctx_lo = ctx_from // KEY_CHUNK
    ctx_n = (ctx_to + KEY_CHUNK - 1) // KEY_CHUNK - ctx_lo
    new_from = pick(row_starts, first)
    new_to = jnp.arange(1, blocks + 1, dtype=jnp.int32) * ROW_BLOCK
    new_lo = new_from // KEY_CHUNK
    new_n = (new_to + KEY_CHUNK - 1) // KEY_CHUNK - new_lo
    ranges = jnp.stack(
        [ctx_lo, ctx_n, new_lo, new_n, jnp.full((blocks,), ctx_chunks, jnp.int32)], axis=1
    ).astype(jnp.int32)
    meta = jnp.stack([half, kv_head]).astype(jnp.int32)
    slot_base = ranges.size
    meta_base = slot_base + slots.shape[0]
    request_base = meta_base + meta.shape[0]
    per_request = jnp.stack(
        [page_starts * page_len, context_len, row_starts, row_counts], axis=1
    ).astype(jnp.int32)
    scalars = jnp.concatenate(
        [ranges.reshape(-1), slots.astype(jnp.int32), meta, per_request.reshape(-1)]
    )
    key_info = jnp.stack(
        [key_owner.reshape(chunks, KEY_CHUNK), key_pos.reshape(chunks, KEY_CHUNK)], axis=1
    )
    whole = lambda b, s: (0, 0, 0)
    by_head = lambda b, s: (0, s[meta_base + 1])
    return pl.pallas_call(
        functools.partial(
            attention_kernel,
            slot_base=slot_base,
            meta_base=meta_base,
            request_base=request_base,
            requests=row_counts.shape[0],
            ctx_total=ctx_total,
        ),
        grid_spec=pltpu.PrefetchScalarGridSpec(
            num_scalar_prefetch=1,
            grid=(blocks,),
            in_specs=[
                pl.BlockSpec((ROW_BLOCK, heads * HD), lambda b, s: (b, 0)),
                pl.BlockSpec(own_pages.shape, whole),
                pl.BlockSpec(partner_pages.shape, whole),
                pl.BlockSpec((row_total, HD), by_head),
                pl.BlockSpec((row_total, HD), by_head),
            ],
            out_specs=pl.BlockSpec((ROW_BLOCK, heads * HD), lambda b, s: (b, 0)),
            scratch_shapes=[
                pltpu.VMEM((chunks, heads * ROW_BLOCK, KEY_CHUNK), jnp.float32),
                pltpu.VMEM((heads * ROW_BLOCK, HD), jnp.float32),
            ],
        ),
        out_shape=jax.ShapeDtypeStruct((row_total, heads * HD), jnp.bfloat16),
    )(
        scalars,
        queries,
        own_pages,
        partner_pages,
        new_keys,
        new_values,
    )


def rows_to_columns(x, axis_name):
    count = lax.axis_size(axis_name)
    me = lax.axis_index(axis_name)
    parts = x.reshape(count, x.shape[0] // count, x.shape[1])
    received = [parts[me]]
    for shift in range(1, count):
        outgoing = lax.dynamic_index_in_dim(parts, (me + shift) % count, 0, keepdims=False)
        perm = [(i, (i + shift) % count) for i in range(count)]
        received.append(lax.ppermute(outgoing, axis_name, perm))
    order = (me - jnp.arange(count, dtype=jnp.int32)) % count
    blocks = jnp.stack(received)[order]
    return jnp.transpose(blocks, (1, 0, 2)).reshape(parts.shape[1], count * x.shape[1])


def columns_to_rows(x, axis_name):
    count = lax.axis_size(axis_name)
    me = lax.axis_index(axis_name)
    width = x.shape[1] // count
    received = [lax.dynamic_slice_in_dim(x, me * width, width, 1)]
    for shift in range(1, count):
        outgoing = lax.dynamic_slice_in_dim(x, ((me + shift) % count) * width, width, 1)
        perm = [(i, (i + shift) % count) for i in range(count)]
        received.append(lax.ppermute(outgoing, axis_name, perm))
    order = (me - jnp.arange(count, dtype=jnp.int32)) % count
    return jnp.stack(received)[order].reshape(count * x.shape[0], width)


def shards(
    hidden,
    queries,
    new_keys,
    new_values,
    cache_keys,
    cache_values,
    out_weight,
    attn_gain,
    ple_input,
    ple_gate_weight,
    ple_proj_weight,
    ple_gain,
    page_holder,
    page_slot,
    page_counts,
    last_fill,
    row_counts,
):
    row_total = hidden.shape[0]
    page_total = cache_keys.shape[0]
    page_len = cache_keys.shape[1]
    req_count = lax.axis_size("req")
    tp_index = lax.axis_index("tp")
    local_heads = queries.shape[1] // HD
    kv_head = tp_index // 2
    capacity = max(2, page_total // req_count)
    holders = page_holder[:, 0]
    places = page_slot[:, 0]
    ref_index = jnp.arange(page_total, dtype=jnp.int32)
    earlier = (holders[:, None] == holders[None, :]) & (ref_index[:, None] > ref_index[None, :])
    ranking = jnp.sum(earlier.astype(jnp.int32), axis=1)
    matched = (holders[:, None, None] == jnp.arange(req_count, dtype=jnp.int32)[None, :, None]) & (
        ranking[:, None, None] == jnp.arange(capacity, dtype=jnp.int32)[None, None, :]
    )
    request_table = jnp.sum(jnp.where(matched, places[:, None, None] + 1, 0), axis=0) - 1
    asked = lax.all_to_all(request_table, "req", split_axis=0, concat_axis=0, tiled=True)
    wanted = jnp.maximum(asked, 0)
    tp_count = lax.axis_size("tp")
    half = tp_index % 2
    partner = [(i, i ^ 1) for i in range(tp_count)]
    arrival_index = holders * capacity + ranking

    own_cache = jnp.where(half == 0, cache_keys, cache_values)
    outgoing = lax.dynamic_slice_in_dim(own_cache, kv_head * HD, HD, 2)[wanted]
    arrived = lax.all_to_all(outgoing, "req", split_axis=0, concat_axis=0, tiled=True)
    swapped = lax.ppermute(arrived, "tp", partner)
    attention = sparse_attention(
        queries,
        arrived.reshape(-1, page_len, HD),
        swapped.reshape(-1, page_len, HD),
        arrival_index,
        new_keys,
        new_values,
        half,
        kv_head,
        page_counts[0], last_fill[0], row_counts[0], page_total,
    )
    tp_size = lax.axis_size("tp")
    full_weight = lax.all_gather(out_weight, "tp", axis=0, tiled=True)
    ple_joined = lax.all_gather(
        jnp.concatenate([ple_gate_weight, ple_proj_weight.T], axis=1), "tp", axis=0, tiled=True
    )
    full_gate_weight = ple_joined[:, : ple_gate_weight.shape[1]]
    full_proj_weight_t = ple_joined[:, ple_gate_weight.shape[1] :]
    hidden_parts = hidden.reshape(tp_size, -1, hidden.shape[1])
    gain_rows = jnp.zeros((8, hidden.shape[1]), hidden.dtype).at[0].set(attn_gain).at[1].set(ple_gain)
    with_gains = jnp.concatenate(
        [hidden_parts, jnp.broadcast_to(gain_rows[None], (tp_size, 8, hidden.shape[1]))], axis=1
    )
    row_hidden_gains = rows_to_columns(with_gains.reshape(-1, hidden.shape[1]), "tp")
    row_hidden = row_hidden_gains[: hidden_parts.shape[1]]
    full_attn_gain = row_hidden_gains[hidden_parts.shape[1]]
    full_ple_gain = row_hidden_gains[hidden_parts.shape[1] + 1]
    parts = attention.reshape(tp_size, -1, attention.shape[1])
    width = attention.shape[1]
    projected = jnp.dot(
        parts[tp_index],
        lax.dynamic_slice_in_dim(full_weight, tp_index * width, width, 0),
        preferred_element_type=jnp.float32,
    )
    for shift in range(1, tp_size):
        outgoing = lax.dynamic_index_in_dim(parts, (tp_index + shift) % tp_size, 0, keepdims=False)
        perm = [(i, (i + shift) % tp_size) for i in range(tp_size)]
        piece = lax.ppermute(outgoing, "tp", perm)
        source = (tp_index - shift) % tp_size
        projected = projected + jnp.dot(
            piece,
            lax.dynamic_slice_in_dim(full_weight, source * width, width, 0),
            preferred_element_type=jnp.float32,
        )
    part_rows = parts.shape[1]
    row_ple = lax.dynamic_slice_in_dim(ple_input, tp_index * part_rows, part_rows, 0)
    squares = jnp.sum(projected * projected, axis=1)
    normed = (
        projected
        * lax.rsqrt(squares / D + 1e-06)[:, None]
        * full_attn_gain.astype(jnp.float32)[None, :]
    )
    mixed_state = (row_hidden.astype(jnp.float32) + normed).astype(jnp.bfloat16)
    gate = jnp.dot(mixed_state, full_gate_weight, preferred_element_type=jnp.float32)
    activated = (jax.nn.gelu(gate, approximate=True) * row_ple.astype(jnp.float32)).astype(
        jnp.bfloat16
    )
    lifted = lax.dot_general(
        activated, full_proj_weight_t, (((1,), (1,)), ((), ())), preferred_element_type=jnp.float32
    )
    lift_squares = jnp.sum(lifted * lifted, axis=1)
    lift_normed = (
        lifted
        * lax.rsqrt(lift_squares / D + 1e-06)[:, None]
        * full_ple_gain.astype(jnp.float32)[None, :]
    )
    row_out = (mixed_state.astype(jnp.float32) + lift_normed).astype(jnp.bfloat16)
    return columns_to_rows(row_out, "tp")


def solution(mesh):
    return jax.shard_map(
        shards,
        mesh=mesh,
        in_specs=(
            P("req", "tp"),
            P("req", "tp"),
            P("req", None),
            P("req", None),
            P("req", None, None),
            P("req", None, None),
            P("tp", None),
            P("tp"),
            P("req", None),
            P("tp", None),
            P(None, "tp"),
            P("tp"),
            P("req", None),
            P("req", None),
            P("req", None),
            P("req", None),
            P("req", None),
        ),
        out_specs=P("req", "tp"),
        check_vma=False,
    )
```

```python
import functools
import math

import jax
import jax.numpy as jnp
from jax import lax
from jax.experimental import pallas as pl
from jax.experimental.pallas import tpu as pltpu
from jax.sharding import PartitionSpec as P

D = 2048
HD = 256


def slot_lookup(positions, counts):
    starts = jnp.cumsum(counts) - counts
    owning = jnp.sum((positions[:, None] >= starts[None, :]).astype(jnp.int32), axis=1) - 1
    return (owning, starts)


def table_pick(table, owning):
    onehot = owning[:, None] == jnp.arange(table.shape[0], dtype=jnp.int32)[None, :]
    return jnp.sum(jnp.where(onehot, table[None, :], 0), axis=1)


def attend_masks(counts_of_pages, fill_row, counts_of_rows, page_len, page_total, row_total):
    key_index = jnp.arange(page_total * page_len, dtype=jnp.int32)
    page_ref = key_index // page_len
    within = key_index % page_len
    page_owner, page_starts = slot_lookup(page_ref, counts_of_pages)
    context_len = (counts_of_pages - 1) * page_len + fill_row
    position = (page_ref - table_pick(page_starts, page_owner)) * page_len + within
    valid = position < table_pick(context_len, page_owner)
    row_index = jnp.arange(row_total, dtype=jnp.int32)
    row_owner = slot_lookup(row_index, counts_of_rows)[0]
    context_mask = (row_owner[:, None] == page_owner[None, :]) & valid[None, :]
    causal = (row_owner[:, None] == row_owner[None, :]) & (row_index[None, :] <= row_index[:, None])
    return jnp.concatenate([context_mask, causal], axis=1)


ROW_BLOCK = 256
KEY_CHUNK = 512


def pick(table, index):
    onehot = index[:, None] == jnp.arange(table.shape[0], dtype=jnp.int32)[None, :]
    return jnp.sum(jnp.where(onehot, table[None, :], 0), axis=1)


def attention_kernel(
    scalars_ref,
    q_ref,
    own_ref,
    partner_ref,
    fresh_k_ref,
    fresh_v_ref,
    kinfo_ref,
    rown_ref,
    o_ref,
    s_scr,
    acc_scr,
    *,
    slot_base,
    meta_base,
):
    block = pl.program_id(0)
    ctx_lo = scalars_ref[block * 5]
    ctx_n = scalars_ref[block * 5 + 1]
    new_lo = scalars_ref[block * 5 + 2]
    total = ctx_n + scalars_ref[block * 5 + 3]
    ctx_chunks = scalars_ref[block * 5 + 4]
    keys_are_own = scalars_ref[meta_base] == 0
    heads = q_ref.shape[1] // HD
    page_len = own_ref.shape[1]
    per_chunk = KEY_CHUNK // page_len
    q = q_ref[...]
    stacked = jnp.concatenate([q[:, h * HD:(h + 1) * HD] for h in range(heads)], axis=0)
    row_owner = rown_ref[...]
    row_index = block * ROW_BLOCK + lax.broadcasted_iota(jnp.int32, (ROW_BLOCK, 1), 0)
    scale = 1.0 / math.sqrt(HD)

    def chunk_of(t):
        return jnp.where(t < ctx_n, ctx_lo + t, ctx_chunks + new_lo + t - ctx_n)

    def load_chunk(c, want_keys, fresh_ref):
        pick_own = keys_are_own == want_keys

        def cached():
            pages = []
            for i in range(per_chunk):
                slot = scalars_ref[slot_base + c * per_chunk + i]
                pages.append(jnp.where(pick_own, own_ref[slot], partner_ref[slot]))
            return jnp.concatenate(pages, axis=0)

        def fresh():
            start = pl.multiple_of((c - ctx_chunks) * KEY_CHUNK, KEY_CHUNK)
            return fresh_ref[pl.ds(start, KEY_CHUNK), :]

        return lax.cond(c < ctx_chunks, cached, fresh)

    def scores_pass(t, highest):
        c = chunk_of(t)
        keys = load_chunk(c, True, fresh_k_ref)
        s = lax.dot_general(
            stacked, keys, (((1,), (1,)), ((), ())), preferred_element_type=jnp.float32
        ) * scale
        info = kinfo_ref[c]
        seen = (info[0:1] == row_owner) & (info[1:2] <= row_index)
        s = jnp.where(seen[None], s.reshape(heads, ROW_BLOCK, KEY_CHUNK), -1e30).reshape(
            heads * ROW_BLOCK, KEY_CHUNK
        )
        s_scr[c] = s
        return jnp.maximum(highest, jnp.max(s, axis=1, keepdims=True))

    highest = lax.fori_loop(
        0, total, scores_pass, jnp.full((heads * ROW_BLOCK, 1), -1e30, jnp.float32)
    )

    def exp_pass(t, summed):
        c = chunk_of(t)
        e = jnp.exp(s_scr[c] - highest)
        s_scr[c] = e
        return summed + jnp.sum(e, axis=1, keepdims=True)

    summed = lax.fori_loop(0, total, exp_pass, jnp.zeros((heads * ROW_BLOCK, 1), jnp.float32))
    inverse = 1.0 / summed
    acc_scr[...] = jnp.zeros(acc_scr.shape, jnp.float32)

    def value_pass(t, carry):
        c = chunk_of(t)
        w = (s_scr[c] * inverse).astype(jnp.bfloat16)
        values = load_chunk(c, False, fresh_v_ref)
        acc_scr[...] += jnp.dot(w, values, preferred_element_type=jnp.float32)
        return carry

    lax.fori_loop(0, total, value_pass, 0)
    for h in range(heads):
        o_ref[:, h * HD:(h + 1) * HD] = acc_scr[h * ROW_BLOCK:(h + 1) * ROW_BLOCK, :].astype(
            jnp.bfloat16
        )


def sparse_attention(
    queries, own_pages, partner_pages, slots, new_keys, new_values, half, kv_head,
    page_counts, last_fill, row_counts, page_total,
):
    row_total = queries.shape[0]
    page_len = own_pages.shape[1]
    ctx_total = page_total * page_len
    key_total = ctx_total + row_total
    heads = queries.shape[1] // HD
    blocks = row_total // ROW_BLOCK
    chunks = key_total // KEY_CHUNK
    ctx_chunks = ctx_total // KEY_CHUNK
    key_index = jnp.arange(ctx_total, dtype=jnp.int32)
    page_ref = key_index // page_len
    page_owner, page_starts = slot_lookup(page_ref, page_counts)
    context_len = (page_counts - 1) * page_len + last_fill
    position = (page_ref - table_pick(page_starts, page_owner)) * page_len + key_index % page_len
    valid = position < table_pick(context_len, page_owner)
    row_index = jnp.arange(row_total, dtype=jnp.int32)
    row_owner, row_starts = slot_lookup(row_index, row_counts)
    key_owner = jnp.concatenate([jnp.where(valid, page_owner, -1), row_owner])
    key_pos = jnp.concatenate([jnp.full((ctx_total,), -1, jnp.int32), row_index])
    first = row_owner[::ROW_BLOCK]
    last = row_owner[ROW_BLOCK - 1::ROW_BLOCK]
    ctx_from = pick(page_starts, first) * page_len
    ctx_to = (pick(page_starts, last) + pick(page_counts, last)) * page_len
    ctx_lo = ctx_from // KEY_CHUNK
    ctx_n = (ctx_to + KEY_CHUNK - 1) // KEY_CHUNK - ctx_lo
    new_from = pick(row_starts, first)
    new_to = jnp.arange(1, blocks + 1, dtype=jnp.int32) * ROW_BLOCK
    new_lo = new_from // KEY_CHUNK
    new_n = (new_to + KEY_CHUNK - 1) // KEY_CHUNK - new_lo
    ranges = jnp.stack(
        [ctx_lo, ctx_n, new_lo, new_n, jnp.full((blocks,), ctx_chunks, jnp.int32)], axis=1
    ).astype(jnp.int32)
    meta = jnp.stack([half, kv_head]).astype(jnp.int32)
    slot_base = ranges.size
    meta_base = slot_base + slots.shape[0]
    scalars = jnp.concatenate([ranges.reshape(-1), slots.astype(jnp.int32), meta])
    key_info = jnp.stack(
        [key_owner.reshape(chunks, KEY_CHUNK), key_pos.reshape(chunks, KEY_CHUNK)], axis=1
    )
    whole = lambda b, s: (0, 0, 0)
    by_head = lambda b, s: (0, s[meta_base + 1])
    return pl.pallas_call(
        functools.partial(attention_kernel, slot_base=slot_base, meta_base=meta_base),
        grid_spec=pltpu.PrefetchScalarGridSpec(
            num_scalar_prefetch=1,
            grid=(blocks,),
            in_specs=[
                pl.BlockSpec((ROW_BLOCK, heads * HD), lambda b, s: (b, 0)),
                pl.BlockSpec(own_pages.shape, whole),
                pl.BlockSpec(partner_pages.shape, whole),
                pl.BlockSpec((row_total, HD), by_head),
                pl.BlockSpec((row_total, HD), by_head),
                pl.BlockSpec((chunks, 2, KEY_CHUNK), whole),
                pl.BlockSpec((ROW_BLOCK, 1), lambda b, s: (b, 0)),
            ],
            out_specs=pl.BlockSpec((ROW_BLOCK, heads * HD), lambda b, s: (b, 0)),
            scratch_shapes=[
                pltpu.VMEM((chunks, heads * ROW_BLOCK, KEY_CHUNK), jnp.float32),
                pltpu.VMEM((heads * ROW_BLOCK, HD), jnp.float32),
            ],
        ),
        out_shape=jax.ShapeDtypeStruct((row_total, heads * HD), jnp.bfloat16),
    )(
        scalars,
        queries,
        own_pages,
        partner_pages,
        new_keys,
        new_values,
        key_info,
        row_owner.reshape(row_total, 1),
    )


def rows_to_columns(x, axis_name):
    count = lax.axis_size(axis_name)
    me = lax.axis_index(axis_name)
    parts = x.reshape(count, x.shape[0] // count, x.shape[1])
    received = [parts[me]]
    for shift in range(1, count):
        outgoing = lax.dynamic_index_in_dim(parts, (me + shift) % count, 0, keepdims=False)
        perm = [(i, (i + shift) % count) for i in range(count)]
        received.append(lax.ppermute(outgoing, axis_name, perm))
    order = (me - jnp.arange(count, dtype=jnp.int32)) % count
    blocks = jnp.stack(received)[order]
    return jnp.transpose(blocks, (1, 0, 2)).reshape(parts.shape[1], count * x.shape[1])


def columns_to_rows(x, axis_name):
    count = lax.axis_size(axis_name)
    me = lax.axis_index(axis_name)
    width = x.shape[1] // count
    received = [lax.dynamic_slice_in_dim(x, me * width, width, 1)]
    for shift in range(1, count):
        outgoing = lax.dynamic_slice_in_dim(x, ((me + shift) % count) * width, width, 1)
        perm = [(i, (i + shift) % count) for i in range(count)]
        received.append(lax.ppermute(outgoing, axis_name, perm))
    order = (me - jnp.arange(count, dtype=jnp.int32)) % count
    return jnp.stack(received)[order].reshape(count * x.shape[0], width)


def shards(
    hidden,
    queries,
    new_keys,
    new_values,
    cache_keys,
    cache_values,
    out_weight,
    attn_gain,
    ple_input,
    ple_gate_weight,
    ple_proj_weight,
    ple_gain,
    page_holder,
    page_slot,
    page_counts,
    last_fill,
    row_counts,
):
    row_total = hidden.shape[0]
    page_total = cache_keys.shape[0]
    page_len = cache_keys.shape[1]
    req_count = lax.axis_size("req")
    tp_index = lax.axis_index("tp")
    local_heads = queries.shape[1] // HD
    kv_head = tp_index // 2
    capacity = max(2, page_total // req_count)
    holders = page_holder[:, 0]
    places = page_slot[:, 0]
    ref_index = jnp.arange(page_total, dtype=jnp.int32)
    earlier = (holders[:, None] == holders[None, :]) & (ref_index[:, None] > ref_index[None, :])
    ranking = jnp.sum(earlier.astype(jnp.int32), axis=1)
    matched = (holders[:, None, None] == jnp.arange(req_count, dtype=jnp.int32)[None, :, None]) & (
        ranking[:, None, None] == jnp.arange(capacity, dtype=jnp.int32)[None, None, :]
    )
    request_table = jnp.sum(jnp.where(matched, places[:, None, None] + 1, 0), axis=0) - 1
    asked = lax.all_to_all(request_table, "req", split_axis=0, concat_axis=0, tiled=True)
    wanted = jnp.maximum(asked, 0)
    tp_count = lax.axis_size("tp")
    half = tp_index % 2
    partner = [(i, i ^ 1) for i in range(tp_count)]
    arrival_index = holders * capacity + ranking

    own_cache = jnp.where(half == 0, cache_keys, cache_values)
    outgoing = lax.dynamic_slice_in_dim(own_cache, kv_head * HD, HD, 2)[wanted]
    arrived = lax.all_to_all(outgoing, "req", split_axis=0, concat_axis=0, tiled=True)
    swapped = lax.ppermute(arrived, "tp", partner)
    attention = sparse_attention(
        queries,
        arrived.reshape(-1, page_len, HD),
        swapped.reshape(-1, page_len, HD),
        arrival_index,
        new_keys,
        new_values,
        half,
        kv_head,
        page_counts[0], last_fill[0], row_counts[0], page_total,
    )
    tp_size = lax.axis_size("tp")
    full_weight = lax.all_gather(out_weight, "tp", axis=0, tiled=True)
    ple_joined = lax.all_gather(
        jnp.concatenate([ple_gate_weight, ple_proj_weight.T], axis=1), "tp", axis=0, tiled=True
    )
    full_gate_weight = ple_joined[:, : ple_gate_weight.shape[1]]
    full_proj_weight_t = ple_joined[:, ple_gate_weight.shape[1] :]
    hidden_parts = hidden.reshape(tp_size, -1, hidden.shape[1])
    gain_rows = jnp.zeros((8, hidden.shape[1]), hidden.dtype).at[0].set(attn_gain).at[1].set(ple_gain)
    with_gains = jnp.concatenate(
        [hidden_parts, jnp.broadcast_to(gain_rows[None], (tp_size, 8, hidden.shape[1]))], axis=1
    )
    row_hidden_gains = rows_to_columns(with_gains.reshape(-1, hidden.shape[1]), "tp")
    row_hidden = row_hidden_gains[: hidden_parts.shape[1]]
    full_attn_gain = row_hidden_gains[hidden_parts.shape[1]]
    full_ple_gain = row_hidden_gains[hidden_parts.shape[1] + 1]
    parts = attention.reshape(tp_size, -1, attention.shape[1])
    width = attention.shape[1]
    projected = jnp.dot(parts[tp_index], out_weight, preferred_element_type=jnp.float32)
    for shift in range(1, tp_size):
        outgoing = lax.dynamic_index_in_dim(parts, (tp_index + shift) % tp_size, 0, keepdims=False)
        perm = [(i, (i + shift) % tp_size) for i in range(tp_size)]
        piece = lax.ppermute(outgoing, "tp", perm)
        source = (tp_index - shift) % tp_size
        projected = projected + jnp.dot(
            piece,
            lax.dynamic_slice_in_dim(full_weight, source * width, width, 0),
            preferred_element_type=jnp.float32,
        )
    part_rows = parts.shape[1]
    row_ple = lax.dynamic_slice_in_dim(ple_input, tp_index * part_rows, part_rows, 0)
    squares = jnp.sum(projected * projected, axis=1)
    normed = (
        projected
        * lax.rsqrt(squares / D + 1e-06)[:, None]
        * full_attn_gain.astype(jnp.float32)[None, :]
    )
    mixed_state = (row_hidden.astype(jnp.float32) + normed).astype(jnp.bfloat16)
    gate = jnp.dot(mixed_state, full_gate_weight, preferred_element_type=jnp.float32)
    activated = (jax.nn.gelu(gate, approximate=True) * row_ple.astype(jnp.float32)).astype(
        jnp.bfloat16
    )
    lifted = lax.dot_general(
        activated, full_proj_weight_t, (((1,), (1,)), ((), ())), preferred_element_type=jnp.float32
    )
    lift_squares = jnp.sum(lifted * lifted, axis=1)
    lift_normed = (
        lifted
        * lax.rsqrt(lift_squares / D + 1e-06)[:, None]
        * full_ple_gain.astype(jnp.float32)[None, :]
    )
    row_out = (mixed_state.astype(jnp.float32) + lift_normed).astype(jnp.bfloat16)
    return columns_to_rows(row_out, "tp")


def solution(mesh):
    return jax.shard_map(
        shards,
        mesh=mesh,
        in_specs=(
            P("req", "tp"),
            P("req", "tp"),
            P("req", None),
            P("req", None),
            P("req", None, None),
            P("req", None, None),
            P("tp", None),
            P("tp"),
            P("req", None),
            P("tp", None),
            P(None, "tp"),
            P("tp"),
            P("req", None),
            P("req", None),
            P("req", None),
            P("req", None),
            P("req", None),
        ),
        out_specs=P("req", "tp"),
        check_vma=False,
    )
```

```python
import functools
import math

import jax
import jax.numpy as jnp
from jax import lax
from jax.experimental import pallas as pl
from jax.experimental.pallas import tpu as pltpu
from jax.sharding import PartitionSpec as P

D = 2048
HD = 256


def slot_lookup(positions, counts):
    starts = jnp.cumsum(counts) - counts
    owning = jnp.sum((positions[:, None] >= starts[None, :]).astype(jnp.int32), axis=1) - 1
    return (owning, starts)


def table_pick(table, owning):
    onehot = owning[:, None] == jnp.arange(table.shape[0], dtype=jnp.int32)[None, :]
    return jnp.sum(jnp.where(onehot, table[None, :], 0), axis=1)


def attend_masks(counts_of_pages, fill_row, counts_of_rows, page_len, page_total, row_total):
    key_index = jnp.arange(page_total * page_len, dtype=jnp.int32)
    page_ref = key_index // page_len
    within = key_index % page_len
    page_owner, page_starts = slot_lookup(page_ref, counts_of_pages)
    context_len = (counts_of_pages - 1) * page_len + fill_row
    position = (page_ref - table_pick(page_starts, page_owner)) * page_len + within
    valid = position < table_pick(context_len, page_owner)
    row_index = jnp.arange(row_total, dtype=jnp.int32)
    row_owner = slot_lookup(row_index, counts_of_rows)[0]
    context_mask = (row_owner[:, None] == page_owner[None, :]) & valid[None, :]
    causal = (row_owner[:, None] == row_owner[None, :]) & (row_index[None, :] <= row_index[:, None])
    return jnp.concatenate([context_mask, causal], axis=1)


ROW_BLOCK = 256
KEY_CHUNK = 512


def pick(table, index):
    onehot = index[:, None] == jnp.arange(table.shape[0], dtype=jnp.int32)[None, :]
    return jnp.sum(jnp.where(onehot, table[None, :], 0), axis=1)


def attention_kernel(
    scalars_ref,
    q_ref,
    own_ref,
    partner_ref,
    fresh_k_ref,
    fresh_v_ref,
    kinfo_ref,
    o_ref,
    s_scr,
    acc_scr,
    *,
    slot_base,
    meta_base,
    request_base,
    requests,
):
    block = pl.program_id(0)
    ctx_lo = scalars_ref[block * 5]
    ctx_n = scalars_ref[block * 5 + 1]
    new_lo = scalars_ref[block * 5 + 2]
    total = ctx_n + scalars_ref[block * 5 + 3]
    ctx_chunks = scalars_ref[block * 5 + 4]
    keys_are_own = scalars_ref[meta_base] == 0
    heads = q_ref.shape[1] // HD
    page_len = own_ref.shape[1]
    per_chunk = KEY_CHUNK // page_len
    q = q_ref[...]
    stacked = jnp.concatenate([q[:, h * HD:(h + 1) * HD] for h in range(heads)], axis=0)
    row_index = block * ROW_BLOCK + lax.broadcasted_iota(jnp.int32, (ROW_BLOCK, 1), 0)
    row_owner = jnp.full((ROW_BLOCK, 1), -1, jnp.int32)
    for r in range(requests):
        lo = scalars_ref[request_base + 2 * r]
        hi = lo + scalars_ref[request_base + 2 * r + 1]
        row_owner = jnp.where((row_index >= lo) & (row_index < hi), r, row_owner)
    scale = 1.0 / math.sqrt(HD)

    def chunk_of(t):
        return jnp.where(t < ctx_n, ctx_lo + t, ctx_chunks + new_lo + t - ctx_n)

    def load_chunk(c, want_keys, fresh_ref):
        pick_own = keys_are_own == want_keys

        def cached():
            pages = []
            for i in range(per_chunk):
                slot = scalars_ref[slot_base + c * per_chunk + i]
                pages.append(jnp.where(pick_own, own_ref[slot], partner_ref[slot]))
            return jnp.concatenate(pages, axis=0)

        def fresh():
            start = pl.multiple_of((c - ctx_chunks) * KEY_CHUNK, KEY_CHUNK)
            return fresh_ref[pl.ds(start, KEY_CHUNK), :]

        return lax.cond(c < ctx_chunks, cached, fresh)

    def scores_pass(t, highest):
        c = chunk_of(t)
        keys = load_chunk(c, True, fresh_k_ref)
        s = lax.dot_general(
            stacked, keys, (((1,), (1,)), ((), ())), preferred_element_type=jnp.float32
        ) * scale
        info = kinfo_ref[c]
        seen = (info[0:1] == row_owner) & (info[1:2] <= row_index)
        s = jnp.where(seen[None], s.reshape(heads, ROW_BLOCK, KEY_CHUNK), -1e30).reshape(
            heads * ROW_BLOCK, KEY_CHUNK
        )
        s_scr[c] = s
        return jnp.maximum(highest, jnp.max(s, axis=1, keepdims=True))

    highest = lax.fori_loop(
        0, total, scores_pass, jnp.full((heads * ROW_BLOCK, 1), -1e30, jnp.float32)
    )

    def exp_pass(t, summed):
        c = chunk_of(t)
        e = jnp.exp(s_scr[c] - highest)
        s_scr[c] = e
        return summed + jnp.sum(e, axis=1, keepdims=True)

    summed = lax.fori_loop(0, total, exp_pass, jnp.zeros((heads * ROW_BLOCK, 1), jnp.float32))
    inverse = 1.0 / summed
    acc_scr[...] = jnp.zeros(acc_scr.shape, jnp.float32)

    def value_pass(t, carry):
        c = chunk_of(t)
        w = (s_scr[c] * inverse).astype(jnp.bfloat16)
        values = load_chunk(c, False, fresh_v_ref)
        acc_scr[...] += jnp.dot(w, values, preferred_element_type=jnp.float32)
        return carry

    lax.fori_loop(0, total, value_pass, 0)
    for h in range(heads):
        o_ref[:, h * HD:(h + 1) * HD] = acc_scr[h * ROW_BLOCK:(h + 1) * ROW_BLOCK, :].astype(
            jnp.bfloat16
        )


def sparse_attention(
    queries, own_pages, partner_pages, slots, new_keys, new_values, half, kv_head,
    page_counts, last_fill, row_counts, page_total,
):
    row_total = queries.shape[0]
    page_len = own_pages.shape[1]
    ctx_total = page_total * page_len
    key_total = ctx_total + row_total
    heads = queries.shape[1] // HD
    blocks = row_total // ROW_BLOCK
    chunks = key_total // KEY_CHUNK
    ctx_chunks = ctx_total // KEY_CHUNK
    key_index = jnp.arange(ctx_total, dtype=jnp.int32)
    page_ref = key_index // page_len
    page_owner, page_starts = slot_lookup(page_ref, page_counts)
    context_len = (page_counts - 1) * page_len + last_fill
    position = (page_ref - table_pick(page_starts, page_owner)) * page_len + key_index % page_len
    valid = position < table_pick(context_len, page_owner)
    row_index = jnp.arange(row_total, dtype=jnp.int32)
    row_owner, row_starts = slot_lookup(row_index, row_counts)
    key_owner = jnp.concatenate([jnp.where(valid, page_owner, -1), row_owner])
    key_pos = jnp.concatenate([jnp.full((ctx_total,), -1, jnp.int32), row_index])
    first = row_owner[::ROW_BLOCK]
    last = row_owner[ROW_BLOCK - 1::ROW_BLOCK]
    ctx_from = pick(page_starts, first) * page_len
    ctx_to = (pick(page_starts, last) + pick(page_counts, last)) * page_len
    ctx_lo = ctx_from // KEY_CHUNK
    ctx_n = (ctx_to + KEY_CHUNK - 1) // KEY_CHUNK - ctx_lo
    new_from = pick(row_starts, first)
    new_to = jnp.arange(1, blocks + 1, dtype=jnp.int32) * ROW_BLOCK
    new_lo = new_from // KEY_CHUNK
    new_n = (new_to + KEY_CHUNK - 1) // KEY_CHUNK - new_lo
    ranges = jnp.stack(
        [ctx_lo, ctx_n, new_lo, new_n, jnp.full((blocks,), ctx_chunks, jnp.int32)], axis=1
    ).astype(jnp.int32)
    meta = jnp.stack([half, kv_head]).astype(jnp.int32)
    slot_base = ranges.size
    meta_base = slot_base + slots.shape[0]
    request_base = meta_base + meta.shape[0]
    per_request = jnp.stack([row_starts, row_counts], axis=1).astype(jnp.int32)
    scalars = jnp.concatenate(
        [ranges.reshape(-1), slots.astype(jnp.int32), meta, per_request.reshape(-1)]
    )
    key_info = jnp.stack(
        [key_owner.reshape(chunks, KEY_CHUNK), key_pos.reshape(chunks, KEY_CHUNK)], axis=1
    )
    whole = lambda b, s: (0, 0, 0)
    by_head = lambda b, s: (0, s[meta_base + 1])
    return pl.pallas_call(
        functools.partial(
            attention_kernel,
            slot_base=slot_base,
            meta_base=meta_base,
            request_base=request_base,
            requests=row_counts.shape[0],
        ),
        grid_spec=pltpu.PrefetchScalarGridSpec(
            num_scalar_prefetch=1,
            grid=(blocks,),
            in_specs=[
                pl.BlockSpec((ROW_BLOCK, heads * HD), lambda b, s: (b, 0)),
                pl.BlockSpec(own_pages.shape, whole),
                pl.BlockSpec(partner_pages.shape, whole),
                pl.BlockSpec((row_total, HD), by_head),
                pl.BlockSpec((row_total, HD), by_head),
                pl.BlockSpec((chunks, 2, KEY_CHUNK), whole),
            ],
            out_specs=pl.BlockSpec((ROW_BLOCK, heads * HD), lambda b, s: (b, 0)),
            scratch_shapes=[
                pltpu.VMEM((chunks, heads * ROW_BLOCK, KEY_CHUNK), jnp.float32),
                pltpu.VMEM((heads * ROW_BLOCK, HD), jnp.float32),
            ],
        ),
        out_shape=jax.ShapeDtypeStruct((row_total, heads * HD), jnp.bfloat16),
    )(
        scalars,
        queries,
        own_pages,
        partner_pages,
        new_keys,
        new_values,
        key_info,
    )


def rows_to_columns(x, axis_name):
    count = lax.axis_size(axis_name)
    me = lax.axis_index(axis_name)
    parts = x.reshape(count, x.shape[0] // count, x.shape[1])
    received = [parts[me]]
    for shift in range(1, count):
        outgoing = lax.dynamic_index_in_dim(parts, (me + shift) % count, 0, keepdims=False)
        perm = [(i, (i + shift) % count) for i in range(count)]
        received.append(lax.ppermute(outgoing, axis_name, perm))
    order = (me - jnp.arange(count, dtype=jnp.int32)) % count
    blocks = jnp.stack(received)[order]
    return jnp.transpose(blocks, (1, 0, 2)).reshape(parts.shape[1], count * x.shape[1])


def columns_to_rows(x, axis_name):
    count = lax.axis_size(axis_name)
    me = lax.axis_index(axis_name)
    width = x.shape[1] // count
    received = [lax.dynamic_slice_in_dim(x, me * width, width, 1)]
    for shift in range(1, count):
        outgoing = lax.dynamic_slice_in_dim(x, ((me + shift) % count) * width, width, 1)
        perm = [(i, (i + shift) % count) for i in range(count)]
        received.append(lax.ppermute(outgoing, axis_name, perm))
    order = (me - jnp.arange(count, dtype=jnp.int32)) % count
    return jnp.stack(received)[order].reshape(count * x.shape[0], width)


def shards(
    hidden,
    queries,
    new_keys,
    new_values,
    cache_keys,
    cache_values,
    out_weight,
    attn_gain,
    ple_input,
    ple_gate_weight,
    ple_proj_weight,
    ple_gain,
    page_holder,
    page_slot,
    page_counts,
    last_fill,
    row_counts,
):
    row_total = hidden.shape[0]
    page_total = cache_keys.shape[0]
    page_len = cache_keys.shape[1]
    req_count = lax.axis_size("req")
    tp_index = lax.axis_index("tp")
    local_heads = queries.shape[1] // HD
    kv_head = tp_index // 2
    capacity = max(2, page_total // req_count)
    holders = page_holder[:, 0]
    places = page_slot[:, 0]
    ref_index = jnp.arange(page_total, dtype=jnp.int32)
    earlier = (holders[:, None] == holders[None, :]) & (ref_index[:, None] > ref_index[None, :])
    ranking = jnp.sum(earlier.astype(jnp.int32), axis=1)
    matched = (holders[:, None, None] == jnp.arange(req_count, dtype=jnp.int32)[None, :, None]) & (
        ranking[:, None, None] == jnp.arange(capacity, dtype=jnp.int32)[None, None, :]
    )
    request_table = jnp.sum(jnp.where(matched, places[:, None, None] + 1, 0), axis=0) - 1
    asked = lax.all_to_all(request_table, "req", split_axis=0, concat_axis=0, tiled=True)
    wanted = jnp.maximum(asked, 0)
    tp_count = lax.axis_size("tp")
    half = tp_index % 2
    partner = [(i, i ^ 1) for i in range(tp_count)]
    arrival_index = holders * capacity + ranking

    own_cache = jnp.where(half == 0, cache_keys, cache_values)
    outgoing = lax.dynamic_slice_in_dim(own_cache, kv_head * HD, HD, 2)[wanted]
    arrived = lax.all_to_all(outgoing, "req", split_axis=0, concat_axis=0, tiled=True)
    swapped = lax.ppermute(arrived, "tp", partner)
    attention = sparse_attention(
        queries,
        arrived.reshape(-1, page_len, HD),
        swapped.reshape(-1, page_len, HD),
        arrival_index,
        new_keys,
        new_values,
        half,
        kv_head,
        page_counts[0], last_fill[0], row_counts[0], page_total,
    )
    tp_size = lax.axis_size("tp")
    full_weight = lax.all_gather(out_weight, "tp", axis=0, tiled=True)
    ple_joined = lax.all_gather(
        jnp.concatenate([ple_gate_weight, ple_proj_weight.T], axis=1), "tp", axis=0, tiled=True
    )
    full_gate_weight = ple_joined[:, : ple_gate_weight.shape[1]]
    full_proj_weight_t = ple_joined[:, ple_gate_weight.shape[1] :]
    hidden_parts = hidden.reshape(tp_size, -1, hidden.shape[1])
    gain_rows = jnp.zeros((8, hidden.shape[1]), hidden.dtype).at[0].set(attn_gain).at[1].set(ple_gain)
    with_gains = jnp.concatenate(
        [hidden_parts, jnp.broadcast_to(gain_rows[None], (tp_size, 8, hidden.shape[1]))], axis=1
    )
    row_hidden_gains = rows_to_columns(with_gains.reshape(-1, hidden.shape[1]), "tp")
    row_hidden = row_hidden_gains[: hidden_parts.shape[1]]
    full_attn_gain = row_hidden_gains[hidden_parts.shape[1]]
    full_ple_gain = row_hidden_gains[hidden_parts.shape[1] + 1]
    parts = attention.reshape(tp_size, -1, attention.shape[1])
    width = attention.shape[1]
    projected = jnp.dot(
        parts[tp_index],
        lax.dynamic_slice_in_dim(full_weight, tp_index * width, width, 0),
        preferred_element_type=jnp.float32,
    )
    for shift in range(1, tp_size):
        outgoing = lax.dynamic_index_in_dim(parts, (tp_index + shift) % tp_size, 0, keepdims=False)
        perm = [(i, (i + shift) % tp_size) for i in range(tp_size)]
        piece = lax.ppermute(outgoing, "tp", perm)
        source = (tp_index - shift) % tp_size
        projected = projected + jnp.dot(
            piece,
            lax.dynamic_slice_in_dim(full_weight, source * width, width, 0),
            preferred_element_type=jnp.float32,
        )
    part_rows = parts.shape[1]
    row_ple = lax.dynamic_slice_in_dim(ple_input, tp_index * part_rows, part_rows, 0)
    squares = jnp.sum(projected * projected, axis=1)
    normed = (
        projected
        * lax.rsqrt(squares / D + 1e-06)[:, None]
        * full_attn_gain.astype(jnp.float32)[None, :]
    )
    mixed_state = (row_hidden.astype(jnp.float32) + normed).astype(jnp.bfloat16)
    gate = jnp.dot(mixed_state, full_gate_weight, preferred_element_type=jnp.float32)
    activated = (jax.nn.gelu(gate, approximate=True) * row_ple.astype(jnp.float32)).astype(
        jnp.bfloat16
    )
    lifted = lax.dot_general(
        activated, full_proj_weight_t, (((1,), (1,)), ((), ())), preferred_element_type=jnp.float32
    )
    lift_squares = jnp.sum(lifted * lifted, axis=1)
    lift_normed = (
        lifted
        * lax.rsqrt(lift_squares / D + 1e-06)[:, None]
        * full_ple_gain.astype(jnp.float32)[None, :]
    )
    row_out = (mixed_state.astype(jnp.float32) + lift_normed).astype(jnp.bfloat16)
    return columns_to_rows(row_out, "tp")


def solution(mesh):
    return jax.shard_map(
        shards,
        mesh=mesh,
        in_specs=(
            P("req", "tp"),
            P("req", "tp"),
            P("req", None),
            P("req", None),
            P("req", None, None),
            P("req", None, None),
            P("tp", None),
            P("tp"),
            P("req", None),
            P("tp", None),
            P(None, "tp"),
            P("tp"),
            P("req", None),
            P("req", None),
            P("req", None),
            P("req", None),
            P("req", None),
        ),
        out_specs=P("req", "tp"),
        check_vma=False,
    )
```

```python
import functools
import math

import jax
import jax.numpy as jnp
from jax import lax
from jax.experimental import pallas as pl
from jax.experimental.pallas import tpu as pltpu
from jax.sharding import PartitionSpec as P

D = 2048
HD = 256


def slot_lookup(positions, counts):
    starts = jnp.cumsum(counts) - counts
    owning = jnp.sum((positions[:, None] >= starts[None, :]).astype(jnp.int32), axis=1) - 1
    return (owning, starts)


def table_pick(table, owning):
    onehot = owning[:, None] == jnp.arange(table.shape[0], dtype=jnp.int32)[None, :]
    return jnp.sum(jnp.where(onehot, table[None, :], 0), axis=1)


def attend_masks(counts_of_pages, fill_row, counts_of_rows, page_len, page_total, row_total):
    key_index = jnp.arange(page_total * page_len, dtype=jnp.int32)
    page_ref = key_index // page_len
    within = key_index % page_len
    page_owner, page_starts = slot_lookup(page_ref, counts_of_pages)
    context_len = (counts_of_pages - 1) * page_len + fill_row
    position = (page_ref - table_pick(page_starts, page_owner)) * page_len + within
    valid = position < table_pick(context_len, page_owner)
    row_index = jnp.arange(row_total, dtype=jnp.int32)
    row_owner = slot_lookup(row_index, counts_of_rows)[0]
    context_mask = (row_owner[:, None] == page_owner[None, :]) & valid[None, :]
    causal = (row_owner[:, None] == row_owner[None, :]) & (row_index[None, :] <= row_index[:, None])
    return jnp.concatenate([context_mask, causal], axis=1)


ROW_BLOCK = 128
KEY_CHUNK = 512


def pick(table, index):
    onehot = index[:, None] == jnp.arange(table.shape[0], dtype=jnp.int32)[None, :]
    return jnp.sum(jnp.where(onehot, table[None, :], 0), axis=1)


def attention_kernel(
    scalars_ref,
    q_ref,
    own_ref,
    partner_ref,
    fresh_k_ref,
    fresh_v_ref,
    kinfo_ref,
    rown_ref,
    o_ref,
    s_scr,
    acc_scr,
    *,
    slot_base,
    meta_base,
):
    block = pl.program_id(0)
    ctx_lo = scalars_ref[block * 5]
    ctx_n = scalars_ref[block * 5 + 1]
    new_lo = scalars_ref[block * 5 + 2]
    total = ctx_n + scalars_ref[block * 5 + 3]
    ctx_chunks = scalars_ref[block * 5 + 4]
    keys_are_own = scalars_ref[meta_base] == 0
    heads = q_ref.shape[1] // HD
    page_len = own_ref.shape[1]
    per_chunk = KEY_CHUNK // page_len
    q = q_ref[...]
    stacked = jnp.concatenate([q[:, h * HD:(h + 1) * HD] for h in range(heads)], axis=0)
    row_owner = rown_ref[...]
    row_index = block * ROW_BLOCK + lax.broadcasted_iota(jnp.int32, (ROW_BLOCK, 1), 0)
    scale = 1.0 / math.sqrt(HD)

    def chunk_of(t):
        return jnp.where(t < ctx_n, ctx_lo + t, ctx_chunks + new_lo + t - ctx_n)

    def load_chunk(c, want_keys, fresh_ref):
        pick_own = keys_are_own == want_keys

        def cached():
            pages = []
            for i in range(per_chunk):
                slot = scalars_ref[slot_base + c * per_chunk + i]
                pages.append(jnp.where(pick_own, own_ref[slot], partner_ref[slot]))
            return jnp.concatenate(pages, axis=0)

        def fresh():
            start = pl.multiple_of((c - ctx_chunks) * KEY_CHUNK, KEY_CHUNK)
            return fresh_ref[pl.ds(start, KEY_CHUNK), :]

        return lax.cond(c < ctx_chunks, cached, fresh)

    def scores_pass(t, highest):
        c = chunk_of(t)
        keys = load_chunk(c, True, fresh_k_ref)
        s = lax.dot_general(
            stacked, keys, (((1,), (1,)), ((), ())), preferred_element_type=jnp.float32
        ) * scale
        info = kinfo_ref[c]
        seen = (info[0:1] == row_owner) & (info[1:2] <= row_index)
        s = jnp.where(seen[None], s.reshape(heads, ROW_BLOCK, KEY_CHUNK), -1e30).reshape(
            heads * ROW_BLOCK, KEY_CHUNK
        )
        s_scr[c] = s
        return jnp.maximum(highest, jnp.max(s, axis=1, keepdims=True))

    highest = lax.fori_loop(
        0, total, scores_pass, jnp.full((heads * ROW_BLOCK, 1), -1e30, jnp.float32)
    )

    def exp_pass(t, summed):
        c = chunk_of(t)
        e = jnp.exp(s_scr[c] - highest)
        s_scr[c] = e
        return summed + jnp.sum(e, axis=1, keepdims=True)

    summed = lax.fori_loop(0, total, exp_pass, jnp.zeros((heads * ROW_BLOCK, 1), jnp.float32))
    inverse = 1.0 / summed
    acc_scr[...] = jnp.zeros(acc_scr.shape, jnp.float32)

    def value_pass(t, carry):
        c = chunk_of(t)
        w = (s_scr[c] * inverse).astype(jnp.bfloat16)
        values = load_chunk(c, False, fresh_v_ref)
        acc_scr[...] += jnp.dot(w, values, preferred_element_type=jnp.float32)
        return carry

    lax.fori_loop(0, total, value_pass, 0)
    for h in range(heads):
        o_ref[:, h * HD:(h + 1) * HD] = acc_scr[h * ROW_BLOCK:(h + 1) * ROW_BLOCK, :].astype(
            jnp.bfloat16
        )


def sparse_attention(
    queries, own_pages, partner_pages, slots, new_keys, new_values, half, kv_head,
    page_counts, last_fill, row_counts, page_total,
):
    row_total = queries.shape[0]
    page_len = own_pages.shape[1]
    ctx_total = page_total * page_len
    key_total = ctx_total + row_total
    heads = queries.shape[1] // HD
    blocks = row_total // ROW_BLOCK
    chunks = key_total // KEY_CHUNK
    ctx_chunks = ctx_total // KEY_CHUNK
    key_index = jnp.arange(ctx_total, dtype=jnp.int32)
    page_ref = key_index // page_len
    page_owner, page_starts = slot_lookup(page_ref, page_counts)
    context_len = (page_counts - 1) * page_len + last_fill
    position = (page_ref - table_pick(page_starts, page_owner)) * page_len + key_index % page_len
    valid = position < table_pick(context_len, page_owner)
    row_index = jnp.arange(row_total, dtype=jnp.int32)
    row_owner, row_starts = slot_lookup(row_index, row_counts)
    key_owner = jnp.concatenate([jnp.where(valid, page_owner, -1), row_owner])
    key_pos = jnp.concatenate([jnp.full((ctx_total,), -1, jnp.int32), row_index])
    first = row_owner[::ROW_BLOCK]
    last = row_owner[ROW_BLOCK - 1::ROW_BLOCK]
    ctx_from = pick(page_starts, first) * page_len
    ctx_to = (pick(page_starts, last) + pick(page_counts, last)) * page_len
    ctx_lo = ctx_from // KEY_CHUNK
    ctx_n = (ctx_to + KEY_CHUNK - 1) // KEY_CHUNK - ctx_lo
    new_from = pick(row_starts, first)
    new_to = jnp.arange(1, blocks + 1, dtype=jnp.int32) * ROW_BLOCK
    new_lo = new_from // KEY_CHUNK
    new_n = (new_to + KEY_CHUNK - 1) // KEY_CHUNK - new_lo
    ranges = jnp.stack(
        [ctx_lo, ctx_n, new_lo, new_n, jnp.full((blocks,), ctx_chunks, jnp.int32)], axis=1
    ).astype(jnp.int32)
    meta = jnp.stack([half, kv_head]).astype(jnp.int32)
    slot_base = ranges.size
    meta_base = slot_base + slots.shape[0]
    scalars = jnp.concatenate([ranges.reshape(-1), slots.astype(jnp.int32), meta])
    key_info = jnp.stack(
        [key_owner.reshape(chunks, KEY_CHUNK), key_pos.reshape(chunks, KEY_CHUNK)], axis=1
    )
    whole = lambda b, s: (0, 0, 0)
    by_head = lambda b, s: (0, s[meta_base + 1])
    return pl.pallas_call(
        functools.partial(attention_kernel, slot_base=slot_base, meta_base=meta_base),
        grid_spec=pltpu.PrefetchScalarGridSpec(
            num_scalar_prefetch=1,
            grid=(blocks,),
            in_specs=[
                pl.BlockSpec((ROW_BLOCK, heads * HD), lambda b, s: (b, 0)),
                pl.BlockSpec(own_pages.shape, whole),
                pl.BlockSpec(partner_pages.shape, whole),
                pl.BlockSpec((row_total, HD), by_head),
                pl.BlockSpec((row_total, HD), by_head),
                pl.BlockSpec((chunks, 2, KEY_CHUNK), whole),
                pl.BlockSpec((ROW_BLOCK, 1), lambda b, s: (b, 0)),
            ],
            out_specs=pl.BlockSpec((ROW_BLOCK, heads * HD), lambda b, s: (b, 0)),
            scratch_shapes=[
                pltpu.VMEM((chunks, heads * ROW_BLOCK, KEY_CHUNK), jnp.float32),
                pltpu.VMEM((heads * ROW_BLOCK, HD), jnp.float32),
            ],
        ),
        out_shape=jax.ShapeDtypeStruct((row_total, heads * HD), jnp.bfloat16),
    )(
        scalars,
        queries,
        own_pages,
        partner_pages,
        new_keys,
        new_values,
        key_info,
        row_owner.reshape(row_total, 1),
    )


def rows_to_columns(x, axis_name):
    count = lax.axis_size(axis_name)
    me = lax.axis_index(axis_name)
    parts = x.reshape(count, x.shape[0] // count, x.shape[1])
    received = [parts[me]]
    for shift in range(1, count):
        outgoing = lax.dynamic_index_in_dim(parts, (me + shift) % count, 0, keepdims=False)
        perm = [(i, (i + shift) % count) for i in range(count)]
        received.append(lax.ppermute(outgoing, axis_name, perm))
    order = (me - jnp.arange(count, dtype=jnp.int32)) % count
    blocks = jnp.stack(received)[order]
    return jnp.transpose(blocks, (1, 0, 2)).reshape(parts.shape[1], count * x.shape[1])


def columns_to_rows(x, axis_name):
    count = lax.axis_size(axis_name)
    me = lax.axis_index(axis_name)
    width = x.shape[1] // count
    received = [lax.dynamic_slice_in_dim(x, me * width, width, 1)]
    for shift in range(1, count):
        outgoing = lax.dynamic_slice_in_dim(x, ((me + shift) % count) * width, width, 1)
        perm = [(i, (i + shift) % count) for i in range(count)]
        received.append(lax.ppermute(outgoing, axis_name, perm))
    order = (me - jnp.arange(count, dtype=jnp.int32)) % count
    return jnp.stack(received)[order].reshape(count * x.shape[0], width)


def shards(
    hidden,
    queries,
    new_keys,
    new_values,
    cache_keys,
    cache_values,
    out_weight,
    attn_gain,
    ple_input,
    ple_gate_weight,
    ple_proj_weight,
    ple_gain,
    page_holder,
    page_slot,
    page_counts,
    last_fill,
    row_counts,
):
    row_total = hidden.shape[0]
    page_total = cache_keys.shape[0]
    page_len = cache_keys.shape[1]
    req_count = lax.axis_size("req")
    tp_index = lax.axis_index("tp")
    local_heads = queries.shape[1] // HD
    kv_head = tp_index // 2
    capacity = max(2, page_total // req_count)
    holders = page_holder[:, 0]
    places = page_slot[:, 0]
    ref_index = jnp.arange(page_total, dtype=jnp.int32)
    earlier = (holders[:, None] == holders[None, :]) & (ref_index[:, None] > ref_index[None, :])
    ranking = jnp.sum(earlier.astype(jnp.int32), axis=1)
    matched = (holders[:, None, None] == jnp.arange(req_count, dtype=jnp.int32)[None, :, None]) & (
        ranking[:, None, None] == jnp.arange(capacity, dtype=jnp.int32)[None, None, :]
    )
    request_table = jnp.sum(jnp.where(matched, places[:, None, None] + 1, 0), axis=0) - 1
    asked = lax.all_to_all(request_table, "req", split_axis=0, concat_axis=0, tiled=True)
    wanted = jnp.maximum(asked, 0)
    tp_count = lax.axis_size("tp")
    half = tp_index % 2
    partner = [(i, i ^ 1) for i in range(tp_count)]
    arrival_index = holders * capacity + ranking

    own_cache = jnp.where(half == 0, cache_keys, cache_values)
    outgoing = lax.dynamic_slice_in_dim(own_cache, kv_head * HD, HD, 2)[wanted]
    arrived = lax.all_to_all(outgoing, "req", split_axis=0, concat_axis=0, tiled=True)
    swapped = lax.ppermute(arrived, "tp", partner)
    attention = sparse_attention(
        queries,
        arrived.reshape(-1, page_len, HD),
        swapped.reshape(-1, page_len, HD),
        arrival_index,
        new_keys,
        new_values,
        half,
        kv_head,
        page_counts[0], last_fill[0], row_counts[0], page_total,
    )
    tp_size = lax.axis_size("tp")
    full_weight = lax.all_gather(out_weight, "tp", axis=0, tiled=True)
    ple_joined = lax.all_gather(
        jnp.concatenate([ple_gate_weight, ple_proj_weight.T], axis=1), "tp", axis=0, tiled=True
    )
    full_gate_weight = ple_joined[:, : ple_gate_weight.shape[1]]
    full_proj_weight_t = ple_joined[:, ple_gate_weight.shape[1] :]
    hidden_parts = hidden.reshape(tp_size, -1, hidden.shape[1])
    gain_rows = jnp.zeros((8, hidden.shape[1]), hidden.dtype).at[0].set(attn_gain).at[1].set(ple_gain)
    with_gains = jnp.concatenate(
        [hidden_parts, jnp.broadcast_to(gain_rows[None], (tp_size, 8, hidden.shape[1]))], axis=1
    )
    row_hidden_gains = rows_to_columns(with_gains.reshape(-1, hidden.shape[1]), "tp")
    row_hidden = row_hidden_gains[: hidden_parts.shape[1]]
    full_attn_gain = row_hidden_gains[hidden_parts.shape[1]]
    full_ple_gain = row_hidden_gains[hidden_parts.shape[1] + 1]
    parts = attention.reshape(tp_size, -1, attention.shape[1])
    width = attention.shape[1]
    projected = jnp.dot(
        parts[tp_index],
        lax.dynamic_slice_in_dim(full_weight, tp_index * width, width, 0),
        preferred_element_type=jnp.float32,
    )
    for shift in range(1, tp_size):
        outgoing = lax.dynamic_index_in_dim(parts, (tp_index + shift) % tp_size, 0, keepdims=False)
        perm = [(i, (i + shift) % tp_size) for i in range(tp_size)]
        piece = lax.ppermute(outgoing, "tp", perm)
        source = (tp_index - shift) % tp_size
        projected = projected + jnp.dot(
            piece,
            lax.dynamic_slice_in_dim(full_weight, source * width, width, 0),
            preferred_element_type=jnp.float32,
        )
    part_rows = parts.shape[1]
    row_ple = lax.dynamic_slice_in_dim(ple_input, tp_index * part_rows, part_rows, 0)
    squares = jnp.sum(projected * projected, axis=1)
    normed = (
        projected
        * lax.rsqrt(squares / D + 1e-06)[:, None]
        * full_attn_gain.astype(jnp.float32)[None, :]
    )
    mixed_state = (row_hidden.astype(jnp.float32) + normed).astype(jnp.bfloat16)
    gate = jnp.dot(mixed_state, full_gate_weight, preferred_element_type=jnp.float32)
    activated = (jax.nn.gelu(gate, approximate=True) * row_ple.astype(jnp.float32)).astype(
        jnp.bfloat16
    )
    lifted = lax.dot_general(
        activated, full_proj_weight_t, (((1,), (1,)), ((), ())), preferred_element_type=jnp.float32
    )
    lift_squares = jnp.sum(lifted * lifted, axis=1)
    lift_normed = (
        lifted
        * lax.rsqrt(lift_squares / D + 1e-06)[:, None]
        * full_ple_gain.astype(jnp.float32)[None, :]
    )
    row_out = (mixed_state.astype(jnp.float32) + lift_normed).astype(jnp.bfloat16)
    return columns_to_rows(row_out, "tp")


def solution(mesh):
    return jax.shard_map(
        shards,
        mesh=mesh,
        in_specs=(
            P("req", "tp"),
            P("req", "tp"),
            P("req", None),
            P("req", None),
            P("req", None, None),
            P("req", None, None),
            P("tp", None),
            P("tp"),
            P("req", None),
            P("tp", None),
            P(None, "tp"),
            P("tp"),
            P("req", None),
            P("req", None),
            P("req", None),
            P("req", None),
            P("req", None),
        ),
        out_specs=P("req", "tp"),
        check_vma=False,
    )
```
